32 devices in a mesh: groups: 2 (over x), gx: 8 (over z, y), gy: 2 (over core).
Axes of the slice: x: 2, y: 2, z: 4, core: 2. Of those that a mesh axis runs over, the one named last changes fastest.
Arguments:
- values: float32 [96, 12, 64, 128], P(('groups', 'gx'), 'gy'), parts along dimension 0, may hold values from -6 to 6
- drift: float32 [2, 96, 12], P(None, ('groups', 'gx'), 'gy'), parts along dimension 1, may hold values from -6 to 6
- params: float32 [8], P('groups'), parts along dimension 0, may hold values from 0.5 to 1.5
Outputs:
- advanced: float32 [96, 12, 64, 128], P(('groups', 'gx'), 'gy'), parts along dimension 0
The draws below stay inside these ranges and needn't reach their ends.
There are 2 independent parts, one for each index of `groups`. The reference program is written for one: setup_inputs(seed, part) draws one part's arguments, and reference() takes and returns one part's arrays. A program takes and returns all parts, laid end to end along the dimension named above; each array names one. Nothing has to cross between parts.
All inputs are finite; a program needn't handle non-finite values.
Results may differ from the reference program's by a relative error of at most 0.0003.
Values sent between devices are 32-bit elements; how exact they have to be, the bound alone decides.
No kernel may reach another device: no remote copies, remote signals or barrier semaphores. Data moves between devices by JAX's collectives and lax.ppermute only.
A program may use at most 64 MiB of HBM per device.

```python
import math
import jax
import jax.numpy as jnp
from jax import lax

NPSI = 64
NV = 128
NPAR = 4
NX = 48
NY = 12


def block_scale(stream_key, shape, shards, least, top_value):
    def one(position, blocks):
        draws = jax.random.uniform(jax.random.fold_in(jax.random.fold_in(stream_key, 6), position), (blocks,), jnp.float32, least / len(shards), top_value / len(shards))
        return jnp.repeat(jnp.exp(draws), shape[position] // blocks).reshape((-1,) + (1,) * (len(shape) - position - 1))

    level = one(*shards[0])
    for cut in shards[1:]:
        level = level * one(*cut)
    return level


def centred(own_key, shape, width, most, split=(), held_as=jnp.bfloat16):
    level = block_scale(own_key, shape, split, -0.22, 0.18) if split else 1.0
    array = jax.random.normal(own_key, shape, jnp.float32) * width * level
    return jnp.minimum(jnp.maximum(array, -most), most).astype(held_as)


def setup_inputs(seed: int = 0, part: int = 0) -> dict:
    splits = jax.random.split(jax.random.key(seed), 4)
    own_keys = jax.random.split(jax.random.fold_in(splits[3], part), 4)
    return {
        "values": centred(own_keys[0], (NX, NY, NPSI, NV), 1.0, 6.0, ((0, 8), (1, 2)), jnp.float32),
        "drift": centred(own_keys[1], (2, NX, NY), 0.5, 6.0, ((1, 8), (2, 2)), jnp.float32),
        "params": jnp.clip(jax.random.uniform(own_keys[2], (NPAR,), jnp.float32, 0.5, 1.5), 0.5, 1.5),
    }


cfl_number = 0.5
weno_eps = 1e-6
cell_span = 1.0 / 64.0


def weno_value(first, second, third, fourth, fifth):
    stencil_one = first / 3.0 - 7.0 * second / 6.0 + 11.0 * third / 6.0
    stencil_two = -second / 6.0 + 5.0 * third / 6.0 + fourth / 3.0
    stencil_three = third / 3.0 + 5.0 * fourth / 6.0 - fifth / 6.0
    smooth_one = 13.0 / 12.0 * (first - 2.0 * second + third) ** 2 + 0.25 * (first - 4.0 * second + 3.0 * third) ** 2
    smooth_two = 13.0 / 12.0 * (second - 2.0 * third + fourth) ** 2 + 0.25 * (second - fourth) ** 2
    smooth_three = 13.0 / 12.0 * (third - 2.0 * fourth + fifth) ** 2 + 0.25 * (3.0 * third - 4.0 * fourth + fifth) ** 2
    weight_one = 0.1 / (weno_eps + smooth_one) ** 2
    weight_two = 0.6 / (weno_eps + smooth_two) ** 2
    weight_three = 0.3 / (weno_eps + smooth_three) ** 2
    total = weight_one * stencil_one + weight_two * stencil_two + weight_three * stencil_three
    return total / (weight_one + weight_two + weight_three)


def both_sides(window):
    backward = weno_value(window(0), window(1), window(2), window(3), window(4))
    forward = weno_value(window(5), window(4), window(3), window(2), window(1))
    return backward, forward


def one_sided(padded, along, spacing, length):
    extent = padded.shape[along]
    differences = (lax.slice_in_dim(padded, 1, extent, axis=along) - lax.slice_in_dim(padded, 0, extent - 1, axis=along)) / spacing

    def window(offset):
        return lax.slice_in_dim(differences, offset, offset + length, axis=along)

    return both_sides(window)


def periodic_sided(field, along, spacing):
    differences = (field - jnp.roll(field, 1, axis=along)) / spacing

    def window(offset):
        return jnp.roll(differences, 2 - offset, axis=along)

    return both_sides(window)


def clamped_sided(field, along, spacing):
    extent = field.shape[along]
    inner = (lax.slice_in_dim(field, 1, extent, axis=along) - lax.slice_in_dim(field, 0, extent - 1, axis=along)) / spacing
    differences = jnp.concatenate([lax.slice_in_dim(inner, 0, 1, axis=along), inner], axis=along)
    low_edge = lax.slice_in_dim(differences, 0, 1, axis=along)
    high_edge = lax.slice_in_dim(differences, extent - 1, extent, axis=along)

    def window(offset):
        shift_by = offset - 2
        if shift_by > 0:
            return jnp.concatenate([lax.slice_in_dim(differences, shift_by, extent, axis=along)] + [high_edge] * shift_by, axis=along)
        if shift_by < 0:
            return jnp.concatenate([low_edge] * (-shift_by) + [lax.slice_in_dim(differences, 0, extent + shift_by, axis=along)], axis=along)
        return differences

    return both_sides(window)


def edge_fill(field, along, margin, at_low, at_high):
    extent = field.shape[along]
    shape_dist = [1] * field.ndim
    shape_dist[along] = margin
    inner_low = lax.slice_in_dim(field, margin, margin + 1, axis=along)
    next_low = lax.slice_in_dim(field, margin + 1, margin + 2, axis=along)
    dist_low = jnp.arange(margin, 0, -1).astype(jnp.float32).reshape(tuple(shape_dist))
    low_fill = inner_low + dist_low * (inner_low - next_low)
    inner_high = lax.slice_in_dim(field, extent - margin - 1, extent - margin, axis=along)
    next_high = lax.slice_in_dim(field, extent - margin - 2, extent - margin - 1, axis=along)
    dist_high = jnp.arange(1, margin + 1).astype(jnp.float32).reshape(tuple(shape_dist))
    high_fill = inner_high + dist_high * (inner_high - next_high)
    new_low = jnp.where(at_low, low_fill, lax.slice_in_dim(field, 0, margin, axis=along))
    new_high = jnp.where(at_high, high_fill, lax.slice_in_dim(field, extent - margin, extent, axis=along))
    middle = lax.slice_in_dim(field, margin, extent - margin, axis=along)
    return jnp.concatenate([new_low, middle, new_high], axis=along)


def speed_bounds(drift_field, x_coord, y_coord, turn_a, along_one, along_two):
    first_hi = jnp.max(along_one)
    first_lo = jnp.min(along_one)
    second_hi = jnp.max(along_two)
    second_lo = jnp.min(along_two)
    bound_one = jnp.max(jnp.maximum(drift_field[0] + first_hi, -(drift_field[0] + first_lo)) + turn_a * jnp.abs(y_coord)[None, :])
    bound_two = jnp.max(jnp.maximum(drift_field[1] + second_hi, -(drift_field[1] + second_lo)) + turn_a * jnp.abs(x_coord)[:, None])
    return bound_one, bound_two


def hamilton_rate(backs, fores, x_coord, y_coord, flow_x, flow_y, along_one, along_two, params, alphas):
    mean_one = 0.5 * (backs[0] + fores[0])
    mean_two = 0.5 * (backs[1] + fores[1])
    mean_three = 0.5 * (backs[2] + fores[2])
    mean_four = 0.5 * (backs[3] + fores[3])
    x_col = x_coord[:, None, None, None]
    y_col = y_coord[None, :, None, None]
    ham = mean_one * (along_one[None, None] + flow_x[:, :, None, None])
    ham = ham + mean_two * (along_two[None, None] + flow_y[:, :, None, None])
    ham = ham + params[1] * jnp.abs(mean_one * y_col - mean_two * x_col - mean_three)
    ham = ham - params[2] * jnp.abs(mean_three) + params[3] * jnp.abs(mean_four)
    dissipation = alphas[0] * (fores[0] - backs[0]) + alphas[1] * (fores[1] - backs[1])
    dissipation = dissipation + alphas[2] * (fores[2] - backs[2]) + alphas[3] * (fores[3] - backs[3])
    return ham + 0.5 * dissipation


def reference(values, drift, params):
    step_x = cell_span
    step_y = cell_span
    step_psi = 2.0 * math.pi / NPSI
    step_speed = 1.0 / NV
    x_coord = (jnp.arange(NX).astype(jnp.float32) + 0.5 - 0.5 * NX) * step_x
    y_coord = (jnp.arange(NY).astype(jnp.float32) + 0.5 - 0.5 * NY) * step_y
    psi_grid = jnp.arange(NPSI).astype(jnp.float32) * step_psi - math.pi
    speed_grid = 0.5 + (jnp.arange(NV).astype(jnp.float32) + 0.5) * step_speed
    along_one = -speed_grid[None, :] + params[0] * jnp.cos(psi_grid)[:, None]
    along_two = params[0] * jnp.sin(psi_grid)[:, None]
    bound_one, bound_two = speed_bounds(drift, x_coord, y_coord, params[1], along_one, along_two)
    alphas = (bound_one, bound_two, params[1] + params[2], params[3])
    step_time = cfl_number / (alphas[0] / step_x + alphas[1] / step_y + alphas[2] / step_psi + alphas[3] / step_speed)

    def rate(field):
        padded_x = edge_fill(jnp.pad(field, ((3, 3), (0, 0), (0, 0), (0, 0))), 0, 3, True, True)
        back_one, fore_one = one_sided(padded_x, 0, step_x, NX)
        padded_y = edge_fill(jnp.pad(field, ((0, 0), (3, 3), (0, 0), (0, 0))), 1, 3, True, True)
        back_two, fore_two = one_sided(padded_y, 1, step_y, NY)
        back_three, fore_three = periodic_sided(field, 2, step_psi)
        back_four, fore_four = clamped_sided(field, 3, step_speed)
        return hamilton_rate((back_one, back_two, back_three, back_four), (fore_one, fore_two, fore_three, fore_four), x_coord, y_coord, drift[0], drift[1], along_one, along_two, params, alphas)

    first = values + step_time * rate(values)
    second = 0.75 * values + 0.25 * (first + step_time * rate(first))
    return values * (1.0 / 3.0) + (2.0 / 3.0) * (second + step_time * rate(second))
```

```python
import math

import jax
import jax.numpy as jnp
from jax import lax
from jax.sharding import PartitionSpec as P

cfl_number = 0.5
weno_eps = 1e-06
cell_span = 1.0 / 64.0


def with_halo(cells, sides, width):
    for axis, dim in sides:
        count = lax.axis_size(axis)
        ends = count - 1
        head = lax.slice_in_dim(cells, 0, width, axis=dim)
        tail = lax.slice_in_dim(cells, cells.shape[dim] - width, cells.shape[dim], axis=dim)
        cells = jnp.concatenate(
            [
                lax.ppermute(tail, axis, [(i, (i + 1) % count) for i in range(ends)]),
                cells,
                lax.ppermute(head, axis, [((i + 1) % count, i) for i in range(ends)]),
            ],
            axis=dim,
        )
    return cells


def weno_value(first, second, third, fourth, fifth):
    stencil_one = first / 3.0 - 7.0 * second / 6.0 + 11.0 * third / 6.0
    stencil_two = -second / 6.0 + 5.0 * third / 6.0 + fourth / 3.0
    stencil_three = third / 3.0 + 5.0 * fourth / 6.0 - fifth / 6.0
    smooth_one = (
        13.0 / 12.0 * (first - 2.0 * second + third) ** 2
        + 0.25 * (first - 4.0 * second + 3.0 * third) ** 2
    )
    smooth_two = 13.0 / 12.0 * (second - 2.0 * third + fourth) ** 2 + 0.25 * (second - fourth) ** 2
    smooth_three = (
        13.0 / 12.0 * (third - 2.0 * fourth + fifth) ** 2
        + 0.25 * (3.0 * third - 4.0 * fourth + fifth) ** 2
    )
    weight_one = 0.1 / (weno_eps + smooth_one) ** 2
    weight_two = 0.6 / (weno_eps + smooth_two) ** 2
    weight_three = 0.3 / (weno_eps + smooth_three) ** 2
    total = weight_one * stencil_one + weight_two * stencil_two + weight_three * stencil_three
    return total / (weight_one + weight_two + weight_three)


def both_sides(window):
    backward = weno_value(window(0), window(1), window(2), window(3), window(4))
    forward = weno_value(window(5), window(4), window(3), window(2), window(1))
    return (backward, forward)


def one_sided(padded, along, spacing, length):
    extent = padded.shape[along]
    differences = (
        lax.slice_in_dim(padded, 1, extent, axis=along)
        - lax.slice_in_dim(padded, 0, extent - 1, axis=along)
    ) / spacing

    def window(offset):
        return lax.slice_in_dim(differences, offset, offset + length, axis=along)

    return both_sides(window)


def periodic_sided(field, along, spacing):
    differences = (field - jnp.roll(field, 1, axis=along)) / spacing

    def window(offset):
        return jnp.roll(differences, 2 - offset, axis=along)

    return both_sides(window)


def clamped_sided(field, along, spacing):
    extent = field.shape[along]
    inner = (
        lax.slice_in_dim(field, 1, extent, axis=along)
        - lax.slice_in_dim(field, 0, extent - 1, axis=along)
    ) / spacing
    differences = jnp.concatenate([lax.slice_in_dim(inner, 0, 1, axis=along), inner], axis=along)
    low_edge = lax.slice_in_dim(differences, 0, 1, axis=along)
    high_edge = lax.slice_in_dim(differences, extent - 1, extent, axis=along)

    def window(offset):
        shift_by = offset - 2
        if shift_by > 0:
            return jnp.concatenate(
                [lax.slice_in_dim(differences, shift_by, extent, axis=along)]
                + [high_edge] * shift_by,
                axis=along,
            )
        if shift_by < 0:
            return jnp.concatenate(
                [low_edge] * -shift_by
                + [lax.slice_in_dim(differences, 0, extent + shift_by, axis=along)],
                axis=along,
            )
        return differences

    return both_sides(window)


def edge_fill(field, along, margin, at_low, at_high):
    extent = field.shape[along]
    shape_dist = [1] * field.ndim
    shape_dist[along] = margin
    inner_low = lax.slice_in_dim(field, margin, margin + 1, axis=along)
    next_low = lax.slice_in_dim(field, margin + 1, margin + 2, axis=along)
    dist_low = jnp.arange(margin, 0, -1).astype(jnp.float32).reshape(tuple(shape_dist))
    low_fill = inner_low + dist_low * (inner_low - next_low)
    inner_high = lax.slice_in_dim(field, extent - margin - 1, extent - margin, axis=along)
    next_high = lax.slice_in_dim(field, extent - margin - 2, extent - margin - 1, axis=along)
    dist_high = jnp.arange(1, margin + 1).astype(jnp.float32).reshape(tuple(shape_dist))
    high_fill = inner_high + dist_high * (inner_high - next_high)
    new_low = jnp.where(at_low, low_fill, lax.slice_in_dim(field, 0, margin, axis=along))
    new_high = jnp.where(
        at_high, high_fill, lax.slice_in_dim(field, extent - margin, extent, axis=along)
    )
    middle = lax.slice_in_dim(field, margin, extent - margin, axis=along)
    return jnp.concatenate([new_low, middle, new_high], axis=along)


def speed_bounds(drift_field, x_coord, y_coord, turn_a, along_one, along_two):
    first_hi = jnp.max(along_one)
    first_lo = jnp.min(along_one)
    second_hi = jnp.max(along_two)
    second_lo = jnp.min(along_two)
    bound_one = jnp.max(
        jnp.maximum(drift_field[0] + first_hi, -(drift_field[0] + first_lo))
        + turn_a * jnp.abs(y_coord)[None, :]
    )
    bound_two = jnp.max(
        jnp.maximum(drift_field[1] + second_hi, -(drift_field[1] + second_lo))
        + turn_a * jnp.abs(x_coord)[:, None]
    )
    return (bound_one, bound_two)


def hamilton_rate(
    backs, fores, x_coord, y_coord, flow_x, flow_y, along_one, along_two, params, alphas
):
    mean_one = 0.5 * (backs[0] + fores[0])
    mean_two = 0.5 * (backs[1] + fores[1])
    mean_three = 0.5 * (backs[2] + fores[2])
    mean_four = 0.5 * (backs[3] + fores[3])
    x_col = x_coord[:, None, None, None]
    y_col = y_coord[None, :, None, None]
    ham = mean_one * (along_one[None, None] + flow_x[:, :, None, None])
    ham = ham + mean_two * (along_two[None, None] + flow_y[:, :, None, None])
    ham = ham + params[1] * jnp.abs(mean_one * y_col - mean_two * x_col - mean_three)
    ham = ham - params[2] * jnp.abs(mean_three) + params[3] * jnp.abs(mean_four)
    dissipation = alphas[0] * (fores[0] - backs[0]) + alphas[1] * (fores[1] - backs[1])
    dissipation = (
        dissipation + alphas[2] * (fores[2] - backs[2]) + alphas[3] * (fores[3] - backs[3])
    )
    return ham + 0.5 * dissipation


def exchange(field, width):
    pieces = []
    for axis, dim in (("gx", 0), ("gy", 1)):
        extent = field.shape[dim]
        pieces.append(lax.slice_in_dim(field, extent - width, extent, axis=dim))
        pieces.append(lax.slice_in_dim(field, 0, width, axis=dim))
    *pieces, field = lax.optimization_barrier((*pieces, field))
    moved = []
    for index, (axis, dim) in enumerate((("gx", 0), ("gy", 1))):
        count = lax.axis_size(axis)
        ends = count - 1
        tail, head = pieces[2 * index], pieces[2 * index + 1]
        moved.append(lax.ppermute(tail, axis, [(i, (i + 1) % count) for i in range(ends)]))
        moved.append(lax.ppermute(head, axis, [((i + 1) % count, i) for i in range(ends)]))
    return moved, field


def spread_max(local, axes):
    count = 1
    for axis in axes:
        count *= lax.axis_size(axis)
    span = 1
    while span < count:
        moved = [
            lax.ppermute(local, axes, [(i, (i + k * span) % count) for i in range(count)])
            for k in range(1, 4)
            if k * span < count
        ]
        for item in moved:
            local = jnp.maximum(local, item)
        span *= 4
    return local


def on_device(values, drift, params):
    cells_x, cells_y, n_psi, n_speed = values.shape
    devices_x = lax.axis_size("gx")
    devices_y = lax.axis_size("gy")
    total_x = cells_x * devices_x
    total_y = cells_y * devices_y
    step_psi = 2.0 * math.pi / n_psi
    step_speed = 1.0 / n_speed
    place_x = lax.axis_index("gx")
    place_y = lax.axis_index("gy")
    first_x = place_x == 0
    last_x = place_x == devices_x - 1
    first_y = place_y == 0
    last_y = place_y == devices_y - 1
    psi_grid = jnp.arange(n_psi).astype(jnp.float32) * step_psi - math.pi
    speed_grid = 0.5 + (jnp.arange(n_speed).astype(jnp.float32) + 0.5) * step_speed
    along_one = -speed_grid[None, :] + params[0] * jnp.cos(psi_grid)[:, None]
    along_two = params[0] * jnp.sin(psi_grid)[:, None]
    y_coord = (
        (place_y * cells_y + jnp.arange(cells_y)).astype(jnp.float32) + 0.5 - 0.5 * total_y
    ) * cell_span
    x_coord = (
        (place_x * cells_x + jnp.arange(cells_x)).astype(jnp.float32) + 0.5 - 0.5 * total_x
    ) * cell_span
    local_one, local_two = speed_bounds(drift, x_coord, y_coord, params[1], along_one, along_two)
    bounds = spread_max(jnp.stack([local_one, local_two]), ("gx", "gy"))
    bound_one = bounds[0]
    bound_two = bounds[1]
    alpha_three = params[1] + params[2]
    alpha_four = params[3]
    step_time = cfl_number / (
        bound_one / cell_span
        + bound_two / cell_span
        + alpha_three / step_psi
        + alpha_four / step_speed
    )
    x_col = x_coord[:, None, None, None]
    y_col = y_coord[None, :, None, None]
    flow_x = drift[0][:, :, None, None]
    flow_y = drift[1][:, :, None, None]

    def local_part(field):
        back_three, fore_three = periodic_sided(field, 2, step_psi)
        back_four, fore_four = clamped_sided(field, 3, step_speed)
        mean_three = 0.5 * (back_three + fore_three)
        mean_four = 0.5 * (back_four + fore_four)
        partial = -params[2] * jnp.abs(mean_three) + params[3] * jnp.abs(mean_four)
        partial = partial + 0.5 * (
            alpha_three * (fore_three - back_three) + alpha_four * (fore_four - back_four)
        )
        return lax.optimization_barrier((mean_three, partial))

    def section_parts(field):
        (low_x, high_x, low_y, high_y), field = exchange(field, 3)
        mean_three, partial = local_part(field)
        wide_x = edge_fill(jnp.concatenate([low_x, field, high_x], axis=0), 0, 3, first_x, last_x)
        back_one, fore_one = one_sided(wide_x, 0, cell_span, cells_x)
        wide_y = edge_fill(jnp.concatenate([low_y, field, high_y], axis=1), 1, 3, first_y, last_y)
        back_two, fore_two = one_sided(wide_y, 1, cell_span, cells_y)
        mean_one = 0.5 * (back_one + fore_one)
        mean_two = 0.5 * (back_two + fore_two)
        ham = mean_one * (along_one[None, None] + flow_x)
        ham = ham + mean_two * (along_two[None, None] + flow_y)
        ham = ham + params[1] * jnp.abs(mean_one * y_col - mean_two * x_col - mean_three)
        return ham + partial, fore_one - back_one, fore_two - back_two

    def combine(ham, spread_one, spread_two):
        return ham + 0.5 * (bound_one * spread_one + bound_two * spread_two)

    def section_rate(field):
        return combine(*section_parts(field))

    early = lax.optimization_barrier(section_parts(values))
    first = values + step_time * combine(*early)
    second = 0.75 * values + 0.25 * (first + step_time * section_rate(first))
    result = values * (1.0 / 3.0) + 2.0 / 3.0 * (second + step_time * section_rate(second))
    return result


def solution(mesh):
    in_specs = (P(("groups", "gx"), "gy", None, None), P(None, ("groups", "gx"), "gy"), P("groups"))
    out_specs = P(("groups", "gx"), "gy", None, None)
    return jax.shard_map(
        on_device, mesh=mesh, in_specs=in_specs, out_specs=out_specs, check_vma=False
    )
```

```python
import math

import jax
import jax.numpy as jnp
from jax import lax
from jax.sharding import PartitionSpec as P


cfl_number = 0.5
weno_eps = 1e-06
cell_span = 1.0 / 64.0


def weno_value(first, second, third, fourth, fifth):
    stencil_one = first / 3.0 - 7.0 * second / 6.0 + 11.0 * third / 6.0
    stencil_two = -second / 6.0 + 5.0 * third / 6.0 + fourth / 3.0
    stencil_three = third / 3.0 + 5.0 * fourth / 6.0 - fifth / 6.0
    smooth_one = (
        13.0 / 12.0 * (first - 2.0 * second + third) ** 2
        + 0.25 * (first - 4.0 * second + 3.0 * third) ** 2
    )
    smooth_two = 13.0 / 12.0 * (second - 2.0 * third + fourth) ** 2 + 0.25 * (second - fourth) ** 2
    smooth_three = (
        13.0 / 12.0 * (third - 2.0 * fourth + fifth) ** 2
        + 0.25 * (3.0 * third - 4.0 * fourth + fifth) ** 2
    )
    weight_one = 0.1 / (weno_eps + smooth_one) ** 2
    weight_two = 0.6 / (weno_eps + smooth_two) ** 2
    weight_three = 0.3 / (weno_eps + smooth_three) ** 2
    total = weight_one * stencil_one + weight_two * stencil_two + weight_three * stencil_three
    return total / (weight_one + weight_two + weight_three)


def both_sides(window):
    backward = weno_value(window(0), window(1), window(2), window(3), window(4))
    forward = weno_value(window(5), window(4), window(3), window(2), window(1))
    return (backward, forward)


def one_sided(padded, along, spacing, length):
    extent = padded.shape[along]
    differences = (
        lax.slice_in_dim(padded, 1, extent, axis=along)
        - lax.slice_in_dim(padded, 0, extent - 1, axis=along)
    ) / spacing

    def window(offset):
        return lax.slice_in_dim(differences, offset, offset + length, axis=along)

    return both_sides(window)


def periodic_sided(field, along, spacing):
    differences = (field - jnp.roll(field, 1, axis=along)) / spacing

    def window(offset):
        return jnp.roll(differences, 2 - offset, axis=along)

    return both_sides(window)


def clamped_sided(field, along, spacing):
    extent = field.shape[along]
    inner = (
        lax.slice_in_dim(field, 1, extent, axis=along)
        - lax.slice_in_dim(field, 0, extent - 1, axis=along)
    ) / spacing
    differences = jnp.concatenate([lax.slice_in_dim(inner, 0, 1, axis=along), inner], axis=along)
    low_edge = lax.slice_in_dim(differences, 0, 1, axis=along)
    high_edge = lax.slice_in_dim(differences, extent - 1, extent, axis=along)

    def window(offset):
        shift_by = offset - 2
        if shift_by > 0:
            return jnp.concatenate(
                [lax.slice_in_dim(differences, shift_by, extent, axis=along)]
                + [high_edge] * shift_by,
                axis=along,
            )
        if shift_by < 0:
            return jnp.concatenate(
                [low_edge] * -shift_by
                + [lax.slice_in_dim(differences, 0, extent + shift_by, axis=along)],
                axis=along,
            )
        return differences

    return both_sides(window)


def speed_bounds(drift_field, x_coord, y_coord, turn_a, along_one, along_two):
    first_hi = jnp.max(along_one)
    first_lo = jnp.min(along_one)
    second_hi = jnp.max(along_two)
    second_lo = jnp.min(along_two)
    bound_one = jnp.max(
        jnp.maximum(drift_field[0] + first_hi, -(drift_field[0] + first_lo))
        + turn_a * jnp.abs(y_coord)[None, :]
    )
    bound_two = jnp.max(
        jnp.maximum(drift_field[1] + second_hi, -(drift_field[1] + second_lo))
        + turn_a * jnp.abs(x_coord)[:, None]
    )
    return (bound_one, bound_two)


def send_low(piece, axis):
    count = lax.axis_size(axis)
    return lax.ppermute(piece, axis, [(i, (i + 1) % count) for i in range(count - 1)])


def send_high(piece, axis):
    count = lax.axis_size(axis)
    return lax.ppermute(piece, axis, [((i + 1) % count, i) for i in range(count - 1)])


def ghost_low(field, halo, at_low, along):
    shape_dist = [1] * field.ndim
    shape_dist[along] = 3
    inner = lax.slice_in_dim(field, 0, 1, axis=along)
    after = lax.slice_in_dim(field, 1, 2, axis=along)
    dist = jnp.arange(3, 0, -1).astype(jnp.float32).reshape(tuple(shape_dist))
    return jnp.where(at_low, inner + dist * (inner - after), halo)


def ghost_high(field, halo, at_high, along):
    extent = field.shape[along]
    shape_dist = [1] * field.ndim
    shape_dist[along] = 3
    inner = lax.slice_in_dim(field, extent - 1, extent, axis=along)
    before = lax.slice_in_dim(field, extent - 2, extent - 1, axis=along)
    dist = jnp.arange(1, 4).astype(jnp.float32).reshape(tuple(shape_dist))
    return jnp.where(at_high, inner + dist * (inner - before), halo)


def spread_max(local, axes):
    count = 1
    for axis in axes:
        count *= lax.axis_size(axis)
    span = 1
    while span < count:
        moved = [
            lax.ppermute(local, axes, [(i, (i + k * span) % count) for i in range(count)])
            for k in range(1, 4)
            if k * span < count
        ]
        for item in moved:
            local = jnp.maximum(local, item)
        span *= 4
    return local


def on_device(values, drift, params):
    cells_x, cells_y, n_psi, n_speed = values.shape
    devices_x = lax.axis_size("gx")
    devices_y = lax.axis_size("gy")
    total_x = cells_x * devices_x
    total_y = cells_y * devices_y
    step_psi = 2.0 * math.pi / n_psi
    step_speed = 1.0 / n_speed
    place_x = lax.axis_index("gx")
    place_y = lax.axis_index("gy")
    first_x = place_x == 0
    last_x = place_x == devices_x - 1
    first_y = place_y == 0
    last_y = place_y == devices_y - 1
    half = cells_x // 2
    alpha_three = params[1] + params[2]
    alpha_four = params[3]

    def cut(array, side):
        return array[:half] if side == 0 else array[half:]

    def local_part(field):
        back_three, fore_three = periodic_sided(field, 2, step_psi)
        back_four, fore_four = clamped_sided(field, 3, step_speed)
        mean_three = 0.5 * (back_three + fore_three)
        mean_four = 0.5 * (back_four + fore_four)
        partial = -params[2] * jnp.abs(mean_three) + params[3] * jnp.abs(mean_four)
        partial = partial + 0.5 * (
            alpha_three * (fore_three - back_three) + alpha_four * (fore_four - back_four)
        )
        return mean_three, partial

    def local_halves(field):
        pieces = []
        for side in (0, 1):
            pieces.append(lax.optimization_barrier(local_part(cut(field, side))))
        return pieces

    def y_halo(field):
        tail = lax.slice_in_dim(field, cells_y - 3, cells_y, axis=1)
        head = lax.slice_in_dim(field, 0, 3, axis=1)
        tail, head = lax.optimization_barrier((tail, head))
        return send_low(tail, "gy"), send_high(head, "gy")

    x_halos = (send_low(values[cells_x - 3 :], "gx"), send_high(values[:3], "gx"))
    y_halos = y_halo(values)
    psi_grid = jnp.arange(n_psi).astype(jnp.float32) * step_psi - math.pi
    speed_grid = 0.5 + (jnp.arange(n_speed).astype(jnp.float32) + 0.5) * step_speed
    along_one = -speed_grid[None, :] + params[0] * jnp.cos(psi_grid)[:, None]
    along_two = params[0] * jnp.sin(psi_grid)[:, None]
    y_coord = (
        (place_y * cells_y + jnp.arange(cells_y)).astype(jnp.float32) + 0.5 - 0.5 * total_y
    ) * cell_span
    x_coord = (
        (place_x * cells_x + jnp.arange(cells_x)).astype(jnp.float32) + 0.5 - 0.5 * total_x
    ) * cell_span
    local_one, local_two = speed_bounds(drift, x_coord, y_coord, params[1], along_one, along_two)
    bounds = spread_max(jnp.stack([local_one, local_two]), ("gx", "gy"))
    locals_now = local_halves(values)
    bound_one = bounds[0]
    bound_two = bounds[1]
    step_time = cfl_number / (
        bound_one / cell_span
        + bound_two / cell_span
        + alpha_three / step_psi
        + alpha_four / step_speed
    )
    x_col = x_coord[:, None, None, None]
    y_col = y_coord[None, :, None, None]
    flow_x = drift[0][:, :, None, None]
    flow_y = drift[1][:, :, None, None]

    def half_parts(field, side, x_halo, y_low, y_high, mean_three, partial):
        if side == 0:
            start, stop = 0, half
            ghost = ghost_low(field, x_halo, first_x, 0)
            wide_x = jnp.concatenate([ghost, field[: half + 3]], axis=0)
        else:
            start, stop = half, cells_x
            ghost = ghost_high(field, x_halo, last_x, 0)
            wide_x = jnp.concatenate([field[half - 3 :], ghost], axis=0)
        back_one, fore_one = one_sided(wide_x, 0, cell_span, stop - start)
        part = field[start:stop]
        wide_y = jnp.concatenate(
            [
                ghost_low(part, y_low[start:stop], first_y, 1),
                part,
                ghost_high(part, y_high[start:stop], last_y, 1),
            ],
            axis=1,
        )
        back_two, fore_two = one_sided(wide_y, 1, cell_span, cells_y)
        mean_one = 0.5 * (back_one + fore_one)
        mean_two = 0.5 * (back_two + fore_two)
        ham = mean_one * (along_one[None, None] + flow_x[start:stop])
        ham = ham + mean_two * (along_two[None, None] + flow_y[start:stop])
        ham = ham + params[1] * jnp.abs(mean_one * y_col - mean_two * x_col[start:stop] - mean_three)
        ham = ham + partial
        spread = 0.5 * (bound_one * (fore_one - back_one) + bound_two * (fore_two - back_two))
        return ham + spread

    def stage(field, x_halos, y_halos, local_pieces, order, update, last):
        results = [None, None]
        sent = [None, None]
        for side in order:
            rate = half_parts(field, side, x_halos[side], *y_halos, *local_pieces[side])
            results[side] = update(side, rate)
            if last:
                continue
            if side == 0:
                piece = lax.optimization_barrier(results[side][:3])
                sent[side] = send_high(piece, "gx")
            else:
                piece = lax.optimization_barrier(results[side][results[side].shape[0] - 3 :])
                sent[side] = send_low(piece, "gx")
        merged = jnp.concatenate(results, axis=0)
        if last:
            return merged, None, None, None
        next_y = y_halo(merged)
        next_pieces = local_halves(merged)
        return merged, (sent[1], sent[0]), next_y, next_pieces

    first, x_halos, y_halos, locals_now = stage(
        values, x_halos, y_halos, locals_now, (1, 0),
        lambda side, rate: cut(values, side) + step_time * rate, False,
    )
    second, x_halos, y_halos, locals_now = stage(
        first, x_halos, y_halos, locals_now, (0, 1),
        lambda side, rate: 0.75 * cut(values, side) + 0.25 * (cut(first, side) + step_time * rate),
        False,
    )
    result, _, _, _ = stage(
        second, x_halos, y_halos, locals_now, (1, 0),
        lambda side, rate: cut(values, side) * (1.0 / 3.0)
        + 2.0 / 3.0 * (cut(second, side) + step_time * rate),
        True,
    )
    return result


def solution(mesh):
    in_specs = (P(("groups", "gx"), "gy", None, None), P(None, ("groups", "gx"), "gy"), P("groups"))
    out_specs = P(("groups", "gx"), "gy", None, None)
    return jax.shard_map(
        on_device, mesh=mesh, in_specs=in_specs, out_specs=out_specs, check_vma=False
    )
```

```python
import math

import jax
import jax.numpy as jnp
from jax import lax
from jax.sharding import PartitionSpec as P


cfl_number = 0.5
weno_eps = 1e-06
cell_span = 1.0 / 64.0


def weno_value(first, second, third, fourth, fifth):
    stencil_one = first / 3.0 - 7.0 * second / 6.0 + 11.0 * third / 6.0
    stencil_two = -second / 6.0 + 5.0 * third / 6.0 + fourth / 3.0
    stencil_three = third / 3.0 + 5.0 * fourth / 6.0 - fifth / 6.0
    smooth_one = (
        13.0 / 12.0 * (first - 2.0 * second + third) ** 2
        + 0.25 * (first - 4.0 * second + 3.0 * third) ** 2
    )
    smooth_two = 13.0 / 12.0 * (second - 2.0 * third + fourth) ** 2 + 0.25 * (second - fourth) ** 2
    smooth_three = (
        13.0 / 12.0 * (third - 2.0 * fourth + fifth) ** 2
        + 0.25 * (3.0 * third - 4.0 * fourth + fifth) ** 2
    )
    weight_one = 0.1 / (weno_eps + smooth_one) ** 2
    weight_two = 0.6 / (weno_eps + smooth_two) ** 2
    weight_three = 0.3 / (weno_eps + smooth_three) ** 2
    total = weight_one * stencil_one + weight_two * stencil_two + weight_three * stencil_three
    return total / (weight_one + weight_two + weight_three)


def both_sides(window):
    backward = weno_value(window(0), window(1), window(2), window(3), window(4))
    forward = weno_value(window(5), window(4), window(3), window(2), window(1))
    return (backward, forward)


def one_sided(padded, along, spacing, length):
    extent = padded.shape[along]
    differences = (
        lax.slice_in_dim(padded, 1, extent, axis=along)
        - lax.slice_in_dim(padded, 0, extent - 1, axis=along)
    ) / spacing

    def window(offset):
        return lax.slice_in_dim(differences, offset, offset + length, axis=along)

    return both_sides(window)


def periodic_sided(field, along, spacing):
    extent = field.shape[along]
    wrapped = jnp.concatenate(
        [
            lax.slice_in_dim(field, extent - 3, extent, axis=along),
            field,
            lax.slice_in_dim(field, 0, 3, axis=along),
        ],
        axis=along,
    )
    return one_sided(wrapped, along, spacing, extent)


def clamped_sided(field, along, spacing):
    extent = field.shape[along]
    inner = (
        lax.slice_in_dim(field, 1, extent, axis=along)
        - lax.slice_in_dim(field, 0, extent - 1, axis=along)
    ) / spacing
    differences = jnp.concatenate([lax.slice_in_dim(inner, 0, 1, axis=along), inner], axis=along)
    low_edge = lax.slice_in_dim(differences, 0, 1, axis=along)
    high_edge = lax.slice_in_dim(differences, extent - 1, extent, axis=along)

    def window(offset):
        shift_by = offset - 2
        if shift_by > 0:
            return jnp.concatenate(
                [lax.slice_in_dim(differences, shift_by, extent, axis=along)]
                + [high_edge] * shift_by,
                axis=along,
            )
        if shift_by < 0:
            return jnp.concatenate(
                [low_edge] * -shift_by
                + [lax.slice_in_dim(differences, 0, extent + shift_by, axis=along)],
                axis=along,
            )
        return differences

    return both_sides(window)


def speed_bounds(drift_field, x_coord, y_coord, turn_a, along_one, along_two):
    first_hi = jnp.max(along_one)
    first_lo = jnp.min(along_one)
    second_hi = jnp.max(along_two)
    second_lo = jnp.min(along_two)
    bound_one = jnp.max(
        jnp.maximum(drift_field[0] + first_hi, -(drift_field[0] + first_lo))
        + turn_a * jnp.abs(y_coord)[None, :]
    )
    bound_two = jnp.max(
        jnp.maximum(drift_field[1] + second_hi, -(drift_field[1] + second_lo))
        + turn_a * jnp.abs(x_coord)[:, None]
    )
    return (bound_one, bound_two)


def send_low(piece, axis):
    count = lax.axis_size(axis)
    return lax.ppermute(piece, axis, [(i, (i + 1) % count) for i in range(count - 1)])


def send_high(piece, axis):
    count = lax.axis_size(axis)
    return lax.ppermute(piece, axis, [((i + 1) % count, i) for i in range(count - 1)])


def ghost_low(field, halo, at_low, along):
    shape_dist = [1] * field.ndim
    shape_dist[along] = 3
    inner = lax.slice_in_dim(field, 0, 1, axis=along)
    after = lax.slice_in_dim(field, 1, 2, axis=along)
    dist = jnp.arange(3, 0, -1).astype(jnp.float32).reshape(tuple(shape_dist))
    return jnp.where(at_low, inner + dist * (inner - after), halo)


def ghost_high(field, halo, at_high, along):
    extent = field.shape[along]
    shape_dist = [1] * field.ndim
    shape_dist[along] = 3
    inner = lax.slice_in_dim(field, extent - 1, extent, axis=along)
    before = lax.slice_in_dim(field, extent - 2, extent - 1, axis=along)
    dist = jnp.arange(1, 4).astype(jnp.float32).reshape(tuple(shape_dist))
    return jnp.where(at_high, inner + dist * (inner - before), halo)


def spread_max(local, axes):
    count = 1
    for axis in axes:
        count *= lax.axis_size(axis)
    span = 1
    while span < count:
        moved = [
            lax.ppermute(local, axes, [(i, (i + k * span) % count) for i in range(count)])
            for k in range(1, 4)
            if k * span < count
        ]
        for item in moved:
            local = jnp.maximum(local, item)
        span *= 4
    return local


def on_device(values, drift, params):
    cells_x, cells_y, n_psi, n_speed = values.shape
    devices_x = lax.axis_size("gx")
    devices_y = lax.axis_size("gy")
    total_x = cells_x * devices_x
    total_y = cells_y * devices_y
    step_psi = 2.0 * math.pi / n_psi
    step_speed = 1.0 / n_speed
    place_x = lax.axis_index("gx")
    place_y = lax.axis_index("gy")
    first_x = place_x == 0
    last_x = place_x == devices_x - 1
    first_y = place_y == 0
    last_y = place_y == devices_y - 1
    half = cells_x // 2
    alpha_three = params[1] + params[2]
    alpha_four = params[3]

    def cut(array, side):
        return array[:half] if side == 0 else array[half:]

    def local_part(field):
        back_three, fore_three = periodic_sided(field, 2, step_psi)
        back_four, fore_four = clamped_sided(field, 3, step_speed)
        mean_three = 0.5 * (back_three + fore_three)
        mean_four = 0.5 * (back_four + fore_four)
        partial = -params[2] * jnp.abs(mean_three) + params[3] * jnp.abs(mean_four)
        partial = partial + 0.5 * (
            alpha_three * (fore_three - back_three) + alpha_four * (fore_four - back_four)
        )
        return mean_three, partial

    def local_halves(field):
        pieces = []
        for side in (0, 1):
            pieces.append(lax.optimization_barrier(local_part(cut(field, side))))
        return pieces

    def y_halo(field):
        tail = lax.slice_in_dim(field, cells_y - 3, cells_y, axis=1)
        head = lax.slice_in_dim(field, 0, 3, axis=1)
        if devices_y == 2:
            piece = lax.optimization_barrier(jnp.where(first_y, tail, head))
            swapped = lax.ppermute(piece, "gy", [(0, 1), (1, 0)])
            return swapped, swapped
        tail, head = lax.optimization_barrier((tail, head))
        return send_low(tail, "gy"), send_high(head, "gy")

    def local_whole(field):
        mean_three, partial = lax.optimization_barrier(local_part(field))
        return [(cut(mean_three, side), cut(partial, side)) for side in (0, 1)]

    x_halos = (send_low(values[cells_x - 3 :], "gx"), send_high(values[:3], "gx"))
    y_halos = y_halo(values)
    psi_grid = jnp.arange(n_psi).astype(jnp.float32) * step_psi - math.pi
    speed_grid = 0.5 + (jnp.arange(n_speed).astype(jnp.float32) + 0.5) * step_speed
    along_one = -speed_grid[None, :] + params[0] * jnp.cos(psi_grid)[:, None]
    along_two = params[0] * jnp.sin(psi_grid)[:, None]
    y_coord = (
        (place_y * cells_y + jnp.arange(cells_y)).astype(jnp.float32) + 0.5 - 0.5 * total_y
    ) * cell_span
    x_coord = (
        (place_x * cells_x + jnp.arange(cells_x)).astype(jnp.float32) + 0.5 - 0.5 * total_x
    ) * cell_span
    local_one, local_two = speed_bounds(drift, x_coord, y_coord, params[1], along_one, along_two)
    bounds = spread_max(jnp.stack([local_one, local_two]), ("gx", "gy"))
    locals_now = local_halves(values)
    bound_one = bounds[0]
    bound_two = bounds[1]
    step_time = cfl_number / (
        bound_one / cell_span
        + bound_two / cell_span
        + alpha_three / step_psi
        + alpha_four / step_speed
    )
    x_col = x_coord[:, None, None, None]
    y_col = y_coord[None, :, None, None]
    flow_x = drift[0][:, :, None, None]
    flow_y = drift[1][:, :, None, None]

    def half_parts(field, side, x_halo, y_low, y_high, mean_three, partial):
        if side == 0:
            start, stop = 0, half
            ghost = ghost_low(field, x_halo, first_x, 0)
            wide_x = jnp.concatenate([ghost, field[: half + 3]], axis=0)
        else:
            start, stop = half, cells_x
            ghost = ghost_high(field, x_halo, last_x, 0)
            wide_x = jnp.concatenate([field[half - 3 :], ghost], axis=0)
        back_one, fore_one = one_sided(wide_x, 0, cell_span, stop - start)
        part = field[start:stop]
        wide_y = jnp.concatenate(
            [
                ghost_low(part, y_low[start:stop], first_y, 1),
                part,
                ghost_high(part, y_high[start:stop], last_y, 1),
            ],
            axis=1,
        )
        back_two, fore_two = one_sided(wide_y, 1, cell_span, cells_y)
        mean_one = 0.5 * (back_one + fore_one)
        mean_two = 0.5 * (back_two + fore_two)
        ham = mean_one * (along_one[None, None] + flow_x[start:stop])
        ham = ham + mean_two * (along_two[None, None] + flow_y[start:stop])
        ham = ham + params[1] * jnp.abs(mean_one * y_col - mean_two * x_col[start:stop] - mean_three)
        ham = ham + partial
        spread = 0.5 * (bound_one * (fore_one - back_one) + bound_two * (fore_two - back_two))
        return ham + spread

    def stage(field, x_halos, y_halos, local_pieces, order, update, last):
        results = [None, None]
        sent = [None, None]
        for side in order:
            rate = half_parts(field, side, x_halos[side], *y_halos, *local_pieces[side])
            results[side] = update(side, rate)
            if last:
                continue
            if side == 0:
                piece = lax.optimization_barrier(results[side][:3])
                sent[side] = send_high(piece, "gx")
            else:
                piece = lax.optimization_barrier(results[side][results[side].shape[0] - 3 :])
                sent[side] = send_low(piece, "gx")
        merged = jnp.concatenate(results, axis=0)
        if last:
            return merged, None, None, None
        next_y = y_halo(merged)
        next_pieces = local_whole(merged)
        return merged, (sent[1], sent[0]), next_y, next_pieces

    first, x_halos, y_halos, locals_now = stage(
        values, x_halos, y_halos, locals_now, (1, 0),
        lambda side, rate: cut(values, side) + step_time * rate, False,
    )
    second, x_halos, y_halos, locals_now = stage(
        first, x_halos, y_halos, locals_now, (0, 1),
        lambda side, rate: 0.75 * cut(values, side) + 0.25 * (cut(first, side) + step_time * rate),
        False,
    )
    result, _, _, _ = stage(
        second, x_halos, y_halos, locals_now, (1, 0),
        lambda side, rate: cut(values, side) * (1.0 / 3.0)
        + 2.0 / 3.0 * (cut(second, side) + step_time * rate),
        True,
    )
    return result


def solution(mesh):
    in_specs = (P(("groups", "gx"), "gy", None, None), P(None, ("groups", "gx"), "gy"), P("groups"))
    out_specs = P(("groups", "gx"), "gy", None, None)
    return jax.shard_map(
        on_device, mesh=mesh, in_specs=in_specs, out_specs=out_specs, check_vma=False
    )
```

```python
import math

import jax
import jax.numpy as jnp
from jax import lax
from jax.sharding import PartitionSpec as P


cfl_number = 0.5
weno_eps = 1e-06
cell_span = 1.0 / 64.0


def weno_value(first, second, third, fourth, fifth):
    stencil_one = first / 3.0 - 7.0 * second / 6.0 + 11.0 * third / 6.0
    stencil_two = -second / 6.0 + 5.0 * third / 6.0 + fourth / 3.0
    stencil_three = third / 3.0 + 5.0 * fourth / 6.0 - fifth / 6.0
    smooth_one = (
        13.0 / 12.0 * (first - 2.0 * second + third) ** 2
        + 0.25 * (first - 4.0 * second + 3.0 * third) ** 2
    )
    smooth_two = 13.0 / 12.0 * (second - 2.0 * third + fourth) ** 2 + 0.25 * (second - fourth) ** 2
    smooth_three = (
        13.0 / 12.0 * (third - 2.0 * fourth + fifth) ** 2
        + 0.25 * (3.0 * third - 4.0 * fourth + fifth) ** 2
    )
    weight_one = 0.1 / (weno_eps + smooth_one) ** 2
    weight_two = 0.6 / (weno_eps + smooth_two) ** 2
    weight_three = 0.3 / (weno_eps + smooth_three) ** 2
    total = weight_one * stencil_one + weight_two * stencil_two + weight_three * stencil_three
    return total / (weight_one + weight_two + weight_three)


def both_sides(window):
    backward = weno_value(window(0), window(1), window(2), window(3), window(4))
    forward = weno_value(window(5), window(4), window(3), window(2), window(1))
    return (backward, forward)


def one_sided(padded, along, spacing, length):
    extent = padded.shape[along]
    differences = (
        lax.slice_in_dim(padded, 1, extent, axis=along)
        - lax.slice_in_dim(padded, 0, extent - 1, axis=along)
    ) / spacing

    def window(offset):
        return lax.slice_in_dim(differences, offset, offset + length, axis=along)

    return both_sides(window)


def periodic_sided(field, along, spacing):
    extent = field.shape[along]
    wrapped = jnp.concatenate(
        [
            lax.slice_in_dim(field, extent - 3, extent, axis=along),
            field,
            lax.slice_in_dim(field, 0, 3, axis=along),
        ],
        axis=along,
    )
    return one_sided(wrapped, along, spacing, extent)


def clamped_sided(field, along, spacing):
    extent = field.shape[along]
    inner = (
        lax.slice_in_dim(field, 1, extent, axis=along)
        - lax.slice_in_dim(field, 0, extent - 1, axis=along)
    ) / spacing
    differences = jnp.concatenate([lax.slice_in_dim(inner, 0, 1, axis=along), inner], axis=along)
    low_edge = lax.slice_in_dim(differences, 0, 1, axis=along)
    high_edge = lax.slice_in_dim(differences, extent - 1, extent, axis=along)

    def window(offset):
        shift_by = offset - 2
        if shift_by > 0:
            return jnp.concatenate(
                [lax.slice_in_dim(differences, shift_by, extent, axis=along)]
                + [high_edge] * shift_by,
                axis=along,
            )
        if shift_by < 0:
            return jnp.concatenate(
                [low_edge] * -shift_by
                + [lax.slice_in_dim(differences, 0, extent + shift_by, axis=along)],
                axis=along,
            )
        return differences

    return both_sides(window)


def speed_bounds(drift_field, x_coord, y_coord, turn_a, along_one, along_two):
    first_hi = jnp.max(along_one)
    first_lo = jnp.min(along_one)
    second_hi = jnp.max(along_two)
    second_lo = jnp.min(along_two)
    bound_one = jnp.max(
        jnp.maximum(drift_field[0] + first_hi, -(drift_field[0] + first_lo))
        + turn_a * jnp.abs(y_coord)[None, :]
    )
    bound_two = jnp.max(
        jnp.maximum(drift_field[1] + second_hi, -(drift_field[1] + second_lo))
        + turn_a * jnp.abs(x_coord)[:, None]
    )
    return (bound_one, bound_two)


def send_low(piece, axis):
    count = lax.axis_size(axis)
    return lax.ppermute(piece, axis, [(i, (i + 1) % count) for i in range(count - 1)])


def send_high(piece, axis):
    count = lax.axis_size(axis)
    return lax.ppermute(piece, axis, [((i + 1) % count, i) for i in range(count - 1)])


def ghost_low(field, halo, at_low, along):
    shape_dist = [1] * field.ndim
    shape_dist[along] = 3
    inner = lax.slice_in_dim(field, 0, 1, axis=along)
    after = lax.slice_in_dim(field, 1, 2, axis=along)
    dist = jnp.arange(3, 0, -1).astype(jnp.float32).reshape(tuple(shape_dist))
    return jnp.where(at_low, inner + dist * (inner - after), halo)


def ghost_high(field, halo, at_high, along):
    extent = field.shape[along]
    shape_dist = [1] * field.ndim
    shape_dist[along] = 3
    inner = lax.slice_in_dim(field, extent - 1, extent, axis=along)
    before = lax.slice_in_dim(field, extent - 2, extent - 1, axis=along)
    dist = jnp.arange(1, 4).astype(jnp.float32).reshape(tuple(shape_dist))
    return jnp.where(at_high, inner + dist * (inner - before), halo)


def spread_max(local, axes):
    count = 1
    for axis in axes:
        count *= lax.axis_size(axis)
    span = 1
    while span < count:
        moved = [
            lax.ppermute(local, axes, [(i, (i + k * span) % count) for i in range(count)])
            for k in range(1, 4)
            if k * span < count
        ]
        for item in moved:
            local = jnp.maximum(local, item)
        span *= 4
    return local


def on_device(values, drift, params):
    cells_x, cells_y, n_psi, n_speed = values.shape
    devices_x = lax.axis_size("gx")
    devices_y = lax.axis_size("gy")
    total_x = cells_x * devices_x
    total_y = cells_y * devices_y
    step_psi = 2.0 * math.pi / n_psi
    step_speed = 1.0 / n_speed
    place_x = lax.axis_index("gx")
    place_y = lax.axis_index("gy")
    first_x = place_x == 0
    last_x = place_x == devices_x - 1
    first_y = place_y == 0
    last_y = place_y == devices_y - 1
    half = cells_x // 2
    alpha_three = params[1] + params[2]
    alpha_four = params[3]

    def cut(array, side):
        if side == 0:
            return array[:half]
        if side == 1:
            return array[half:]
        return array

    def local_part(field):
        back_three, fore_three = periodic_sided(field, 2, step_psi)
        back_four, fore_four = clamped_sided(field, 3, step_speed)
        mean_three = 0.5 * (back_three + fore_three)
        mean_four = 0.5 * (back_four + fore_four)
        partial = -params[2] * jnp.abs(mean_three) + params[3] * jnp.abs(mean_four)
        partial = partial + 0.5 * (
            alpha_three * (fore_three - back_three) + alpha_four * (fore_four - back_four)
        )
        return mean_three, partial

    def y_halo(field):
        tail = lax.slice_in_dim(field, cells_y - 3, cells_y, axis=1)
        head = lax.slice_in_dim(field, 0, 3, axis=1)
        if devices_y == 2:
            piece = lax.optimization_barrier(jnp.where(first_y, tail, head))
            swapped = lax.ppermute(piece, "gy", [(0, 1), (1, 0)])
            return swapped, swapped
        tail, head = lax.optimization_barrier((tail, head))
        return send_low(tail, "gy"), send_high(head, "gy")

    def local_whole(field):
        return lax.optimization_barrier(local_part(field))

    x_halos = (send_low(values[cells_x - 3 :], "gx"), send_high(values[:3], "gx"))
    y_halos = y_halo(values)
    psi_grid = jnp.arange(n_psi).astype(jnp.float32) * step_psi - math.pi
    speed_grid = 0.5 + (jnp.arange(n_speed).astype(jnp.float32) + 0.5) * step_speed
    along_one = -speed_grid[None, :] + params[0] * jnp.cos(psi_grid)[:, None]
    along_two = params[0] * jnp.sin(psi_grid)[:, None]
    y_coord = (
        (place_y * cells_y + jnp.arange(cells_y)).astype(jnp.float32) + 0.5 - 0.5 * total_y
    ) * cell_span
    x_coord = (
        (place_x * cells_x + jnp.arange(cells_x)).astype(jnp.float32) + 0.5 - 0.5 * total_x
    ) * cell_span
    local_one, local_two = speed_bounds(drift, x_coord, y_coord, params[1], along_one, along_two)
    locals_now = local_whole(values)
    bounds = spread_max(jnp.stack([local_one, local_two]), ("gx", "gy"))
    bound_one = bounds[0]
    bound_two = bounds[1]
    step_time = cfl_number / (
        bound_one / cell_span
        + bound_two / cell_span
        + alpha_three / step_psi
        + alpha_four / step_speed
    )
    x_col = x_coord[:, None, None, None]
    y_col = y_coord[None, :, None, None]
    flow_x = drift[0][:, :, None, None]
    flow_y = drift[1][:, :, None, None]

    def half_parts(field, side, x_halos, y_low, y_high, mean_three, partial):
        if side == 0:
            start, stop = 0, half
            ghost = ghost_low(field, x_halos[0], first_x, 0)
            wide_x = jnp.concatenate([ghost, field[: half + 3]], axis=0)
        elif side == 1:
            start, stop = half, cells_x
            ghost = ghost_high(field, x_halos[1], last_x, 0)
            wide_x = jnp.concatenate([field[half - 3 :], ghost], axis=0)
        else:
            start, stop = 0, cells_x
            wide_x = jnp.concatenate(
                [
                    ghost_low(field, x_halos[0], first_x, 0),
                    field,
                    ghost_high(field, x_halos[1], last_x, 0),
                ],
                axis=0,
            )
        mean_three = mean_three[start:stop]
        partial = partial[start:stop]
        back_one, fore_one = one_sided(wide_x, 0, cell_span, stop - start)
        part = field[start:stop]
        wide_y = jnp.concatenate(
            [
                ghost_low(part, y_low[start:stop], first_y, 1),
                part,
                ghost_high(part, y_high[start:stop], last_y, 1),
            ],
            axis=1,
        )
        back_two, fore_two = one_sided(wide_y, 1, cell_span, cells_y)
        mean_one = 0.5 * (back_one + fore_one)
        mean_two = 0.5 * (back_two + fore_two)
        ham = mean_one * (along_one[None, None] + flow_x[start:stop])
        ham = ham + mean_two * (along_two[None, None] + flow_y[start:stop])
        ham = ham + params[1] * jnp.abs(mean_one * y_col - mean_two * x_col[start:stop] - mean_three)
        ham = ham + partial
        return ham, fore_one - back_one, fore_two - back_two

    def combine(ham, spread_one, spread_two):
        return ham + 0.5 * (bound_one * spread_one + bound_two * spread_two)

    def stage(layer, field, x_halos, y_halos, local_pieces, order, update, last):
        results = [None, None]
        sent = [None, None]
        if last:
            rate = combine(*half_parts(field, 2, x_halos, *y_halos, *local_pieces))
            return update(2, rate), None, None, None
        for position, side in enumerate(order):
            parts = half_parts(field, side, x_halos, *y_halos, *local_pieces)
            if layer == 1 and position == 0:
                parts = lax.optimization_barrier(parts)
            results[side] = update(side, combine(*parts))
            if last:
                continue
            if side == 0:
                piece = lax.optimization_barrier(results[side][:3])
                sent[side] = send_high(piece, "gx")
            else:
                piece = lax.optimization_barrier(results[side][results[side].shape[0] - 3 :])
                sent[side] = send_low(piece, "gx")
        merged = jnp.concatenate(results, axis=0)
        if last:
            return merged, None, None, None
        next_y = y_halo(merged)
        next_pieces = local_whole(merged)
        return merged, (sent[1], sent[0]), next_y, next_pieces

    first, x_halos, y_halos, locals_now = stage(
        1, values, x_halos, y_halos, locals_now, (1, 0),
        lambda side, rate: cut(values, side) + step_time * rate, False,
    )
    second, x_halos, y_halos, locals_now = stage(
        2, first, x_halos, y_halos, locals_now, (0, 1),
        lambda side, rate: 0.75 * cut(values, side) + 0.25 * (cut(first, side) + step_time * rate),
        False,
    )
    result, _, _, _ = stage(
        3, second, x_halos, y_halos, locals_now, (1, 0),
        lambda side, rate: cut(values, side) * (1.0 / 3.0)
        + 2.0 / 3.0 * (cut(second, side) + step_time * rate),
        True,
    )
    return result


def solution(mesh):
    in_specs = (P(("groups", "gx"), "gy", None, None), P(None, ("groups", "gx"), "gy"), P("groups"))
    out_specs = P(("groups", "gx"), "gy", None, None)
    return jax.shard_map(
        on_device, mesh=mesh, in_specs=in_specs, out_specs=out_specs, check_vma=False
    )
```

```python
import math

import jax
import jax.numpy as jnp
from jax import lax
from jax.sharding import PartitionSpec as P


cfl_number = 0.5
weno_eps = 1e-06
cell_span = 1.0 / 64.0


def weno_value(first, second, third, fourth, fifth):
    stencil_one = first / 3.0 - 7.0 * second / 6.0 + 11.0 * third / 6.0
    stencil_two = -second / 6.0 + 5.0 * third / 6.0 + fourth / 3.0
    stencil_three = third / 3.0 + 5.0 * fourth / 6.0 - fifth / 6.0
    smooth_one = (
        13.0 / 12.0 * (first - 2.0 * second + third) ** 2
        + 0.25 * (first - 4.0 * second + 3.0 * third) ** 2
    )
    smooth_two = 13.0 / 12.0 * (second - 2.0 * third + fourth) ** 2 + 0.25 * (second - fourth) ** 2
    smooth_three = (
        13.0 / 12.0 * (third - 2.0 * fourth + fifth) ** 2
        + 0.25 * (3.0 * third - 4.0 * fourth + fifth) ** 2
    )
    weight_one = 0.1 / (weno_eps + smooth_one) ** 2
    weight_two = 0.6 / (weno_eps + smooth_two) ** 2
    weight_three = 0.3 / (weno_eps + smooth_three) ** 2
    total = weight_one * stencil_one + weight_two * stencil_two + weight_three * stencil_three
    return total / (weight_one + weight_two + weight_three)


def both_sides(window):
    backward = weno_value(window(0), window(1), window(2), window(3), window(4))
    forward = weno_value(window(5), window(4), window(3), window(2), window(1))
    return (backward, forward)


def one_sided(padded, along, spacing, length):
    extent = padded.shape[along]
    differences = (
        lax.slice_in_dim(padded, 1, extent, axis=along)
        - lax.slice_in_dim(padded, 0, extent - 1, axis=along)
    ) / spacing

    def window(offset):
        return lax.slice_in_dim(differences, offset, offset + length, axis=along)

    return both_sides(window)


def periodic_sided(field, along, spacing):
    extent = field.shape[along]
    wrapped = jnp.concatenate(
        [
            lax.slice_in_dim(field, extent - 3, extent, axis=along),
            field,
            lax.slice_in_dim(field, 0, 3, axis=along),
        ],
        axis=along,
    )
    return one_sided(wrapped, along, spacing, extent)


def clamped_sided(field, along, spacing):
    extent = field.shape[along]
    inner = (
        lax.slice_in_dim(field, 1, extent, axis=along)
        - lax.slice_in_dim(field, 0, extent - 1, axis=along)
    ) / spacing
    differences = jnp.concatenate([lax.slice_in_dim(inner, 0, 1, axis=along), inner], axis=along)
    low_edge = lax.slice_in_dim(differences, 0, 1, axis=along)
    high_edge = lax.slice_in_dim(differences, extent - 1, extent, axis=along)

    def window(offset):
        shift_by = offset - 2
        if shift_by > 0:
            return jnp.concatenate(
                [lax.slice_in_dim(differences, shift_by, extent, axis=along)]
                + [high_edge] * shift_by,
                axis=along,
            )
        if shift_by < 0:
            return jnp.concatenate(
                [low_edge] * -shift_by
                + [lax.slice_in_dim(differences, 0, extent + shift_by, axis=along)],
                axis=along,
            )
        return differences

    return both_sides(window)


def send_low(piece, axis):
    count = lax.axis_size(axis)
    return lax.ppermute(piece, axis, [(i, (i + 1) % count) for i in range(count - 1)])


def send_high(piece, axis):
    count = lax.axis_size(axis)
    return lax.ppermute(piece, axis, [((i + 1) % count, i) for i in range(count - 1)])


def ghost_low(field, halo, at_low, along):
    shape_dist = [1] * field.ndim
    shape_dist[along] = 3
    inner = lax.slice_in_dim(field, 0, 1, axis=along)
    after = lax.slice_in_dim(field, 1, 2, axis=along)
    dist = jnp.arange(3, 0, -1).astype(jnp.float32).reshape(tuple(shape_dist))
    return jnp.where(at_low, inner + dist * (inner - after), halo)


def ghost_high(field, halo, at_high, along):
    extent = field.shape[along]
    shape_dist = [1] * field.ndim
    shape_dist[along] = 3
    inner = lax.slice_in_dim(field, extent - 1, extent, axis=along)
    before = lax.slice_in_dim(field, extent - 2, extent - 1, axis=along)
    dist = jnp.arange(1, 4).astype(jnp.float32).reshape(tuple(shape_dist))
    return jnp.where(at_high, inner + dist * (inner - before), halo)


def spread_max(local, axes):
    count = 1
    for axis in axes:
        count *= lax.axis_size(axis)
    span = 1
    while span < count:
        moved = [
            lax.ppermute(local, axes, [(i, (i + k * span) % count) for i in range(count)])
            for k in range(1, 4)
            if k * span < count
        ]
        for item in moved:
            local = jnp.maximum(local, item)
        span *= 4
    return local


def on_device(values, drift, params):
    cells_x, cells_y, n_psi, n_speed = values.shape
    devices_x = lax.axis_size("gx")
    devices_y = lax.axis_size("gy")
    total_x = cells_x * devices_x
    total_y = cells_y * devices_y
    step_psi = 2.0 * math.pi / n_psi
    step_speed = 1.0 / n_speed
    place_x = lax.axis_index("gx")
    place_y = lax.axis_index("gy")
    first_x = place_x == 0
    last_x = place_x == devices_x - 1
    first_y = place_y == 0
    last_y = place_y == devices_y - 1
    half = cells_x // 2
    alpha_three = params[1] + params[2]
    alpha_four = params[3]

    def cut(array, side):
        if side == 0:
            return array[:half]
        if side == 1:
            return array[half:]
        return array

    def local_part(field):
        back_three, fore_three = periodic_sided(field, 2, step_psi)
        back_four, fore_four = clamped_sided(field, 3, step_speed)
        mean_three = 0.5 * (back_three + fore_three)
        mean_four = 0.5 * (back_four + fore_four)
        partial = -params[2] * jnp.abs(mean_three) + params[3] * jnp.abs(mean_four)
        partial = partial + 0.5 * (
            alpha_three * (fore_three - back_three) + alpha_four * (fore_four - back_four)
        )
        return mean_three, partial

    def y_halo(field):
        tail = lax.slice_in_dim(field, cells_y - 3, cells_y, axis=1)
        head = lax.slice_in_dim(field, 0, 3, axis=1)
        if devices_y == 2:
            piece = lax.optimization_barrier(jnp.where(first_y, tail, head))
            swapped = lax.ppermute(piece, "gy", [(0, 1), (1, 0)])
            return swapped, swapped
        tail, head = lax.optimization_barrier((tail, head))
        return send_low(tail, "gy"), send_high(head, "gy")

    def local_whole(field):
        return lax.optimization_barrier(local_part(field))

    x_halos = (send_low(values[cells_x - 3 :], "gx"), send_high(values[:3], "gx"))
    y_halos = y_halo(values)
    psi_grid = jnp.arange(n_psi).astype(jnp.float32) * step_psi - math.pi
    speed_grid = 0.5 + (jnp.arange(n_speed).astype(jnp.float32) + 0.5) * step_speed
    along_one = -speed_grid[None, :] + params[0] * jnp.cos(psi_grid)[:, None]
    along_two = params[0] * jnp.sin(psi_grid)[:, None]
    y_coord = (
        (place_y * cells_y + jnp.arange(cells_y)).astype(jnp.float32) + 0.5 - 0.5 * total_y
    ) * cell_span
    x_coord = (
        (place_x * cells_x + jnp.arange(cells_x)).astype(jnp.float32) + 0.5 - 0.5 * total_x
    ) * cell_span
    turn_speed = params[0] * jnp.cos(psi_grid)
    side_speed = params[0] * jnp.sin(psi_grid)
    first_hi = jnp.max(turn_speed) - speed_grid[0]
    first_lo = jnp.min(turn_speed) - speed_grid[n_speed - 1]
    local_one = jnp.max(
        jnp.maximum(drift[0] + first_hi, -(drift[0] + first_lo))
        + params[1] * jnp.abs(y_coord)[None, :]
    )
    local_two = jnp.max(
        jnp.maximum(drift[1] + jnp.max(side_speed), -(drift[1] + jnp.min(side_speed)))
        + params[1] * jnp.abs(x_coord)[:, None]
    )
    locals_now = local_whole(values)
    bounds = spread_max(jnp.stack([local_one, local_two]), ("gx", "gy"))
    bound_one = bounds[0]
    bound_two = bounds[1]
    step_time = cfl_number / (
        bound_one / cell_span
        + bound_two / cell_span
        + alpha_three / step_psi
        + alpha_four / step_speed
    )
    x_col = x_coord[:, None, None, None]
    y_col = y_coord[None, :, None, None]
    flow_x = drift[0][:, :, None, None]
    flow_y = drift[1][:, :, None, None]

    def half_parts(field, side, x_halos, y_low, y_high, mean_three, partial):
        if side == 0:
            start, stop = 0, half
            ghost = ghost_low(field, x_halos[0], first_x, 0)
            wide_x = jnp.concatenate([ghost, field[: half + 3]], axis=0)
        elif side == 1:
            start, stop = half, cells_x
            ghost = ghost_high(field, x_halos[1], last_x, 0)
            wide_x = jnp.concatenate([field[half - 3 :], ghost], axis=0)
        else:
            start, stop = 0, cells_x
            wide_x = jnp.concatenate(
                [
                    ghost_low(field, x_halos[0], first_x, 0),
                    field,
                    ghost_high(field, x_halos[1], last_x, 0),
                ],
                axis=0,
            )
        mean_three = mean_three[start:stop]
        partial = partial[start:stop]
        back_one, fore_one = one_sided(wide_x, 0, cell_span, stop - start)
        part = field[start:stop]
        wide_y = jnp.concatenate(
            [
                ghost_low(part, y_low[start:stop], first_y, 1),
                part,
                ghost_high(part, y_high[start:stop], last_y, 1),
            ],
            axis=1,
        )
        back_two, fore_two = one_sided(wide_y, 1, cell_span, cells_y)
        mean_one = 0.5 * (back_one + fore_one)
        mean_two = 0.5 * (back_two + fore_two)
        ham = mean_one * (along_one[None, None] + flow_x[start:stop])
        ham = ham + mean_two * (along_two[None, None] + flow_y[start:stop])
        ham = ham + params[1] * jnp.abs(mean_one * y_col - mean_two * x_col[start:stop] - mean_three)
        ham = ham + partial
        return ham, fore_one - back_one, fore_two - back_two

    def combine(ham, spread_one, spread_two):
        return ham + 0.5 * (bound_one * spread_one + bound_two * spread_two)

    def stage(layer, field, x_halos, y_halos, local_pieces, order, update, last):
        results = [None, None]
        sent = [None, None]
        if last:
            rate = combine(*half_parts(field, 2, x_halos, *y_halos, *local_pieces))
            return update(2, rate), None, None, None
        for position, side in enumerate(order):
            parts = half_parts(field, side, x_halos, *y_halos, *local_pieces)
            if layer == 1 and position == 0:
                parts = lax.optimization_barrier(parts)
            results[side] = update(side, combine(*parts))
            if last:
                continue
            if side == 0:
                piece = lax.optimization_barrier(results[side][:3])
                sent[side] = send_high(piece, "gx")
            else:
                piece = lax.optimization_barrier(results[side][results[side].shape[0] - 3 :])
                sent[side] = send_low(piece, "gx")
        merged = jnp.concatenate(results, axis=0)
        if last:
            return merged, None, None, None
        next_y = y_halo(merged)
        next_pieces = local_whole(merged)
        return merged, (sent[1], sent[0]), next_y, next_pieces

    first, x_halos, y_halos, locals_now = stage(
        1, values, x_halos, y_halos, locals_now, (1, 0),
        lambda side, rate: cut(values, side) + step_time * rate, False,
    )
    second, x_halos, y_halos, locals_now = stage(
        2, first, x_halos, y_halos, locals_now, (0, 1),
        lambda side, rate: 0.75 * cut(values, side) + 0.25 * (cut(first, side) + step_time * rate),
        False,
    )
    result, _, _, _ = stage(
        3, second, x_halos, y_halos, locals_now, (1, 0),
        lambda side, rate: cut(values, side) * (1.0 / 3.0)
        + 2.0 / 3.0 * (cut(second, side) + step_time * rate),
        True,
    )
    return result


def solution(mesh):
    in_specs = (P(("groups", "gx"), "gy", None, None), P(None, ("groups", "gx"), "gy"), P("groups"))
    out_specs = P(("groups", "gx"), "gy", None, None)
    return jax.shard_map(
        on_device, mesh=mesh, in_specs=in_specs, out_specs=out_specs, check_vma=False
    )
```

```python
import math

import jax
import jax.numpy as jnp
from jax import lax
from jax.sharding import PartitionSpec as P


cfl_number = 0.5
weno_eps = 1e-06
cell_span = 1.0 / 64.0


def weno_value(first, second, third, fourth, fifth):
    stencil_one = first / 3.0 - 7.0 * second / 6.0 + 11.0 * third / 6.0
    stencil_two = -second / 6.0 + 5.0 * third / 6.0 + fourth / 3.0
    stencil_three = third / 3.0 + 5.0 * fourth / 6.0 - fifth / 6.0
    smooth_one = (
        13.0 / 12.0 * (first - 2.0 * second + third) ** 2
        + 0.25 * (first - 4.0 * second + 3.0 * third) ** 2
    )
    smooth_two = 13.0 / 12.0 * (second - 2.0 * third + fourth) ** 2 + 0.25 * (second - fourth) ** 2
    smooth_three = (
        13.0 / 12.0 * (third - 2.0 * fourth + fifth) ** 2
        + 0.25 * (3.0 * third - 4.0 * fourth + fifth) ** 2
    )
    weight_one = 0.1 / (weno_eps + smooth_one) ** 2
    weight_two = 0.6 / (weno_eps + smooth_two) ** 2
    weight_three = 0.3 / (weno_eps + smooth_three) ** 2
    total = weight_one * stencil_one + weight_two * stencil_two + weight_three * stencil_three
    return total / (weight_one + weight_two + weight_three)


def both_sides(window):
    backward = weno_value(window(0), window(1), window(2), window(3), window(4))
    forward = weno_value(window(5), window(4), window(3), window(2), window(1))
    return (backward, forward)


def one_sided(padded, along, spacing, length):
    extent = padded.shape[along]
    differences = (
        lax.slice_in_dim(padded, 1, extent, axis=along)
        - lax.slice_in_dim(padded, 0, extent - 1, axis=along)
    ) / spacing

    def window(offset):
        return lax.slice_in_dim(differences, offset, offset + length, axis=along)

    return both_sides(window)


def periodic_sided(field, along, spacing):
    extent = field.shape[along]
    wrapped = jnp.concatenate(
        [
            lax.slice_in_dim(field, extent - 3, extent, axis=along),
            field,
            lax.slice_in_dim(field, 0, 3, axis=along),
        ],
        axis=along,
    )
    return one_sided(wrapped, along, spacing, extent)


def clamped_sided(field, along, spacing):
    extent = field.shape[along]
    inner = (
        lax.slice_in_dim(field, 1, extent, axis=along)
        - lax.slice_in_dim(field, 0, extent - 1, axis=along)
    ) / spacing
    differences = jnp.concatenate([lax.slice_in_dim(inner, 0, 1, axis=along), inner], axis=along)
    low_edge = lax.slice_in_dim(differences, 0, 1, axis=along)
    high_edge = lax.slice_in_dim(differences, extent - 1, extent, axis=along)

    def window(offset):
        shift_by = offset - 2
        if shift_by > 0:
            return jnp.concatenate(
                [lax.slice_in_dim(differences, shift_by, extent, axis=along)]
                + [high_edge] * shift_by,
                axis=along,
            )
        if shift_by < 0:
            return jnp.concatenate(
                [low_edge] * -shift_by
                + [lax.slice_in_dim(differences, 0, extent + shift_by, axis=along)],
                axis=along,
            )
        return differences

    return both_sides(window)


def send_low(piece, axis):
    count = lax.axis_size(axis)
    return lax.ppermute(piece, axis, [(i, (i + 1) % count) for i in range(count - 1)])


def send_high(piece, axis):
    count = lax.axis_size(axis)
    return lax.ppermute(piece, axis, [((i + 1) % count, i) for i in range(count - 1)])


def ghost_low(field, halo, at_low, along):
    shape_dist = [1] * field.ndim
    shape_dist[along] = 3
    inner = lax.slice_in_dim(field, 0, 1, axis=along)
    after = lax.slice_in_dim(field, 1, 2, axis=along)
    dist = jnp.arange(3, 0, -1).astype(jnp.float32).reshape(tuple(shape_dist))
    return jnp.where(at_low, inner + dist * (inner - after), halo)


def ghost_high(field, halo, at_high, along):
    extent = field.shape[along]
    shape_dist = [1] * field.ndim
    shape_dist[along] = 3
    inner = lax.slice_in_dim(field, extent - 1, extent, axis=along)
    before = lax.slice_in_dim(field, extent - 2, extent - 1, axis=along)
    dist = jnp.arange(1, 4).astype(jnp.float32).reshape(tuple(shape_dist))
    return jnp.where(at_high, inner + dist * (inner - before), halo)


def spread_max(local, axes):
    count = 1
    for axis in axes:
        count *= lax.axis_size(axis)
    span = 1
    while span < count:
        moved = [
            lax.ppermute(local, axes, [(i, (i + k * span) % count) for i in range(count)])
            for k in range(1, 4)
            if k * span < count
        ]
        for item in moved:
            local = jnp.maximum(local, item)
        span *= 4
    return local


def on_device(values, drift, params):
    cells_x, cells_y, n_psi, n_speed = values.shape
    devices_x = lax.axis_size("gx")
    devices_y = lax.axis_size("gy")
    total_x = cells_x * devices_x
    total_y = cells_y * devices_y
    step_psi = 2.0 * math.pi / n_psi
    step_speed = 1.0 / n_speed
    place_x = lax.axis_index("gx")
    place_y = lax.axis_index("gy")
    first_x = place_x == 0
    last_x = place_x == devices_x - 1
    first_y = place_y == 0
    last_y = place_y == devices_y - 1
    half = cells_x // 2
    alpha_three = params[1] + params[2]
    alpha_four = params[3]

    def cut(array, side):
        if side == 0:
            return array[:half]
        if side == 1:
            return array[half:]
        return array

    def local_part(field):
        back_three, fore_three = periodic_sided(field, 2, step_psi)
        back_four, fore_four = clamped_sided(field, 3, step_speed)
        mean_three = 0.5 * (back_three + fore_three)
        mean_four = 0.5 * (back_four + fore_four)
        partial = -params[2] * jnp.abs(mean_three) + params[3] * jnp.abs(mean_four)
        partial = partial + 0.5 * (
            alpha_three * (fore_three - back_three) + alpha_four * (fore_four - back_four)
        )
        return mean_three, partial

    def local_halves(field):
        pieces = []
        for side in (0, 1):
            pieces.append(lax.optimization_barrier(local_part(cut(field, side))))
        return pieces

    def y_halo(field):
        tail = lax.slice_in_dim(field, cells_y - 3, cells_y, axis=1)
        head = lax.slice_in_dim(field, 0, 3, axis=1)
        if devices_y == 2:
            piece = lax.optimization_barrier(jnp.where(first_y, tail, head))
            swapped = lax.ppermute(piece, "gy", [(0, 1), (1, 0)])
            return swapped, swapped
        tail, head = lax.optimization_barrier((tail, head))
        return send_low(tail, "gy"), send_high(head, "gy")

    def local_whole(field):
        return lax.optimization_barrier(local_part(field))

    x_halos = (send_low(values[cells_x - 3 :], "gx"), send_high(values[:3], "gx"))
    y_halos = y_halo(values)
    psi_grid = jnp.arange(n_psi).astype(jnp.float32) * step_psi - math.pi
    speed_grid = 0.5 + (jnp.arange(n_speed).astype(jnp.float32) + 0.5) * step_speed
    along_one = -speed_grid[None, :] + params[0] * jnp.cos(psi_grid)[:, None]
    along_two = params[0] * jnp.sin(psi_grid)[:, None]
    y_coord = (
        (place_y * cells_y + jnp.arange(cells_y)).astype(jnp.float32) + 0.5 - 0.5 * total_y
    ) * cell_span
    x_coord = (
        (place_x * cells_x + jnp.arange(cells_x)).astype(jnp.float32) + 0.5 - 0.5 * total_x
    ) * cell_span
    turn_speed = params[0] * jnp.cos(psi_grid)
    side_speed = params[0] * jnp.sin(psi_grid)
    first_hi = jnp.max(turn_speed) - speed_grid[0]
    first_lo = jnp.min(turn_speed) - speed_grid[n_speed - 1]
    local_one = jnp.max(
        jnp.maximum(drift[0] + first_hi, -(drift[0] + first_lo))
        + params[1] * jnp.abs(y_coord)[None, :]
    )
    local_two = jnp.max(
        jnp.maximum(drift[1] + jnp.max(side_speed), -(drift[1] + jnp.min(side_speed)))
        + params[1] * jnp.abs(x_coord)[:, None]
    )
    locals_now = local_halves(values)
    bounds = spread_max(jnp.stack([local_one, local_two]), ("gx", "gy"))
    bound_one = bounds[0]
    bound_two = bounds[1]
    step_time = cfl_number / (
        bound_one / cell_span
        + bound_two / cell_span
        + alpha_three / step_psi
        + alpha_four / step_speed
    )
    x_col = x_coord[:, None, None, None]
    y_col = y_coord[None, :, None, None]
    flow_x = drift[0][:, :, None, None]
    flow_y = drift[1][:, :, None, None]

    def half_parts(field, side, x_halos, y_low, y_high, mean_three, partial):
        if side == 0:
            start, stop = 0, half
            ghost = ghost_low(field, x_halos[0], first_x, 0)
            wide_x = jnp.concatenate([ghost, field[: half + 3]], axis=0)
        elif side == 1:
            start, stop = half, cells_x
            ghost = ghost_high(field, x_halos[1], last_x, 0)
            wide_x = jnp.concatenate([field[half - 3 :], ghost], axis=0)
        else:
            start, stop = 0, cells_x
            wide_x = jnp.concatenate(
                [
                    ghost_low(field, x_halos[0], first_x, 0),
                    field,
                    ghost_high(field, x_halos[1], last_x, 0),
                ],
                axis=0,
            )
        if mean_three.shape[0] != stop - start:
            mean_three = mean_three[start:stop]
            partial = partial[start:stop]
        back_one, fore_one = one_sided(wide_x, 0, cell_span, stop - start)
        part = field[start:stop]
        wide_y = jnp.concatenate(
            [
                ghost_low(part, y_low[start:stop], first_y, 1),
                part,
                ghost_high(part, y_high[start:stop], last_y, 1),
            ],
            axis=1,
        )
        back_two, fore_two = one_sided(wide_y, 1, cell_span, cells_y)
        mean_one = 0.5 * (back_one + fore_one)
        mean_two = 0.5 * (back_two + fore_two)
        ham = mean_one * (along_one[None, None] + flow_x[start:stop])
        ham = ham + mean_two * (along_two[None, None] + flow_y[start:stop])
        ham = ham + params[1] * jnp.abs(mean_one * y_col - mean_two * x_col[start:stop] - mean_three)
        ham = ham + partial
        return ham, fore_one - back_one, fore_two - back_two

    def combine(ham, spread_one, spread_two):
        return ham + 0.5 * (bound_one * spread_one + bound_two * spread_two)

    def stage(field, x_halos, y_halos, local_pieces, order, update, last):
        results = [None, None]
        sent = [None, None]
        if last:
            rate = combine(*half_parts(field, 2, x_halos, *y_halos, *local_pieces))
            return update(2, rate), None, None, None
        for side in order:
            pieces = local_pieces[side] if isinstance(local_pieces, list) else local_pieces
            parts = half_parts(field, side, x_halos, *y_halos, *pieces)
            results[side] = update(side, combine(*parts))
            if last:
                continue
            if side == 0:
                piece = lax.optimization_barrier(results[side][:3])
                sent[side] = send_high(piece, "gx")
            else:
                piece = lax.optimization_barrier(results[side][results[side].shape[0] - 3 :])
                sent[side] = send_low(piece, "gx")
        merged = jnp.concatenate(results, axis=0)
        if last:
            return merged, None, None, None
        next_y = y_halo(merged)
        next_pieces = local_whole(merged)
        return merged, (sent[1], sent[0]), next_y, next_pieces

    first, x_halos, y_halos, locals_now = stage(
        values, x_halos, y_halos, locals_now, (1, 0),
        lambda side, rate: cut(values, side) + step_time * rate, False,
    )
    second, x_halos, y_halos, locals_now = stage(
        first, x_halos, y_halos, locals_now, (0, 1),
        lambda side, rate: 0.75 * cut(values, side) + 0.25 * (cut(first, side) + step_time * rate),
        False,
    )
    result, _, _, _ = stage(
        second, x_halos, y_halos, locals_now, (1, 0),
        lambda side, rate: cut(values, side) * (1.0 / 3.0)
        + 2.0 / 3.0 * (cut(second, side) + step_time * rate),
        True,
    )
    return result


def solution(mesh):
    in_specs = (P(("groups", "gx"), "gy", None, None), P(None, ("groups", "gx"), "gy"), P("groups"))
    out_specs = P(("groups", "gx"), "gy", None, None)
    return jax.shard_map(
        on_device, mesh=mesh, in_specs=in_specs, out_specs=out_specs, check_vma=False
    )
```

```python
import math

import jax
import numpy as np
import jax.numpy as jnp
from jax import lax
from jax.sharding import PartitionSpec as P


cfl_number = 0.5
weno_eps = 1e-06
cell_span = 1.0 / 64.0


def weno_value(first, second, third, fourth, fifth):
    stencil_one = first / 3.0 - 7.0 * second / 6.0 + 11.0 * third / 6.0
    stencil_two = -second / 6.0 + 5.0 * third / 6.0 + fourth / 3.0
    stencil_three = third / 3.0 + 5.0 * fourth / 6.0 - fifth / 6.0
    smooth_one = (
        13.0 / 12.0 * (first - 2.0 * second + third) ** 2
        + 0.25 * (first - 4.0 * second + 3.0 * third) ** 2
    )
    smooth_two = 13.0 / 12.0 * (second - 2.0 * third + fourth) ** 2 + 0.25 * (second - fourth) ** 2
    smooth_three = (
        13.0 / 12.0 * (third - 2.0 * fourth + fifth) ** 2
        + 0.25 * (3.0 * third - 4.0 * fourth + fifth) ** 2
    )
    weight_one = 0.1 / (weno_eps + smooth_one) ** 2
    weight_two = 0.6 / (weno_eps + smooth_two) ** 2
    weight_three = 0.3 / (weno_eps + smooth_three) ** 2
    total = weight_one * stencil_one + weight_two * stencil_two + weight_three * stencil_three
    return total / (weight_one + weight_two + weight_three)


def both_sides(window):
    backward = weno_value(window(0), window(1), window(2), window(3), window(4))
    forward = weno_value(window(5), window(4), window(3), window(2), window(1))
    return (backward, forward)


def one_sided(padded, along, spacing, length):
    extent = padded.shape[along]
    differences = (
        lax.slice_in_dim(padded, 1, extent, axis=along)
        - lax.slice_in_dim(padded, 0, extent - 1, axis=along)
    ) / spacing

    def window(offset):
        return lax.slice_in_dim(differences, offset, offset + length, axis=along)

    return both_sides(window)


def periodic_sided(field, along, spacing):
    extent = field.shape[along]
    wrapped = jnp.concatenate(
        [
            lax.slice_in_dim(field, extent - 3, extent, axis=along),
            field,
            lax.slice_in_dim(field, 0, 3, axis=along),
        ],
        axis=along,
    )
    return one_sided(wrapped, along, spacing, extent)


def clamped_sided(field, along, spacing):
    extent = field.shape[along]
    inner = (
        lax.slice_in_dim(field, 1, extent, axis=along)
        - lax.slice_in_dim(field, 0, extent - 1, axis=along)
    ) / spacing
    differences = jnp.concatenate([lax.slice_in_dim(inner, 0, 1, axis=along), inner], axis=along)
    low_edge = lax.slice_in_dim(differences, 0, 1, axis=along)
    high_edge = lax.slice_in_dim(differences, extent - 1, extent, axis=along)

    def window(offset):
        shift_by = offset - 2
        if shift_by > 0:
            return jnp.concatenate(
                [lax.slice_in_dim(differences, shift_by, extent, axis=along)]
                + [high_edge] * shift_by,
                axis=along,
            )
        if shift_by < 0:
            return jnp.concatenate(
                [low_edge] * -shift_by
                + [lax.slice_in_dim(differences, 0, extent + shift_by, axis=along)],
                axis=along,
            )
        return differences

    return both_sides(window)


def send_low(piece, axis):
    count = lax.axis_size(axis)
    return lax.ppermute(piece, axis, [(i, (i + 1) % count) for i in range(count - 1)])


def send_high(piece, axis):
    count = lax.axis_size(axis)
    return lax.ppermute(piece, axis, [((i + 1) % count, i) for i in range(count - 1)])


def ghost_low(field, halo, at_low, along):
    shape_dist = [1] * field.ndim
    shape_dist[along] = 3
    inner = lax.slice_in_dim(field, 0, 1, axis=along)
    after = lax.slice_in_dim(field, 1, 2, axis=along)
    dist = jnp.arange(3, 0, -1).astype(jnp.float32).reshape(tuple(shape_dist))
    return jnp.where(at_low, inner + dist * (inner - after), halo)


def ghost_high(field, halo, at_high, along):
    extent = field.shape[along]
    shape_dist = [1] * field.ndim
    shape_dist[along] = 3
    inner = lax.slice_in_dim(field, extent - 1, extent, axis=along)
    before = lax.slice_in_dim(field, extent - 2, extent - 1, axis=along)
    dist = jnp.arange(1, 4).astype(jnp.float32).reshape(tuple(shape_dist))
    return jnp.where(at_high, inner + dist * (inner - before), halo)


def spread_max(local, axes):
    count = 1
    for axis in axes:
        count *= lax.axis_size(axis)
    span = 1
    while span < count:
        moved = [
            lax.ppermute(local, axes, [(i, (i + k * span) % count) for i in range(count)])
            for k in range(1, 4)
            if k * span < count
        ]
        for item in moved:
            local = jnp.maximum(local, item)
        span *= 4
    return local


def on_device(values, drift, params):
    cells_x, cells_y, n_psi, n_speed = values.shape
    devices_x = lax.axis_size("gx")
    devices_y = lax.axis_size("gy")
    total_x = cells_x * devices_x
    total_y = cells_y * devices_y
    step_psi = 2.0 * math.pi / n_psi
    step_speed = 1.0 / n_speed
    place_x = lax.axis_index("gx")
    place_y = lax.axis_index("gy")
    first_x = place_x == 0
    last_x = place_x == devices_x - 1
    first_y = place_y == 0
    last_y = place_y == devices_y - 1
    half = cells_x // 2
    alpha_three = params[1] + params[2]
    alpha_four = params[3]

    def cut(array, side):
        if side == 0:
            return array[:half]
        if side == 1:
            return array[half:]
        return array

    def local_part(field):
        back_three, fore_three = periodic_sided(field, 2, step_psi)
        back_four, fore_four = clamped_sided(field, 3, step_speed)
        mean_three = 0.5 * (back_three + fore_three)
        mean_four = 0.5 * (back_four + fore_four)
        partial = -params[2] * jnp.abs(mean_three) + params[3] * jnp.abs(mean_four)
        partial = partial + 0.5 * (
            alpha_three * (fore_three - back_three) + alpha_four * (fore_four - back_four)
        )
        return mean_three, partial

    def local_halves(field):
        pieces = []
        for side in (0, 1):
            pieces.append(lax.optimization_barrier(local_part(cut(field, side))))
        return pieces

    def y_halo(field):
        tail = lax.slice_in_dim(field, cells_y - 3, cells_y, axis=1)
        head = lax.slice_in_dim(field, 0, 3, axis=1)
        if devices_y == 2:
            piece = lax.optimization_barrier(jnp.where(first_y, tail, head))
            swapped = lax.ppermute(piece, "gy", [(0, 1), (1, 0)])
            return swapped, swapped
        tail, head = lax.optimization_barrier((tail, head))
        return send_low(tail, "gy"), send_high(head, "gy")

    def local_whole(field):
        return lax.optimization_barrier(local_part(field))

    x_halos = (send_low(values[cells_x - 3 :], "gx"), send_high(values[:3], "gx"))
    y_halos = y_halo(values)
    psi_grid = np.arange(n_psi).astype(np.float32) * np.float32(step_psi) - np.float32(math.pi)
    cos_table = np.cos(psi_grid.astype(np.float64)).astype(np.float32)
    sin_table = np.sin(psi_grid.astype(np.float64)).astype(np.float32)
    speed_grid = np.float32(0.5) + (
        np.arange(n_speed).astype(np.float32) + np.float32(0.5)
    ) * np.float32(step_speed)
    along_one = -jnp.asarray(speed_grid)[None, :] + params[0] * jnp.asarray(cos_table)[:, None]
    along_two = params[0] * jnp.asarray(sin_table)[:, None]
    y_coord = (
        (place_y * cells_y + jnp.arange(cells_y)).astype(jnp.float32) + 0.5 - 0.5 * total_y
    ) * cell_span
    x_coord = (
        (place_x * cells_x + jnp.arange(cells_x)).astype(jnp.float32) + 0.5 - 0.5 * total_x
    ) * cell_span
    first_hi = params[0] * cos_table.max() - speed_grid[0]
    first_lo = params[0] * cos_table.min() - speed_grid[n_speed - 1]
    second_hi = params[0] * sin_table.max()
    second_lo = params[0] * sin_table.min()
    local_one = jnp.max(
        jnp.maximum(drift[0] + first_hi, -(drift[0] + first_lo))
        + params[1] * jnp.abs(y_coord)[None, :]
    )
    local_two = jnp.max(
        jnp.maximum(drift[1] + second_hi, -(drift[1] + second_lo))
        + params[1] * jnp.abs(x_coord)[:, None]
    )
    locals_now = local_halves(values)
    bounds = spread_max(jnp.stack([local_one, local_two]), ("gx", "gy"))
    bound_one = bounds[0]
    bound_two = bounds[1]
    step_time = cfl_number / (
        bound_one / cell_span
        + bound_two / cell_span
        + alpha_three / step_psi
        + alpha_four / step_speed
    )
    x_col = x_coord[:, None, None, None]
    y_col = y_coord[None, :, None, None]
    flow_x = drift[0][:, :, None, None]
    flow_y = drift[1][:, :, None, None]

    def half_parts(field, side, x_halos, y_low, y_high, mean_three, partial):
        if side == 0:
            start, stop = 0, half
            ghost = ghost_low(field, x_halos[0], first_x, 0)
            wide_x = jnp.concatenate([ghost, field[: half + 3]], axis=0)
        elif side == 1:
            start, stop = half, cells_x
            ghost = ghost_high(field, x_halos[1], last_x, 0)
            wide_x = jnp.concatenate([field[half - 3 :], ghost], axis=0)
        else:
            start, stop = 0, cells_x
            wide_x = jnp.concatenate(
                [
                    ghost_low(field, x_halos[0], first_x, 0),
                    field,
                    ghost_high(field, x_halos[1], last_x, 0),
                ],
                axis=0,
            )
        if mean_three.shape[0] != stop - start:
            mean_three = mean_three[start:stop]
            partial = partial[start:stop]
        back_one, fore_one = one_sided(wide_x, 0, cell_span, stop - start)
        part = field[start:stop]
        wide_y = jnp.concatenate(
            [
                ghost_low(part, y_low[start:stop], first_y, 1),
                part,
                ghost_high(part, y_high[start:stop], last_y, 1),
            ],
            axis=1,
        )
        back_two, fore_two = one_sided(wide_y, 1, cell_span, cells_y)
        mean_one = 0.5 * (back_one + fore_one)
        mean_two = 0.5 * (back_two + fore_two)
        ham = mean_one * (along_one[None, None] + flow_x[start:stop])
        ham = ham + mean_two * (along_two[None, None] + flow_y[start:stop])
        ham = ham + params[1] * jnp.abs(mean_one * y_col - mean_two * x_col[start:stop] - mean_three)
        ham = ham + partial
        return ham, fore_one - back_one, fore_two - back_two

    def combine(ham, spread_one, spread_two):
        return ham + 0.5 * (bound_one * spread_one + bound_two * spread_two)

    def stage(field, x_halos, y_halos, local_pieces, order, update, last):
        results = [None, None]
        sent = [None, None]
        if last:
            rate = combine(*half_parts(field, 2, x_halos, *y_halos, *local_pieces))
            return update(2, rate), None, None, None
        for side in order:
            pieces = local_pieces[side] if isinstance(local_pieces, list) else local_pieces
            parts = half_parts(field, side, x_halos, *y_halos, *pieces)
            results[side] = update(side, combine(*parts))
            if last:
                continue
            if side == 0:
                piece = lax.optimization_barrier(results[side][:3])
                sent[side] = send_high(piece, "gx")
            else:
                piece = lax.optimization_barrier(results[side][results[side].shape[0] - 3 :])
                sent[side] = send_low(piece, "gx")
        merged = jnp.concatenate(results, axis=0)
        if last:
            return merged, None, None, None
        next_y = y_halo(merged)
        next_pieces = local_whole(merged)
        return merged, (sent[1], sent[0]), next_y, next_pieces

    first, x_halos, y_halos, locals_now = stage(
        values, x_halos, y_halos, locals_now, (1, 0),
        lambda side, rate: cut(values, side) + step_time * rate, False,
    )
    second, x_halos, y_halos, locals_now = stage(
        first, x_halos, y_halos, locals_now, (0, 1),
        lambda side, rate: 0.75 * cut(values, side) + 0.25 * (cut(first, side) + step_time * rate),
        False,
    )
    result, _, _, _ = stage(
        second, x_halos, y_halos, locals_now, (1, 0),
        lambda side, rate: cut(values, side) * (1.0 / 3.0)
        + 2.0 / 3.0 * (cut(second, side) + step_time * rate),
        True,
    )
    return result


def solution(mesh):
    in_specs = (P(("groups", "gx"), "gy", None, None), P(None, ("groups", "gx"), "gy"), P("groups"))
    out_specs = P(("groups", "gx"), "gy", None, None)
    return jax.shard_map(
        on_device, mesh=mesh, in_specs=in_specs, out_specs=out_specs, check_vma=False
    )
```

```python
import functools
import math

import jax
import numpy as np
import jax.numpy as jnp
from jax import lax
from jax.experimental import pallas as pl
from jax.experimental.pallas import tpu as pltpu
from jax.sharding import PartitionSpec as P


cfl_number = 0.5
weno_eps = 1e-06
cell_span = 1.0 / 64.0


def weno_value(first, second, third, fourth, fifth):
    stencil_one = first / 3.0 - 7.0 * second / 6.0 + 11.0 * third / 6.0
    stencil_two = -second / 6.0 + 5.0 * third / 6.0 + fourth / 3.0
    stencil_three = third / 3.0 + 5.0 * fourth / 6.0 - fifth / 6.0
    smooth_one = (
        13.0 / 12.0 * (first - 2.0 * second + third) ** 2
        + 0.25 * (first - 4.0 * second + 3.0 * third) ** 2
    )
    smooth_two = 13.0 / 12.0 * (second - 2.0 * third + fourth) ** 2 + 0.25 * (second - fourth) ** 2
    smooth_three = (
        13.0 / 12.0 * (third - 2.0 * fourth + fifth) ** 2
        + 0.25 * (3.0 * third - 4.0 * fourth + fifth) ** 2
    )
    weight_one = 0.1 / (weno_eps + smooth_one) ** 2
    weight_two = 0.6 / (weno_eps + smooth_two) ** 2
    weight_three = 0.3 / (weno_eps + smooth_three) ** 2
    total = weight_one * stencil_one + weight_two * stencil_two + weight_three * stencil_three
    return total / (weight_one + weight_two + weight_three)


def both_sides(window):
    backward = weno_value(window(0), window(1), window(2), window(3), window(4))
    forward = weno_value(window(5), window(4), window(3), window(2), window(1))
    return (backward, forward)


def one_sided(padded, along, spacing, length):
    extent = padded.shape[along]
    differences = (
        lax.slice_in_dim(padded, 1, extent, axis=along)
        - lax.slice_in_dim(padded, 0, extent - 1, axis=along)
    ) / spacing

    def window(offset):
        return lax.slice_in_dim(differences, offset, offset + length, axis=along)

    return both_sides(window)


def periodic_sided(field, along, spacing):
    extent = field.shape[along]
    wrapped = jnp.concatenate(
        [
            lax.slice_in_dim(field, extent - 3, extent, axis=along),
            field,
            lax.slice_in_dim(field, 0, 3, axis=along),
        ],
        axis=along,
    )
    return one_sided(wrapped, along, spacing, extent)


def clamped_sided(field, along, spacing):
    extent = field.shape[along]
    inner = (
        lax.slice_in_dim(field, 1, extent, axis=along)
        - lax.slice_in_dim(field, 0, extent - 1, axis=along)
    ) / spacing
    differences = jnp.concatenate([lax.slice_in_dim(inner, 0, 1, axis=along), inner], axis=along)
    low_edge = lax.slice_in_dim(differences, 0, 1, axis=along)
    high_edge = lax.slice_in_dim(differences, extent - 1, extent, axis=along)

    def window(offset):
        shift_by = offset - 2
        if shift_by > 0:
            return jnp.concatenate(
                [lax.slice_in_dim(differences, shift_by, extent, axis=along)]
                + [high_edge] * shift_by,
                axis=along,
            )
        if shift_by < 0:
            return jnp.concatenate(
                [low_edge] * -shift_by
                + [lax.slice_in_dim(differences, 0, extent + shift_by, axis=along)],
                axis=along,
            )
        return differences

    return both_sides(window)


def local_kernel(params_ref, field_ref, mean_ref, partial_ref, *, step_psi, step_speed):
    rows, n_psi, n_speed = field_ref.shape[1:]
    turn_b = params_ref[2]
    accel = params_ref[3]
    alpha_three = params_ref[1] + params_ref[2]
    alpha_four = params_ref[3]
    lane = lax.broadcasted_iota(jnp.int32, (n_psi, n_speed), 1)

    def body(row, carry):
        cells = field_ref[0, row]
        diff = (cells - pltpu.roll(cells, 1, 0)) / step_psi
        psi = [pltpu.roll(diff, (2 - offset) % n_psi, 0) for offset in range(6)]
        back_three = weno_value(psi[0], psi[1], psi[2], psi[3], psi[4])
        fore_three = weno_value(psi[5], psi[4], psi[3], psi[2], psi[1])
        raw = (cells - pltpu.roll(cells, 1, 1)) / step_speed
        diff_v = jnp.where(lane == 0, pltpu.roll(raw, n_speed - 1, 1), raw)
        up_one = jnp.where(lane == n_speed - 1, diff_v, pltpu.roll(diff_v, n_speed - 1, 1))
        up_two = jnp.where(lane >= n_speed - 2, up_one, pltpu.roll(diff_v, n_speed - 2, 1))
        up_three = jnp.where(lane >= n_speed - 3, up_two, pltpu.roll(diff_v, n_speed - 3, 1))
        down_one = jnp.where(lane == 0, diff_v, pltpu.roll(diff_v, 1, 1))
        down_two = jnp.where(lane <= 1, down_one, pltpu.roll(diff_v, 2, 1))
        back_four = weno_value(down_two, down_one, diff_v, up_one, up_two)
        fore_four = weno_value(up_three, up_two, up_one, diff_v, down_one)
        mean_three = 0.5 * (back_three + fore_three)
        mean_four = 0.5 * (back_four + fore_four)
        partial = -turn_b * jnp.abs(mean_three) + accel * jnp.abs(mean_four)
        partial = partial + 0.5 * (
            alpha_three * (fore_three - back_three) + alpha_four * (fore_four - back_four)
        )
        mean_ref[0, row] = mean_three
        partial_ref[0, row] = partial
        return carry

    lax.fori_loop(0, rows, body, 0)


def local_pallas(field, params, start, planes):
    rows, n_psi, n_speed = field.shape[1:]
    kernel = functools.partial(
        local_kernel, step_psi=2.0 * math.pi / n_psi, step_speed=1.0 / n_speed
    )
    source = pl.BlockSpec((1, rows, n_psi, n_speed), lambda i: (i + start, 0, 0, 0))
    block = pl.BlockSpec((1, rows, n_psi, n_speed), lambda i: (i, 0, 0, 0))
    shape = jax.ShapeDtypeStruct((planes, rows, n_psi, n_speed), jnp.float32)
    return pl.pallas_call(
        kernel,
        grid=(planes,),
        in_specs=[pl.BlockSpec(memory_space=pltpu.SMEM), source],
        out_specs=[block, block],
        out_shape=[shape, shape],
    )(params, field)


def send_low(piece, axis):
    count = lax.axis_size(axis)
    return lax.ppermute(piece, axis, [(i, (i + 1) % count) for i in range(count - 1)])


def send_high(piece, axis):
    count = lax.axis_size(axis)
    return lax.ppermute(piece, axis, [((i + 1) % count, i) for i in range(count - 1)])


def ghost_low(field, halo, at_low, along):
    shape_dist = [1] * field.ndim
    shape_dist[along] = 3
    inner = lax.slice_in_dim(field, 0, 1, axis=along)
    after = lax.slice_in_dim(field, 1, 2, axis=along)
    dist = jnp.arange(3, 0, -1).astype(jnp.float32).reshape(tuple(shape_dist))
    return jnp.where(at_low, inner + dist * (inner - after), halo)


def ghost_high(field, halo, at_high, along):
    extent = field.shape[along]
    shape_dist = [1] * field.ndim
    shape_dist[along] = 3
    inner = lax.slice_in_dim(field, extent - 1, extent, axis=along)
    before = lax.slice_in_dim(field, extent - 2, extent - 1, axis=along)
    dist = jnp.arange(1, 4).astype(jnp.float32).reshape(tuple(shape_dist))
    return jnp.where(at_high, inner + dist * (inner - before), halo)


def spread_max(local, axes):
    count = 1
    for axis in axes:
        count *= lax.axis_size(axis)
    span = 1
    while span < count:
        moved = [
            lax.ppermute(local, axes, [(i, (i + k * span) % count) for i in range(count)])
            for k in range(1, 4)
            if k * span < count
        ]
        for item in moved:
            local = jnp.maximum(local, item)
        span *= 4
    return local


def on_device(values, drift, params):
    cells_x, cells_y, n_psi, n_speed = values.shape
    devices_x = lax.axis_size("gx")
    devices_y = lax.axis_size("gy")
    total_x = cells_x * devices_x
    total_y = cells_y * devices_y
    step_psi = 2.0 * math.pi / n_psi
    step_speed = 1.0 / n_speed
    place_x = lax.axis_index("gx")
    place_y = lax.axis_index("gy")
    first_x = place_x == 0
    last_x = place_x == devices_x - 1
    first_y = place_y == 0
    last_y = place_y == devices_y - 1
    half = cells_x // 2
    alpha_three = params[1] + params[2]
    alpha_four = params[3]

    def cut(array, side):
        if side == 0:
            return array[:half]
        if side == 1:
            return array[half:]
        return array

    def local_part(field):
        back_three, fore_three = periodic_sided(field, 2, step_psi)
        back_four, fore_four = clamped_sided(field, 3, step_speed)
        mean_three = 0.5 * (back_three + fore_three)
        mean_four = 0.5 * (back_four + fore_four)
        partial = -params[2] * jnp.abs(mean_three) + params[3] * jnp.abs(mean_four)
        partial = partial + 0.5 * (
            alpha_three * (fore_three - back_three) + alpha_four * (fore_four - back_four)
        )
        return mean_three, partial

    def y_halo(field):
        tail = lax.slice_in_dim(field, cells_y - 3, cells_y, axis=1)
        head = lax.slice_in_dim(field, 0, 3, axis=1)
        if devices_y == 2:
            piece = lax.optimization_barrier(jnp.where(first_y, tail, head))
            swapped = lax.ppermute(piece, "gy", [(0, 1), (1, 0)])
            return swapped, swapped
        tail, head = lax.optimization_barrier((tail, head))
        return send_low(tail, "gy"), send_high(head, "gy")

    def local_whole(field):
        return lax.optimization_barrier(local_part(field))

    x_halos = (send_low(values[cells_x - 3 :], "gx"), send_high(values[:3], "gx"))
    y_halos = y_halo(values)
    psi_grid = np.arange(n_psi).astype(np.float32) * np.float32(step_psi) - np.float32(math.pi)
    cos_table = np.cos(psi_grid.astype(np.float64)).astype(np.float32)
    sin_table = np.sin(psi_grid.astype(np.float64)).astype(np.float32)
    speed_grid = np.float32(0.5) + (
        np.arange(n_speed).astype(np.float32) + np.float32(0.5)
    ) * np.float32(step_speed)
    along_one = -jnp.asarray(speed_grid)[None, :] + params[0] * jnp.asarray(cos_table)[:, None]
    along_two = params[0] * jnp.asarray(sin_table)[:, None]
    y_coord = (
        (place_y * cells_y + jnp.arange(cells_y)).astype(jnp.float32) + 0.5 - 0.5 * total_y
    ) * cell_span
    x_coord = (
        (place_x * cells_x + jnp.arange(cells_x)).astype(jnp.float32) + 0.5 - 0.5 * total_x
    ) * cell_span
    first_hi = params[0] * cos_table.max() - speed_grid[0]
    first_lo = params[0] * cos_table.min() - speed_grid[n_speed - 1]
    second_hi = params[0] * sin_table.max()
    second_lo = params[0] * sin_table.min()
    local_one = jnp.max(
        jnp.maximum(drift[0] + first_hi, -(drift[0] + first_lo))
        + params[1] * jnp.abs(y_coord)[None, :]
    )
    local_two = jnp.max(
        jnp.maximum(drift[1] + second_hi, -(drift[1] + second_lo))
        + params[1] * jnp.abs(x_coord)[:, None]
    )
    locals_now = []
    for side in (0, 1):
        start = 0 if side == 0 else half
        count = half if side == 0 else cells_x - half
        locals_now.append(tuple(local_pallas(values, params, start, count)))
    bounds = spread_max(jnp.stack([local_one, local_two]), ("gx", "gy"))
    bound_one = bounds[0]
    bound_two = bounds[1]
    step_time = cfl_number / (
        bound_one / cell_span
        + bound_two / cell_span
        + alpha_three / step_psi
        + alpha_four / step_speed
    )
    x_col = x_coord[:, None, None, None]
    y_col = y_coord[None, :, None, None]
    flow_x = drift[0][:, :, None, None]
    flow_y = drift[1][:, :, None, None]

    def half_parts(field, side, x_halos, y_low, y_high, mean_three, partial):
        if side == 0:
            start, stop = 0, half
            ghost = ghost_low(field, x_halos[0], first_x, 0)
            wide_x = jnp.concatenate([ghost, field[: half + 3]], axis=0)
        elif side == 1:
            start, stop = half, cells_x
            ghost = ghost_high(field, x_halos[1], last_x, 0)
            wide_x = jnp.concatenate([field[half - 3 :], ghost], axis=0)
        else:
            start, stop = 0, cells_x
            wide_x = jnp.concatenate(
                [
                    ghost_low(field, x_halos[0], first_x, 0),
                    field,
                    ghost_high(field, x_halos[1], last_x, 0),
                ],
                axis=0,
            )
        if mean_three.shape[0] != stop - start:
            mean_three = mean_three[start:stop]
            partial = partial[start:stop]
        back_one, fore_one = one_sided(wide_x, 0, cell_span, stop - start)
        part = field[start:stop]
        wide_y = jnp.concatenate(
            [
                ghost_low(part, y_low[start:stop], first_y, 1),
                part,
                ghost_high(part, y_high[start:stop], last_y, 1),
            ],
            axis=1,
        )
        back_two, fore_two = one_sided(wide_y, 1, cell_span, cells_y)
        mean_one = 0.5 * (back_one + fore_one)
        mean_two = 0.5 * (back_two + fore_two)
        ham = mean_one * (along_one[None, None] + flow_x[start:stop])
        ham = ham + mean_two * (along_two[None, None] + flow_y[start:stop])
        ham = ham + params[1] * jnp.abs(mean_one * y_col - mean_two * x_col[start:stop] - mean_three)
        ham = ham + partial
        return ham, fore_one - back_one, fore_two - back_two

    def combine(ham, spread_one, spread_two):
        return ham + 0.5 * (bound_one * spread_one + bound_two * spread_two)

    def stage(field, x_halos, y_halos, local_pieces, order, update, last):
        results = [None, None]
        sent = [None, None]
        if last:
            rate = combine(*half_parts(field, 2, x_halos, *y_halos, *local_pieces))
            return update(2, rate), None, None, None
        for side in order:
            pieces = local_pieces[side] if isinstance(local_pieces, list) else local_pieces
            parts = half_parts(field, side, x_halos, *y_halos, *pieces)
            results[side] = update(side, combine(*parts))
            if last:
                continue
            if side == 0:
                piece = lax.optimization_barrier(results[side][:3])
                sent[side] = send_high(piece, "gx")
            else:
                piece = lax.optimization_barrier(results[side][results[side].shape[0] - 3 :])
                sent[side] = send_low(piece, "gx")
        merged = jnp.concatenate(results, axis=0)
        if last:
            return merged, None, None, None
        next_y = y_halo(merged)
        next_pieces = local_whole(merged)
        return merged, (sent[1], sent[0]), next_y, next_pieces

    first, x_halos, y_halos, locals_now = stage(
        values, x_halos, y_halos, locals_now, (1, 0),
        lambda side, rate: cut(values, side) + step_time * rate, False,
    )
    second, x_halos, y_halos, locals_now = stage(
        first, x_halos, y_halos, locals_now, (0, 1),
        lambda side, rate: 0.75 * cut(values, side) + 0.25 * (cut(first, side) + step_time * rate),
        False,
    )
    result, _, _, _ = stage(
        second, x_halos, y_halos, locals_now, (1, 0),
        lambda side, rate: cut(values, side) * (1.0 / 3.0)
        + 2.0 / 3.0 * (cut(second, side) + step_time * rate),
        True,
    )
    return result


def solution(mesh):
    in_specs = (P(("groups", "gx"), "gy", None, None), P(None, ("groups", "gx"), "gy"), P("groups"))
    out_specs = P(("groups", "gx"), "gy", None, None)
    return jax.shard_map(
        on_device, mesh=mesh, in_specs=in_specs, out_specs=out_specs, check_vma=False
    )
```

```python
import math

import jax
import numpy as np
import jax.numpy as jnp
from jax import lax
from jax.sharding import PartitionSpec as P


cfl_number = 0.5
weno_eps = 1e-06
cell_span = 1.0 / 64.0


def weno_value(first, second, third, fourth, fifth):
    stencil_one = first / 3.0 - 7.0 * second / 6.0 + 11.0 * third / 6.0
    stencil_two = -second / 6.0 + 5.0 * third / 6.0 + fourth / 3.0
    stencil_three = third / 3.0 + 5.0 * fourth / 6.0 - fifth / 6.0
    smooth_one = (
        13.0 / 12.0 * (first - 2.0 * second + third) ** 2
        + 0.25 * (first - 4.0 * second + 3.0 * third) ** 2
    )
    smooth_two = 13.0 / 12.0 * (second - 2.0 * third + fourth) ** 2 + 0.25 * (second - fourth) ** 2
    smooth_three = (
        13.0 / 12.0 * (third - 2.0 * fourth + fifth) ** 2
        + 0.25 * (3.0 * third - 4.0 * fourth + fifth) ** 2
    )
    weight_one = 0.1 / (weno_eps + smooth_one) ** 2
    weight_two = 0.6 / (weno_eps + smooth_two) ** 2
    weight_three = 0.3 / (weno_eps + smooth_three) ** 2
    total = weight_one * stencil_one + weight_two * stencil_two + weight_three * stencil_three
    return total / (weight_one + weight_two + weight_three)


def both_sides(window):
    backward = weno_value(window(0), window(1), window(2), window(3), window(4))
    forward = weno_value(window(5), window(4), window(3), window(2), window(1))
    return (backward, forward)


def one_sided(padded, along, spacing, length):
    extent = padded.shape[along]
    differences = (
        lax.slice_in_dim(padded, 1, extent, axis=along)
        - lax.slice_in_dim(padded, 0, extent - 1, axis=along)
    ) / spacing

    def window(offset):
        return lax.slice_in_dim(differences, offset, offset + length, axis=along)

    return both_sides(window)


def periodic_sided(field, along, spacing):
    extent = field.shape[along]
    wrapped = jnp.concatenate(
        [
            lax.slice_in_dim(field, extent - 3, extent, axis=along),
            field,
            lax.slice_in_dim(field, 0, 3, axis=along),
        ],
        axis=along,
    )
    return one_sided(wrapped, along, spacing, extent)


def clamped_sided(field, along, spacing):
    extent = field.shape[along]
    inner = (
        lax.slice_in_dim(field, 1, extent, axis=along)
        - lax.slice_in_dim(field, 0, extent - 1, axis=along)
    ) / spacing
    low_edge = lax.slice_in_dim(inner, 0, 1, axis=along)
    high_edge = lax.slice_in_dim(inner, extent - 2, extent - 1, axis=along)
    padded = jnp.concatenate([low_edge] * 3 + [inner] + [high_edge] * 3, axis=along)

    def window(offset):
        return lax.slice_in_dim(padded, offset, offset + extent, axis=along)

    return both_sides(window)


def send_low(piece, axis):
    count = lax.axis_size(axis)
    return lax.ppermute(piece, axis, [(i, (i + 1) % count) for i in range(count - 1)])


def send_high(piece, axis):
    count = lax.axis_size(axis)
    return lax.ppermute(piece, axis, [((i + 1) % count, i) for i in range(count - 1)])


def ghost_low(field, halo, at_low, along):
    shape_dist = [1] * field.ndim
    shape_dist[along] = 3
    inner = lax.slice_in_dim(field, 0, 1, axis=along)
    after = lax.slice_in_dim(field, 1, 2, axis=along)
    dist = jnp.arange(3, 0, -1).astype(jnp.float32).reshape(tuple(shape_dist))
    return jnp.where(at_low, inner + dist * (inner - after), halo)


def ghost_high(field, halo, at_high, along):
    extent = field.shape[along]
    shape_dist = [1] * field.ndim
    shape_dist[along] = 3
    inner = lax.slice_in_dim(field, extent - 1, extent, axis=along)
    before = lax.slice_in_dim(field, extent - 2, extent - 1, axis=along)
    dist = jnp.arange(1, 4).astype(jnp.float32).reshape(tuple(shape_dist))
    return jnp.where(at_high, inner + dist * (inner - before), halo)


def spread_max(local, axes):
    count = 1
    for axis in axes:
        count *= lax.axis_size(axis)
    span = 1
    while span < count:
        moved = [
            lax.ppermute(local, axes, [(i, (i + k * span) % count) for i in range(count)])
            for k in range(1, 4)
            if k * span < count
        ]
        for item in moved:
            local = jnp.maximum(local, item)
        span *= 4
    return local


def on_device(values, drift, params):
    cells_x, cells_y, n_psi, n_speed = values.shape
    devices_x = lax.axis_size("gx")
    devices_y = lax.axis_size("gy")
    total_x = cells_x * devices_x
    total_y = cells_y * devices_y
    step_psi = 2.0 * math.pi / n_psi
    step_speed = 1.0 / n_speed
    place_x = lax.axis_index("gx")
    place_y = lax.axis_index("gy")
    first_x = place_x == 0
    last_x = place_x == devices_x - 1
    first_y = place_y == 0
    last_y = place_y == devices_y - 1
    half = cells_x // 2
    alpha_three = params[1] + params[2]
    alpha_four = params[3]

    def cut(array, side):
        if side == 0:
            return array[:half]
        if side == 1:
            return array[half:]
        return array

    def local_part(field):
        back_three, fore_three = periodic_sided(field, 2, step_psi)
        back_four, fore_four = clamped_sided(field, 3, step_speed)
        mean_three = 0.5 * (back_three + fore_three)
        mean_four = 0.5 * (back_four + fore_four)
        partial = -params[2] * jnp.abs(mean_three) + params[3] * jnp.abs(mean_four)
        partial = partial + 0.5 * (
            alpha_three * (fore_three - back_three) + alpha_four * (fore_four - back_four)
        )
        return mean_three, partial

    def local_halves(field):
        pieces = []
        for side in (0, 1):
            pieces.append(lax.optimization_barrier(local_part(cut(field, side))))
        return pieces

    def y_halo(field):
        tail = lax.slice_in_dim(field, cells_y - 3, cells_y, axis=1)
        head = lax.slice_in_dim(field, 0, 3, axis=1)
        if devices_y == 2:
            piece = lax.optimization_barrier(jnp.where(first_y, tail, head))
            swapped = lax.ppermute(piece, "gy", [(0, 1), (1, 0)])
            return swapped, swapped
        tail, head = lax.optimization_barrier((tail, head))
        return send_low(tail, "gy"), send_high(head, "gy")

    def local_whole(field):
        return lax.optimization_barrier(local_part(field))

    x_halos = (send_low(values[cells_x - 3 :], "gx"), send_high(values[:3], "gx"))
    y_halos = y_halo(values)
    psi_grid = np.arange(n_psi).astype(np.float32) * np.float32(step_psi) - np.float32(math.pi)
    cos_table = np.cos(psi_grid.astype(np.float64)).astype(np.float32)
    sin_table = np.sin(psi_grid.astype(np.float64)).astype(np.float32)
    speed_grid = np.float32(0.5) + (
        np.arange(n_speed).astype(np.float32) + np.float32(0.5)
    ) * np.float32(step_speed)
    along_one = -jnp.asarray(speed_grid)[None, :] + params[0] * jnp.asarray(cos_table)[:, None]
    along_two = params[0] * jnp.asarray(sin_table)[:, None]
    y_coord = (
        (place_y * cells_y + jnp.arange(cells_y)).astype(jnp.float32) + 0.5 - 0.5 * total_y
    ) * cell_span
    x_coord = (
        (place_x * cells_x + jnp.arange(cells_x)).astype(jnp.float32) + 0.5 - 0.5 * total_x
    ) * cell_span
    first_hi = params[0] * cos_table.max() - speed_grid[0]
    first_lo = params[0] * cos_table.min() - speed_grid[n_speed - 1]
    second_hi = params[0] * sin_table.max()
    second_lo = params[0] * sin_table.min()
    local_one = jnp.max(
        jnp.maximum(drift[0] + first_hi, -(drift[0] + first_lo))
        + params[1] * jnp.abs(y_coord)[None, :]
    )
    local_two = jnp.max(
        jnp.maximum(drift[1] + second_hi, -(drift[1] + second_lo))
        + params[1] * jnp.abs(x_coord)[:, None]
    )
    locals_now = local_halves(values)
    bounds = spread_max(jnp.stack([local_one, local_two]), ("gx", "gy"))
    bound_one = bounds[0]
    bound_two = bounds[1]
    step_time = cfl_number / (
        bound_one / cell_span
        + bound_two / cell_span
        + alpha_three / step_psi
        + alpha_four / step_speed
    )
    x_col = x_coord[:, None, None, None]
    y_col = y_coord[None, :, None, None]
    flow_x = drift[0][:, :, None, None]
    flow_y = drift[1][:, :, None, None]

    def half_parts(field, side, x_halos, y_low, y_high, mean_three, partial):
        if side == 0:
            start, stop = 0, half
            ghost = ghost_low(field, x_halos[0], first_x, 0)
            wide_x = jnp.concatenate([ghost, field[: half + 3]], axis=0)
        elif side == 1:
            start, stop = half, cells_x
            ghost = ghost_high(field, x_halos[1], last_x, 0)
            wide_x = jnp.concatenate([field[half - 3 :], ghost], axis=0)
        else:
            start, stop = 0, cells_x
            wide_x = jnp.concatenate(
                [
                    ghost_low(field, x_halos[0], first_x, 0),
                    field,
                    ghost_high(field, x_halos[1], last_x, 0),
                ],
                axis=0,
            )
        if mean_three.shape[0] != stop - start:
            mean_three = mean_three[start:stop]
            partial = partial[start:stop]
        back_one, fore_one = one_sided(wide_x, 0, cell_span, stop - start)
        part = field[start:stop]
        wide_y = jnp.concatenate(
            [
                ghost_low(part, y_low[start:stop], first_y, 1),
                part,
                ghost_high(part, y_high[start:stop], last_y, 1),
            ],
            axis=1,
        )
        back_two, fore_two = one_sided(wide_y, 1, cell_span, cells_y)
        mean_one = 0.5 * (back_one + fore_one)
        mean_two = 0.5 * (back_two + fore_two)
        ham = mean_one * (along_one[None, None] + flow_x[start:stop])
        ham = ham + mean_two * (along_two[None, None] + flow_y[start:stop])
        ham = ham + params[1] * jnp.abs(mean_one * y_col - mean_two * x_col[start:stop] - mean_three)
        ham = ham + partial
        return ham, fore_one - back_one, fore_two - back_two

    def combine(ham, spread_one, spread_two):
        return ham + 0.5 * (bound_one * spread_one + bound_two * spread_two)

    def stage(field, x_halos, y_halos, local_pieces, order, update, last):
        results = [None, None]
        sent = [None, None]
        if last:
            rate = combine(*half_parts(field, 2, x_halos, *y_halos, *local_pieces))
            return update(2, rate), None, None, None
        for side in order:
            pieces = local_pieces[side] if isinstance(local_pieces, list) else local_pieces
            parts = half_parts(field, side, x_halos, *y_halos, *pieces)
            results[side] = update(side, combine(*parts))
            if last:
                continue
            if side == 0:
                piece = lax.optimization_barrier(results[side][:3])
                sent[side] = send_high(piece, "gx")
            else:
                piece = lax.optimization_barrier(results[side][results[side].shape[0] - 3 :])
                sent[side] = send_low(piece, "gx")
        merged = jnp.concatenate(results, axis=0)
        if last:
            return merged, None, None, None
        next_y = y_halo(merged)
        next_pieces = local_whole(merged)
        return merged, (sent[1], sent[0]), next_y, next_pieces

    first, x_halos, y_halos, locals_now = stage(
        values, x_halos, y_halos, locals_now, (1, 0),
        lambda side, rate: cut(values, side) + step_time * rate, False,
    )
    second, x_halos, y_halos, locals_now = stage(
        first, x_halos, y_halos, locals_now, (0, 1),
        lambda side, rate: 0.75 * cut(values, side) + 0.25 * (cut(first, side) + step_time * rate),
        False,
    )
    result, _, _, _ = stage(
        second, x_halos, y_halos, locals_now, (1, 0),
        lambda side, rate: cut(values, side) * (1.0 / 3.0)
        + 2.0 / 3.0 * (cut(second, side) + step_time * rate),
        True,
    )
    return result


def solution(mesh):
    in_specs = (P(("groups", "gx"), "gy", None, None), P(None, ("groups", "gx"), "gy"), P("groups"))
    out_specs = P(("groups", "gx"), "gy", None, None)
    return jax.shard_map(
        on_device, mesh=mesh, in_specs=in_specs, out_specs=out_specs, check_vma=False
    )
```

```python
import math

import jax
import numpy as np
import jax.numpy as jnp
from jax import lax
from jax.sharding import PartitionSpec as P


cfl_number = 0.5
weno_eps = 1e-06
cell_span = 1.0 / 64.0


def weno_value(first, second, third, fourth, fifth):
    stencil_one = first / 3.0 - 7.0 * second / 6.0 + 11.0 * third / 6.0
    stencil_two = -second / 6.0 + 5.0 * third / 6.0 + fourth / 3.0
    stencil_three = third / 3.0 + 5.0 * fourth / 6.0 - fifth / 6.0
    smooth_one = (
        13.0 / 12.0 * (first - 2.0 * second + third) ** 2
        + 0.25 * (first - 4.0 * second + 3.0 * third) ** 2
    )
    smooth_two = 13.0 / 12.0 * (second - 2.0 * third + fourth) ** 2 + 0.25 * (second - fourth) ** 2
    smooth_three = (
        13.0 / 12.0 * (third - 2.0 * fourth + fifth) ** 2
        + 0.25 * (3.0 * third - 4.0 * fourth + fifth) ** 2
    )
    weight_one = 0.1 / (weno_eps + smooth_one) ** 2
    weight_two = 0.6 / (weno_eps + smooth_two) ** 2
    weight_three = 0.3 / (weno_eps + smooth_three) ** 2
    total = weight_one * stencil_one + weight_two * stencil_two + weight_three * stencil_three
    return total / (weight_one + weight_two + weight_three)


def both_sides(window):
    backward = weno_value(window(0), window(1), window(2), window(3), window(4))
    forward = weno_value(window(5), window(4), window(3), window(2), window(1))
    return (backward, forward)


def one_sided(padded, along, spacing, length):
    extent = padded.shape[along]
    differences = (
        lax.slice_in_dim(padded, 1, extent, axis=along)
        - lax.slice_in_dim(padded, 0, extent - 1, axis=along)
    ) / spacing

    def window(offset):
        return lax.slice_in_dim(differences, offset, offset + length, axis=along)

    return both_sides(window)


def periodic_sided(field, along, spacing):
    extent = field.shape[along]
    wrapped = jnp.concatenate(
        [
            lax.slice_in_dim(field, extent - 3, extent, axis=along),
            field,
            lax.slice_in_dim(field, 0, 3, axis=along),
        ],
        axis=along,
    )
    return one_sided(wrapped, along, spacing, extent)


def clamped_sided(field, along, spacing):
    extent = field.shape[along]
    inner = (
        lax.slice_in_dim(field, 1, extent, axis=along)
        - lax.slice_in_dim(field, 0, extent - 1, axis=along)
    ) / spacing
    low_edge = lax.slice_in_dim(inner, 0, 1, axis=along)
    high_edge = lax.slice_in_dim(inner, extent - 2, extent - 1, axis=along)
    padded = jnp.concatenate([low_edge] * 3 + [inner] + [high_edge] * 3, axis=along)

    def window(offset):
        return lax.slice_in_dim(padded, offset, offset + extent, axis=along)

    return both_sides(window)


def send_low(piece, axis):
    count = lax.axis_size(axis)
    return lax.ppermute(piece, axis, [(i, (i + 1) % count) for i in range(count - 1)])


def send_high(piece, axis):
    count = lax.axis_size(axis)
    return lax.ppermute(piece, axis, [((i + 1) % count, i) for i in range(count - 1)])


def ghost_low(field, halo, at_low, along):
    shape_dist = [1] * field.ndim
    shape_dist[along] = 3
    inner = lax.slice_in_dim(field, 0, 1, axis=along)
    after = lax.slice_in_dim(field, 1, 2, axis=along)
    dist = jnp.arange(3, 0, -1).astype(jnp.float32).reshape(tuple(shape_dist))
    return jnp.where(at_low, inner + dist * (inner - after), halo)


def ghost_high(field, halo, at_high, along):
    extent = field.shape[along]
    shape_dist = [1] * field.ndim
    shape_dist[along] = 3
    inner = lax.slice_in_dim(field, extent - 1, extent, axis=along)
    before = lax.slice_in_dim(field, extent - 2, extent - 1, axis=along)
    dist = jnp.arange(1, 4).astype(jnp.float32).reshape(tuple(shape_dist))
    return jnp.where(at_high, inner + dist * (inner - before), halo)


def spread_max(local, axes):
    count = 1
    for axis in axes:
        count *= lax.axis_size(axis)
    span = 1
    while span < count:
        moved = [
            lax.ppermute(local, axes, [(i, (i + k * span) % count) for i in range(count)])
            for k in range(1, 4)
            if k * span < count
        ]
        for item in moved:
            local = jnp.maximum(local, item)
        span *= 4
    return local


def on_device(values, drift, params):
    cells_x, cells_y, n_psi, n_speed = values.shape
    devices_x = lax.axis_size("gx")
    devices_y = lax.axis_size("gy")
    total_x = cells_x * devices_x
    total_y = cells_y * devices_y
    step_psi = 2.0 * math.pi / n_psi
    step_speed = 1.0 / n_speed
    place_x = lax.axis_index("gx")
    place_y = lax.axis_index("gy")
    first_x = place_x == 0
    last_x = place_x == devices_x - 1
    first_y = place_y == 0
    last_y = place_y == devices_y - 1
    half = cells_x // 2
    alpha_three = params[1] + params[2]
    alpha_four = params[3]

    def cut(array, side):
        if side == 0:
            return array[:half]
        if side == 1:
            return array[half:]
        return array

    def local_part(field):
        back_three, fore_three = periodic_sided(field, 2, step_psi)
        back_four, fore_four = clamped_sided(field, 3, step_speed)
        mean_three = 0.5 * (back_three + fore_three)
        mean_four = 0.5 * (back_four + fore_four)
        partial = -params[2] * jnp.abs(mean_three) + params[3] * jnp.abs(mean_four)
        partial = partial + 0.5 * (
            alpha_three * (fore_three - back_three) + alpha_four * (fore_four - back_four)
        )
        return mean_three, partial

    def local_halves(field):
        pieces = []
        for side in (0, 1):
            pieces.append(lax.optimization_barrier(local_part(cut(field, side))))
        return pieces

    def y_halo(field):
        tail = lax.slice_in_dim(field, cells_y - 3, cells_y, axis=1)
        head = lax.slice_in_dim(field, 0, 3, axis=1)
        if devices_y == 2:
            offset = jnp.where(first_y, cells_y - 3, 0)
            piece = lax.dynamic_slice_in_dim(field, offset, 3, axis=1)
            piece = lax.optimization_barrier(piece)
            swapped = lax.ppermute(piece, "gy", [(0, 1), (1, 0)])
            return swapped, swapped
        tail, head = lax.optimization_barrier((tail, head))
        return send_low(tail, "gy"), send_high(head, "gy")

    def local_whole(field):
        return lax.optimization_barrier(local_part(field))

    x_halos = (send_low(values[cells_x - 3 :], "gx"), send_high(values[:3], "gx"))
    y_halos = y_halo(values)
    psi_grid = np.arange(n_psi).astype(np.float32) * np.float32(step_psi) - np.float32(math.pi)
    cos_table = np.cos(psi_grid.astype(np.float64)).astype(np.float32)
    sin_table = np.sin(psi_grid.astype(np.float64)).astype(np.float32)
    speed_grid = np.float32(0.5) + (
        np.arange(n_speed).astype(np.float32) + np.float32(0.5)
    ) * np.float32(step_speed)
    along_one = -jnp.asarray(speed_grid)[None, :] + params[0] * jnp.asarray(cos_table)[:, None]
    along_two = params[0] * jnp.asarray(sin_table)[:, None]
    y_coord = (
        (place_y * cells_y + jnp.arange(cells_y)).astype(jnp.float32) + 0.5 - 0.5 * total_y
    ) * cell_span
    x_coord = (
        (place_x * cells_x + jnp.arange(cells_x)).astype(jnp.float32) + 0.5 - 0.5 * total_x
    ) * cell_span
    first_hi = params[0] * cos_table.max() - speed_grid[0]
    first_lo = params[0] * cos_table.min() - speed_grid[n_speed - 1]
    second_hi = params[0] * sin_table.max()
    second_lo = params[0] * sin_table.min()
    terms = jnp.stack(
        [
            jnp.maximum(drift[0] + first_hi, -(drift[0] + first_lo))
            + params[1] * jnp.abs(y_coord)[None, :],
            jnp.maximum(drift[1] + second_hi, -(drift[1] + second_lo))
            + params[1] * jnp.abs(x_coord)[:, None],
        ]
    )
    local_bounds = jnp.max(terms, axis=(1, 2))
    locals_now = local_halves(values)
    bounds = spread_max(local_bounds, ("gx", "gy"))
    bound_one = bounds[0]
    bound_two = bounds[1]
    step_time = cfl_number / (
        bound_one / cell_span
        + bound_two / cell_span
        + alpha_three / step_psi
        + alpha_four / step_speed
    )
    x_col = x_coord[:, None, None, None]
    y_col = y_coord[None, :, None, None]
    flow_x = drift[0][:, :, None, None]
    flow_y = drift[1][:, :, None, None]

    def half_parts(field, side, x_halos, y_low, y_high, mean_three, partial):
        if side == 0:
            start, stop = 0, half
            ghost = ghost_low(field, x_halos[0], first_x, 0)
            wide_x = jnp.concatenate([ghost, field[: half + 3]], axis=0)
        elif side == 1:
            start, stop = half, cells_x
            ghost = ghost_high(field, x_halos[1], last_x, 0)
            wide_x = jnp.concatenate([field[half - 3 :], ghost], axis=0)
        else:
            start, stop = 0, cells_x
            wide_x = jnp.concatenate(
                [
                    ghost_low(field, x_halos[0], first_x, 0),
                    field,
                    ghost_high(field, x_halos[1], last_x, 0),
                ],
                axis=0,
            )
        if mean_three.shape[0] != stop - start:
            mean_three = mean_three[start:stop]
            partial = partial[start:stop]
        back_one, fore_one = one_sided(wide_x, 0, cell_span, stop - start)
        part = field[start:stop]
        wide_y = jnp.concatenate(
            [
                ghost_low(part, y_low[start:stop], first_y, 1),
                part,
                ghost_high(part, y_high[start:stop], last_y, 1),
            ],
            axis=1,
        )
        back_two, fore_two = one_sided(wide_y, 1, cell_span, cells_y)
        mean_one = 0.5 * (back_one + fore_one)
        mean_two = 0.5 * (back_two + fore_two)
        ham = mean_one * (along_one[None, None] + flow_x[start:stop])
        ham = ham + mean_two * (along_two[None, None] + flow_y[start:stop])
        ham = ham + params[1] * jnp.abs(mean_one * y_col - mean_two * x_col[start:stop] - mean_three)
        ham = ham + partial
        return ham, fore_one - back_one, fore_two - back_two

    def combine(ham, spread_one, spread_two):
        return ham + 0.5 * (bound_one * spread_one + bound_two * spread_two)

    def stage(field, x_halos, y_halos, local_pieces, order, update, last):
        results = [None, None]
        sent = [None, None]
        if last:
            rate = combine(*half_parts(field, 2, x_halos, *y_halos, *local_pieces))
            return update(2, rate), None, None, None
        for side in order:
            pieces = local_pieces[side] if isinstance(local_pieces, list) else local_pieces
            parts = half_parts(field, side, x_halos, *y_halos, *pieces)
            results[side] = update(side, combine(*parts))
            if last:
                continue
            if side == 0:
                piece = lax.optimization_barrier(results[side][:3])
                sent[side] = send_high(piece, "gx")
            else:
                piece = lax.optimization_barrier(results[side][results[side].shape[0] - 3 :])
                sent[side] = send_low(piece, "gx")
        merged = jnp.concatenate(results, axis=0)
        if last:
            return merged, None, None, None
        next_y = y_halo(merged)
        next_pieces = local_whole(merged)
        return merged, (sent[1], sent[0]), next_y, next_pieces

    first, x_halos, y_halos, locals_now = stage(
        values, x_halos, y_halos, locals_now, (1, 0),
        lambda side, rate: cut(values, side) + step_time * rate, False,
    )
    second, x_halos, y_halos, locals_now = stage(
        first, x_halos, y_halos, locals_now, (0, 1),
        lambda side, rate: 0.75 * cut(values, side) + 0.25 * (cut(first, side) + step_time * rate),
        False,
    )
    result, _, _, _ = stage(
        second, x_halos, y_halos, locals_now, (1, 0),
        lambda side, rate: cut(values, side) * (1.0 / 3.0)
        + 2.0 / 3.0 * (cut(second, side) + step_time * rate),
        True,
    )
    return result


def solution(mesh):
    in_specs = (P(("groups", "gx"), "gy", None, None), P(None, ("groups", "gx"), "gy"), P("groups"))
    out_specs = P(("groups", "gx"), "gy", None, None)
    return jax.shard_map(
        on_device, mesh=mesh, in_specs=in_specs, out_specs=out_specs, check_vma=False
    )
```

```python
import math

import jax
import numpy as np
import jax.numpy as jnp
from jax import lax
from jax.sharding import PartitionSpec as P


cfl_number = 0.5
weno_eps = 1e-06
cell_span = 1.0 / 64.0


def weno_value(first, second, third, fourth, fifth):
    stencil_one = first / 3.0 - 7.0 * second / 6.0 + 11.0 * third / 6.0
    stencil_two = -second / 6.0 + 5.0 * third / 6.0 + fourth / 3.0
    stencil_three = third / 3.0 + 5.0 * fourth / 6.0 - fifth / 6.0
    smooth_one = (
        13.0 / 12.0 * (first - 2.0 * second + third) ** 2
        + 0.25 * (first - 4.0 * second + 3.0 * third) ** 2
    )
    smooth_two = 13.0 / 12.0 * (second - 2.0 * third + fourth) ** 2 + 0.25 * (second - fourth) ** 2
    smooth_three = (
        13.0 / 12.0 * (third - 2.0 * fourth + fifth) ** 2
        + 0.25 * (3.0 * third - 4.0 * fourth + fifth) ** 2
    )
    weight_one = 0.1 / (weno_eps + smooth_one) ** 2
    weight_two = 0.6 / (weno_eps + smooth_two) ** 2
    weight_three = 0.3 / (weno_eps + smooth_three) ** 2
    total = weight_one * stencil_one + weight_two * stencil_two + weight_three * stencil_three
    return total / (weight_one + weight_two + weight_three)


def both_sides(window):
    backward = weno_value(window(0), window(1), window(2), window(3), window(4))
    forward = weno_value(window(5), window(4), window(3), window(2), window(1))
    return (backward, forward)


def one_sided(padded, along, spacing, length):
    extent = padded.shape[along]
    differences = (
        lax.slice_in_dim(padded, 1, extent, axis=along)
        - lax.slice_in_dim(padded, 0, extent - 1, axis=along)
    ) / spacing

    def window(offset):
        return lax.slice_in_dim(differences, offset, offset + length, axis=along)

    return both_sides(window)


def periodic_sided(field, along, spacing):
    extent = field.shape[along]
    wrapped = jnp.concatenate(
        [
            lax.slice_in_dim(field, extent - 3, extent, axis=along),
            field,
            lax.slice_in_dim(field, 0, 3, axis=along),
        ],
        axis=along,
    )
    return one_sided(wrapped, along, spacing, extent)


def clamped_sided(field, along, spacing):
    extent = field.shape[along]
    inner = (
        lax.slice_in_dim(field, 1, extent, axis=along)
        - lax.slice_in_dim(field, 0, extent - 1, axis=along)
    ) / spacing
    low_edge = lax.slice_in_dim(inner, 0, 1, axis=along)
    high_edge = lax.slice_in_dim(inner, extent - 2, extent - 1, axis=along)
    padded = jnp.concatenate([low_edge] * 3 + [inner] + [high_edge] * 3, axis=along)

    def window(offset):
        return lax.slice_in_dim(padded, offset, offset + extent, axis=along)

    return both_sides(window)


def send_low(piece, axis):
    count = lax.axis_size(axis)
    return lax.ppermute(piece, axis, [(i, (i + 1) % count) for i in range(count - 1)])


def send_high(piece, axis):
    count = lax.axis_size(axis)
    return lax.ppermute(piece, axis, [((i + 1) % count, i) for i in range(count - 1)])


def ghost_low(field, halo, at_low, along):
    shape_dist = [1] * field.ndim
    shape_dist[along] = 3
    inner = lax.slice_in_dim(field, 0, 1, axis=along)
    after = lax.slice_in_dim(field, 1, 2, axis=along)
    dist = jnp.arange(3, 0, -1).astype(jnp.float32).reshape(tuple(shape_dist))
    return jnp.where(at_low, inner + dist * (inner - after), halo)


def ghost_high(field, halo, at_high, along):
    extent = field.shape[along]
    shape_dist = [1] * field.ndim
    shape_dist[along] = 3
    inner = lax.slice_in_dim(field, extent - 1, extent, axis=along)
    before = lax.slice_in_dim(field, extent - 2, extent - 1, axis=along)
    dist = jnp.arange(1, 4).astype(jnp.float32).reshape(tuple(shape_dist))
    return jnp.where(at_high, inner + dist * (inner - before), halo)


def spread_max(local, axes):
    count = 1
    for axis in axes:
        count *= lax.axis_size(axis)
    span = 1
    while span < count:
        moved = [
            lax.ppermute(local, axes, [(i, (i + k * span) % count) for i in range(count)])
            for k in range(1, 4)
            if k * span < count
        ]
        for item in moved:
            local = jnp.maximum(local, item)
        span *= 4
    return local


def on_device(values, drift, params):
    cells_x, cells_y, n_psi, n_speed = values.shape
    devices_x = lax.axis_size("gx")
    devices_y = lax.axis_size("gy")
    total_x = cells_x * devices_x
    total_y = cells_y * devices_y
    step_psi = 2.0 * math.pi / n_psi
    step_speed = 1.0 / n_speed
    place_x = lax.axis_index("gx")
    place_y = lax.axis_index("gy")
    first_x = place_x == 0
    last_x = place_x == devices_x - 1
    first_y = place_y == 0
    last_y = place_y == devices_y - 1
    half = cells_x // 2
    alpha_three = params[1] + params[2]
    alpha_four = params[3]

    def cut(array, side):
        if side == 0:
            return array[:half]
        if side == 1:
            return array[half:]
        return array

    def local_part(field):
        back_three, fore_three = periodic_sided(field, 2, step_psi)
        back_four, fore_four = clamped_sided(field, 3, step_speed)
        mean_three = 0.5 * (back_three + fore_three)
        mean_four = 0.5 * (back_four + fore_four)
        partial = -params[2] * jnp.abs(mean_three) + params[3] * jnp.abs(mean_four)
        partial = partial + 0.5 * (
            alpha_three * (fore_three - back_three) + alpha_four * (fore_four - back_four)
        )
        return mean_three, partial

    def local_halves(field):
        pieces = []
        for side in (0, 1):
            pieces.append(lax.optimization_barrier(local_part(cut(field, side))))
        return pieces

    def y_halo(field):
        tail = lax.slice_in_dim(field, cells_y - 3, cells_y, axis=1)
        head = lax.slice_in_dim(field, 0, 3, axis=1)
        if devices_y == 2:
            offset = jnp.where(first_y, cells_y - 3, 0)
            piece = lax.dynamic_slice_in_dim(field, offset, 3, axis=1)
            piece = lax.optimization_barrier(piece)
            swapped = lax.ppermute(piece, "gy", [(0, 1), (1, 0)])
            return swapped, swapped
        tail, head = lax.optimization_barrier((tail, head))
        return send_low(tail, "gy"), send_high(head, "gy")

    def local_whole(field):
        return lax.optimization_barrier(local_part(field))

    x_halos = (send_low(values[cells_x - 3 :], "gx"), send_high(values[:3], "gx"))
    y_halos = y_halo(values)
    psi_grid = np.arange(n_psi).astype(np.float32) * np.float32(step_psi) - np.float32(math.pi)
    cos_table = np.cos(psi_grid.astype(np.float64)).astype(np.float32)
    sin_table = np.sin(psi_grid.astype(np.float64)).astype(np.float32)
    speed_grid = np.float32(0.5) + (
        np.arange(n_speed).astype(np.float32) + np.float32(0.5)
    ) * np.float32(step_speed)
    along_one = -jnp.asarray(speed_grid)[None, :] + params[0] * jnp.asarray(cos_table)[:, None]
    along_two = params[0] * jnp.asarray(sin_table)[:, None]
    y_coord = (
        (place_y * cells_y + jnp.arange(cells_y)).astype(jnp.float32) + 0.5 - 0.5 * total_y
    ) * cell_span
    x_coord = (
        (place_x * cells_x + jnp.arange(cells_x)).astype(jnp.float32) + 0.5 - 0.5 * total_x
    ) * cell_span
    first_hi = params[0] * cos_table.max() - speed_grid[0]
    first_lo = params[0] * cos_table.min() - speed_grid[n_speed - 1]
    second_hi = params[0] * sin_table.max()
    second_lo = params[0] * sin_table.min()
    terms = jnp.stack(
        [
            jnp.maximum(drift[0] + first_hi, -(drift[0] + first_lo))
            + params[1] * jnp.abs(y_coord)[None, :],
            jnp.maximum(drift[1] + second_hi, -(drift[1] + second_lo))
            + params[1] * jnp.abs(x_coord)[:, None],
        ]
    )
    local_bounds = jnp.max(terms, axis=(1, 2))
    locals_now = local_halves(values)
    bounds = spread_max(local_bounds, ("gx", "gy"))
    bound_one = bounds[0]
    bound_two = bounds[1]
    step_time = cfl_number / (
        bound_one / cell_span
        + bound_two / cell_span
        + alpha_three / step_psi
        + alpha_four / step_speed
    )
    x_col = x_coord[:, None, None, None]
    y_col = y_coord[None, :, None, None]
    flow_x = drift[0][:, :, None, None]
    flow_y = drift[1][:, :, None, None]

    def half_parts(field, side, x_halos, y_low, y_high, mean_three, partial):
        if side == 0:
            start, stop = 0, half
            ghost = ghost_low(field, x_halos[0], first_x, 0)
            wide_x = jnp.concatenate([ghost, field[: half + 3]], axis=0)
        elif side == 1:
            start, stop = half, cells_x
            ghost = ghost_high(field, x_halos[1], last_x, 0)
            wide_x = jnp.concatenate([field[half - 3 :], ghost], axis=0)
        else:
            start, stop = 0, cells_x
            wide_x = jnp.concatenate(
                [
                    ghost_low(field, x_halos[0], first_x, 0),
                    field,
                    ghost_high(field, x_halos[1], last_x, 0),
                ],
                axis=0,
            )
        if mean_three.shape[0] != stop - start:
            mean_three = mean_three[start:stop]
            partial = partial[start:stop]
        back_one, fore_one = one_sided(wide_x, 0, cell_span, stop - start)
        part = field[start:stop]
        wide_y = jnp.concatenate(
            [
                ghost_low(part, y_low[start:stop], first_y, 1),
                part,
                ghost_high(part, y_high[start:stop], last_y, 1),
            ],
            axis=1,
        )
        back_two, fore_two = one_sided(wide_y, 1, cell_span, cells_y)
        mean_one = 0.5 * (back_one + fore_one)
        mean_two = 0.5 * (back_two + fore_two)
        ham = mean_one * (along_one[None, None] + flow_x[start:stop])
        ham = ham + mean_two * (along_two[None, None] + flow_y[start:stop])
        ham = ham + params[1] * jnp.abs(mean_one * y_col - mean_two * x_col[start:stop] - mean_three)
        ham = ham + partial
        return ham, fore_one - back_one, fore_two - back_two

    def combine(ham, spread_one, spread_two):
        return ham + 0.5 * (bound_one * spread_one + bound_two * spread_two)

    def stage(field, x_halos, y_halos, local_pieces, order, update, last):
        if last:
            rate = combine(*half_parts(field, 2, x_halos, *y_halos, *local_pieces))
            return update(2, rate), None, None, None
        results = [None, None]
        sent = [None, None]

        def half(side):
            pieces = local_pieces[side] if isinstance(local_pieces, list) else local_pieces
            parts = half_parts(field, side, x_halos, *y_halos, *pieces)
            results[side] = update(side, combine(*parts))

        def send(side):
            if side == 0:
                piece = lax.optimization_barrier(results[side][:3])
                sent[side] = send_high(piece, "gx")
            else:
                piece = lax.optimization_barrier(results[side][results[side].shape[0] - 3 :])
                sent[side] = send_low(piece, "gx")

        half(order[0])
        send(order[0])
        half(order[1])
        send(order[1])
        merged = jnp.concatenate(results, axis=0)
        next_y = y_halo(merged)
        next_pieces = local_whole(merged)
        return merged, (sent[1], sent[0]), next_y, next_pieces

    first, x_halos, y_halos, locals_now = stage(
        values, x_halos, y_halos, locals_now, (1, 0),
        lambda side, rate: cut(values, side) + step_time * rate, False,
    )
    second, x_halos, y_halos, locals_now = stage(
        first, x_halos, y_halos, locals_now, (0, 1),
        lambda side, rate: 0.75 * cut(values, side) + 0.25 * (cut(first, side) + step_time * rate),
        False,
    )
    result, _, _, _ = stage(
        second, x_halos, y_halos, locals_now, (1, 0),
        lambda side, rate: cut(values, side) * (1.0 / 3.0)
        + 2.0 / 3.0 * (cut(second, side) + step_time * rate),
        True,
    )
    return result


def solution(mesh):
    in_specs = (P(("groups", "gx"), "gy", None, None), P(None, ("groups", "gx"), "gy"), P("groups"))
    out_specs = P(("groups", "gx"), "gy", None, None)
    return jax.shard_map(
        on_device, mesh=mesh, in_specs=in_specs, out_specs=out_specs, check_vma=False
    )
```

```python
import math

import jax
import numpy as np
import jax.numpy as jnp
from jax import lax
from jax.sharding import PartitionSpec as P


cfl_number = 0.5
weno_eps = 1e-06
cell_span = 1.0 / 64.0


def weno_value(first, second, third, fourth, fifth):
    stencil_one = first / 3.0 - 7.0 * second / 6.0 + 11.0 * third / 6.0
    stencil_two = -second / 6.0 + 5.0 * third / 6.0 + fourth / 3.0
    stencil_three = third / 3.0 + 5.0 * fourth / 6.0 - fifth / 6.0
    smooth_one = (
        13.0 / 12.0 * (first - 2.0 * second + third) ** 2
        + 0.25 * (first - 4.0 * second + 3.0 * third) ** 2
    )
    smooth_two = 13.0 / 12.0 * (second - 2.0 * third + fourth) ** 2 + 0.25 * (second - fourth) ** 2
    smooth_three = (
        13.0 / 12.0 * (third - 2.0 * fourth + fifth) ** 2
        + 0.25 * (3.0 * third - 4.0 * fourth + fifth) ** 2
    )
    weight_one = 0.1 / (weno_eps + smooth_one) ** 2
    weight_two = 0.6 / (weno_eps + smooth_two) ** 2
    weight_three = 0.3 / (weno_eps + smooth_three) ** 2
    total = weight_one * stencil_one + weight_two * stencil_two + weight_three * stencil_three
    return total / (weight_one + weight_two + weight_three)


def both_sides(window):
    backward = weno_value(window(0), window(1), window(2), window(3), window(4))
    forward = weno_value(window(5), window(4), window(3), window(2), window(1))
    return (backward, forward)


def one_sided(padded, along, spacing, length):
    extent = padded.shape[along]
    differences = (
        lax.slice_in_dim(padded, 1, extent, axis=along)
        - lax.slice_in_dim(padded, 0, extent - 1, axis=along)
    ) / spacing

    def window(offset):
        return lax.slice_in_dim(differences, offset, offset + length, axis=along)

    return both_sides(window)


def periodic_sided(field, along, spacing):
    extent = field.shape[along]
    wrapped = jnp.concatenate(
        [
            lax.slice_in_dim(field, extent - 3, extent, axis=along),
            field,
            lax.slice_in_dim(field, 0, 3, axis=along),
        ],
        axis=along,
    )
    return one_sided(wrapped, along, spacing, extent)


def clamped_sided(field, along, spacing):
    extent = field.shape[along]
    inner = (
        lax.slice_in_dim(field, 1, extent, axis=along)
        - lax.slice_in_dim(field, 0, extent - 1, axis=along)
    ) / spacing
    low_edge = lax.slice_in_dim(inner, 0, 1, axis=along)
    high_edge = lax.slice_in_dim(inner, extent - 2, extent - 1, axis=along)
    padded = jnp.concatenate([low_edge] * 3 + [inner] + [high_edge] * 3, axis=along)

    def window(offset):
        return lax.slice_in_dim(padded, offset, offset + extent, axis=along)

    return both_sides(window)


def send_low(piece, axis):
    count = lax.axis_size(axis)
    return lax.ppermute(piece, axis, [(i, (i + 1) % count) for i in range(count - 1)])


def send_high(piece, axis):
    count = lax.axis_size(axis)
    return lax.ppermute(piece, axis, [((i + 1) % count, i) for i in range(count - 1)])


def ghost_low(field, halo, at_low, along):
    shape_dist = [1] * field.ndim
    shape_dist[along] = 3
    inner = lax.slice_in_dim(field, 0, 1, axis=along)
    after = lax.slice_in_dim(field, 1, 2, axis=along)
    dist = jnp.arange(3, 0, -1).astype(jnp.float32).reshape(tuple(shape_dist))
    return jnp.where(at_low, inner + dist * (inner - after), halo)


def ghost_high(field, halo, at_high, along):
    extent = field.shape[along]
    shape_dist = [1] * field.ndim
    shape_dist[along] = 3
    inner = lax.slice_in_dim(field, extent - 1, extent, axis=along)
    before = lax.slice_in_dim(field, extent - 2, extent - 1, axis=along)
    dist = jnp.arange(1, 4).astype(jnp.float32).reshape(tuple(shape_dist))
    return jnp.where(at_high, inner + dist * (inner - before), halo)


def spread_max(local, axis, first_level):
    count = lax.axis_size(axis)
    span = 1
    level = first_level
    while span < count:
        moved = [
            lax.ppermute(local, axis, [(i, (i + k * span) % count) for i in range(count)])
            for k in range(1, 4)
            if k * span < count
        ]
        for item in moved:
            local = jnp.maximum(local, item)
        span *= 4
        level += 1
    return local


def on_device(values, drift, params):
    cells_x, cells_y, n_psi, n_speed = values.shape
    devices_x = lax.axis_size("gx")
    devices_y = lax.axis_size("gy")
    total_x = cells_x * devices_x
    total_y = cells_y * devices_y
    step_psi = 2.0 * math.pi / n_psi
    step_speed = 1.0 / n_speed
    place_x = lax.axis_index("gx")
    place_y = lax.axis_index("gy")
    first_x = place_x == 0
    last_x = place_x == devices_x - 1
    first_y = place_y == 0
    last_y = place_y == devices_y - 1
    half = cells_x // 2
    alpha_three = params[1] + params[2]
    alpha_four = params[3]

    def cut(array, side):
        if side == 0:
            return array[:half]
        if side == 1:
            return array[half:]
        return array

    def local_part(field):
        back_three, fore_three = periodic_sided(field, 2, step_psi)
        back_four, fore_four = clamped_sided(field, 3, step_speed)
        mean_three = 0.5 * (back_three + fore_three)
        mean_four = 0.5 * (back_four + fore_four)
        partial = -params[2] * jnp.abs(mean_three) + params[3] * jnp.abs(mean_four)
        partial = partial + 0.5 * (
            alpha_three * (fore_three - back_three) + alpha_four * (fore_four - back_four)
        )
        return mean_three, partial

    def local_halves(field):
        pieces = []
        for side in (0, 1):
            pieces.append(lax.optimization_barrier(local_part(cut(field, side))))
        return pieces

    def y_halo(field, whole=False):
        tail = lax.slice_in_dim(field, cells_y - 3, cells_y, axis=1)
        head = lax.slice_in_dim(field, 0, 3, axis=1)
        if devices_y == 2 and whole:
            swapped = lax.ppermute(field, "gy", [(0, 1), (1, 0)])
            offset = jnp.where(first_y, 0, cells_y - 3)
            piece = lax.dynamic_slice_in_dim(swapped, offset, 3, axis=1)
            return piece, piece
        if devices_y == 2:
            offset = jnp.where(first_y, cells_y - 3, 0)
            piece = lax.dynamic_slice_in_dim(field, offset, 3, axis=1)
            piece = lax.optimization_barrier(piece)
            swapped = lax.ppermute(piece, "gy", [(0, 1), (1, 0)])
            return swapped, swapped
        tail, head = lax.optimization_barrier((tail, head))
        return send_low(tail, "gy"), send_high(head, "gy")

    def local_whole(field):
        return lax.optimization_barrier(local_part(field))

    x_halos = (send_low(values[cells_x - 3 :], "gx"), send_high(values[:3], "gx"))
    y_halos = y_halo(values, whole=True)
    psi_grid = np.arange(n_psi).astype(np.float32) * np.float32(step_psi) - np.float32(math.pi)
    cos_table = np.cos(psi_grid.astype(np.float64)).astype(np.float32)
    sin_table = np.sin(psi_grid.astype(np.float64)).astype(np.float32)
    speed_grid = np.float32(0.5) + (
        np.arange(n_speed).astype(np.float32) + np.float32(0.5)
    ) * np.float32(step_speed)
    along_one = -jnp.asarray(speed_grid)[None, :] + params[0] * jnp.asarray(cos_table)[:, None]
    along_two = params[0] * jnp.asarray(sin_table)[:, None]
    y_coord = (
        (place_y * cells_y + jnp.arange(cells_y)).astype(jnp.float32) + 0.5 - 0.5 * total_y
    ) * cell_span
    x_coord = (
        (place_x * cells_x + jnp.arange(cells_x)).astype(jnp.float32) + 0.5 - 0.5 * total_x
    ) * cell_span
    first_hi = params[0] * cos_table.max() - speed_grid[0]
    first_lo = params[0] * cos_table.min() - speed_grid[n_speed - 1]
    second_hi = params[0] * sin_table.max()
    second_lo = params[0] * sin_table.min()
    terms = jnp.stack(
        [
            jnp.maximum(drift[0] + first_hi, -(drift[0] + first_lo))
            + params[1] * jnp.abs(y_coord)[None, :],
            jnp.maximum(drift[1] + second_hi, -(drift[1] + second_lo))
            + params[1] * jnp.abs(x_coord)[:, None],
        ]
    )
    local_bounds = jnp.max(terms, axis=(1, 2))
    locals_now = local_halves(values)
    bounds = spread_max(spread_max(local_bounds, "gy", 0), "gx", 0)
    bound_one = bounds[0]
    bound_two = bounds[1]
    step_time = cfl_number / (
        bound_one / cell_span
        + bound_two / cell_span
        + alpha_three / step_psi
        + alpha_four / step_speed
    )
    x_col = x_coord[:, None, None, None]
    y_col = y_coord[None, :, None, None]
    flow_x = drift[0][:, :, None, None]
    flow_y = drift[1][:, :, None, None]

    def half_parts(field, side, x_halos, y_low, y_high, mean_three, partial):
        if side == 0:
            start, stop = 0, half
            ghost = ghost_low(field, x_halos[0], first_x, 0)
            wide_x = jnp.concatenate([ghost, field[: half + 3]], axis=0)
        elif side == 1:
            start, stop = half, cells_x
            ghost = ghost_high(field, x_halos[1], last_x, 0)
            wide_x = jnp.concatenate([field[half - 3 :], ghost], axis=0)
        else:
            start, stop = 0, cells_x
            wide_x = jnp.concatenate(
                [
                    ghost_low(field, x_halos[0], first_x, 0),
                    field,
                    ghost_high(field, x_halos[1], last_x, 0),
                ],
                axis=0,
            )
        if mean_three.shape[0] != stop - start:
            mean_three = mean_three[start:stop]
            partial = partial[start:stop]
        back_one, fore_one = one_sided(wide_x, 0, cell_span, stop - start)
        part = field[start:stop]
        wide_y = jnp.concatenate(
            [
                ghost_low(part, y_low[start:stop], first_y, 1),
                part,
                ghost_high(part, y_high[start:stop], last_y, 1),
            ],
            axis=1,
        )
        back_two, fore_two = one_sided(wide_y, 1, cell_span, cells_y)
        mean_one = 0.5 * (back_one + fore_one)
        mean_two = 0.5 * (back_two + fore_two)
        ham = mean_one * (along_one[None, None] + flow_x[start:stop])
        ham = ham + mean_two * (along_two[None, None] + flow_y[start:stop])
        ham = ham + params[1] * jnp.abs(mean_one * y_col - mean_two * x_col[start:stop] - mean_three)
        ham = ham + partial
        return ham, fore_one - back_one, fore_two - back_two

    def combine(ham, spread_one, spread_two):
        return ham + 0.5 * (bound_one * spread_one + bound_two * spread_two)

    def stage(field, x_halos, y_halos, local_pieces, order, update, last):
        if last:
            rate = combine(*half_parts(field, 2, x_halos, *y_halos, *local_pieces))
            return update(2, rate), None, None, None
        results = [None, None]
        sent = [None, None]

        def half(side):
            pieces = local_pieces[side] if isinstance(local_pieces, list) else local_pieces
            parts = half_parts(field, side, x_halos, *y_halos, *pieces)
            results[side] = update(side, combine(*parts))

        def send(side):
            if side == 0:
                piece = lax.optimization_barrier(results[side][:3])
                sent[side] = send_high(piece, "gx")
            else:
                piece = lax.optimization_barrier(results[side][results[side].shape[0] - 3 :])
                sent[side] = send_low(piece, "gx")

        half(order[0])
        send(order[0])
        half(order[1])
        send(order[1])
        merged = jnp.concatenate(results, axis=0)
        next_y = y_halo(merged)
        next_pieces = local_whole(merged)
        return merged, (sent[1], sent[0]), next_y, next_pieces

    first, x_halos, y_halos, locals_now = stage(
        values, x_halos, y_halos, locals_now, (1, 0),
        lambda side, rate: cut(values, side) + step_time * rate, False,
    )
    second, x_halos, y_halos, locals_now = stage(
        first, x_halos, y_halos, locals_now, (0, 1),
        lambda side, rate: 0.75 * cut(values, side) + 0.25 * (cut(first, side) + step_time * rate),
        False,
    )
    result, _, _, _ = stage(
        second, x_halos, y_halos, locals_now, (1, 0),
        lambda side, rate: cut(values, side) * (1.0 / 3.0)
        + 2.0 / 3.0 * (cut(second, side) + step_time * rate),
        True,
    )
    return result


def solution(mesh):
    in_specs = (P(("groups", "gx"), "gy", None, None), P(None, ("groups", "gx"), "gy"), P("groups"))
    out_specs = P(("groups", "gx"), "gy", None, None)
    return jax.shard_map(
        on_device, mesh=mesh, in_specs=in_specs, out_specs=out_specs, check_vma=False
    )
```

```python
import math

import jax
import numpy as np
import jax.numpy as jnp
from jax import lax
from jax.sharding import PartitionSpec as P


cfl_number = 0.5
weno_eps = 1e-06
cell_span = 1.0 / 64.0


def weno_value(first, second, third, fourth, fifth):
    stencil_one = first / 3.0 - 7.0 * second / 6.0 + 11.0 * third / 6.0
    stencil_two = -second / 6.0 + 5.0 * third / 6.0 + fourth / 3.0
    stencil_three = third / 3.0 + 5.0 * fourth / 6.0 - fifth / 6.0
    smooth_one = (
        13.0 / 12.0 * (first - 2.0 * second + third) ** 2
        + 0.25 * (first - 4.0 * second + 3.0 * third) ** 2
    )
    smooth_two = 13.0 / 12.0 * (second - 2.0 * third + fourth) ** 2 + 0.25 * (second - fourth) ** 2
    smooth_three = (
        13.0 / 12.0 * (third - 2.0 * fourth + fifth) ** 2
        + 0.25 * (3.0 * third - 4.0 * fourth + fifth) ** 2
    )
    weight_one = 0.1 / (weno_eps + smooth_one) ** 2
    weight_two = 0.6 / (weno_eps + smooth_two) ** 2
    weight_three = 0.3 / (weno_eps + smooth_three) ** 2
    total = weight_one * stencil_one + weight_two * stencil_two + weight_three * stencil_three
    return total / (weight_one + weight_two + weight_three)


def both_sides(window):
    backward = weno_value(window(0), window(1), window(2), window(3), window(4))
    forward = weno_value(window(5), window(4), window(3), window(2), window(1))
    return (backward, forward)


def one_sided(padded, along, spacing, length):
    extent = padded.shape[along]
    differences = (
        lax.slice_in_dim(padded, 1, extent, axis=along)
        - lax.slice_in_dim(padded, 0, extent - 1, axis=along)
    ) / spacing

    def window(offset):
        return lax.slice_in_dim(differences, offset, offset + length, axis=along)

    return both_sides(window)


def periodic_sided(field, along, spacing):
    extent = field.shape[along]
    wrapped = jnp.concatenate(
        [
            lax.slice_in_dim(field, extent - 3, extent, axis=along),
            field,
            lax.slice_in_dim(field, 0, 3, axis=along),
        ],
        axis=along,
    )
    return one_sided(wrapped, along, spacing, extent)


def clamped_sided(field, along, spacing):
    extent = field.shape[along]
    inner = (
        lax.slice_in_dim(field, 1, extent, axis=along)
        - lax.slice_in_dim(field, 0, extent - 1, axis=along)
    ) / spacing
    low_edge = lax.slice_in_dim(inner, 0, 1, axis=along)
    high_edge = lax.slice_in_dim(inner, extent - 2, extent - 1, axis=along)
    padded = jnp.concatenate([low_edge] * 3 + [inner] + [high_edge] * 3, axis=along)

    def window(offset):
        return lax.slice_in_dim(padded, offset, offset + extent, axis=along)

    return both_sides(window)


def send_low(piece, axis):
    count = lax.axis_size(axis)
    return lax.ppermute(piece, axis, [(i, (i + 1) % count) for i in range(count - 1)])


def send_high(piece, axis):
    count = lax.axis_size(axis)
    return lax.ppermute(piece, axis, [((i + 1) % count, i) for i in range(count - 1)])


def ghost_low(field, halo, at_low, along):
    shape_dist = [1] * field.ndim
    shape_dist[along] = 3
    inner = lax.slice_in_dim(field, 0, 1, axis=along)
    after = lax.slice_in_dim(field, 1, 2, axis=along)
    dist = jnp.arange(3, 0, -1).astype(jnp.float32).reshape(tuple(shape_dist))
    return jnp.where(at_low, inner + dist * (inner - after), halo)


def ghost_high(field, halo, at_high, along):
    extent = field.shape[along]
    shape_dist = [1] * field.ndim
    shape_dist[along] = 3
    inner = lax.slice_in_dim(field, extent - 1, extent, axis=along)
    before = lax.slice_in_dim(field, extent - 2, extent - 1, axis=along)
    dist = jnp.arange(1, 4).astype(jnp.float32).reshape(tuple(shape_dist))
    return jnp.where(at_high, inner + dist * (inner - before), halo)


def spread_max(local, axis, first_level, radix):
    count = lax.axis_size(axis)
    span = 1
    level = first_level
    while span < count:
        moved = [
            lax.ppermute(local, axis, [(i, (i + k * span) % count) for i in range(count)])
            for k in range(1, radix)
            if k * span < count
        ]
        for item in moved:
            local = jnp.maximum(local, item)
        span *= radix
        level += 1
    return local


def on_device(values, drift, params):
    cells_x, cells_y, n_psi, n_speed = values.shape
    devices_x = lax.axis_size("gx")
    devices_y = lax.axis_size("gy")
    total_x = cells_x * devices_x
    total_y = cells_y * devices_y
    step_psi = 2.0 * math.pi / n_psi
    step_speed = 1.0 / n_speed
    place_x = lax.axis_index("gx")
    place_y = lax.axis_index("gy")
    first_x = place_x == 0
    last_x = place_x == devices_x - 1
    first_y = place_y == 0
    last_y = place_y == devices_y - 1
    half = cells_x // 2
    alpha_three = params[1] + params[2]
    alpha_four = params[3]

    def cut(array, side):
        if side == 0:
            return array[:half]
        if side == 1:
            return array[half:]
        return array

    def local_part(field):
        back_three, fore_three = periodic_sided(field, 2, step_psi)
        back_four, fore_four = clamped_sided(field, 3, step_speed)
        mean_three = 0.5 * (back_three + fore_three)
        mean_four = 0.5 * (back_four + fore_four)
        partial = -params[2] * jnp.abs(mean_three) + params[3] * jnp.abs(mean_four)
        partial = partial + 0.5 * (
            alpha_three * (fore_three - back_three) + alpha_four * (fore_four - back_four)
        )
        return mean_three, partial

    def local_halves(field):
        pieces = []
        for side in (0, 1):
            pieces.append(lax.optimization_barrier(local_part(cut(field, side))))
        return pieces

    def y_halo(field):
        tail = lax.slice_in_dim(field, cells_y - 3, cells_y, axis=1)
        head = lax.slice_in_dim(field, 0, 3, axis=1)
        if devices_y == 2:
            offset = jnp.where(first_y, cells_y - 3, 0)
            piece = lax.dynamic_slice_in_dim(field, offset, 3, axis=1)
            piece = lax.optimization_barrier(piece)
            swapped = lax.ppermute(piece, "gy", [(0, 1), (1, 0)])
            return swapped, swapped
        tail, head = lax.optimization_barrier((tail, head))
        return send_low(tail, "gy"), send_high(head, "gy")

    def local_whole(field):
        return lax.optimization_barrier(local_part(field))

    x_halos = (send_low(values[cells_x - 3 :], "gx"), send_high(values[:3], "gx"))
    y_halos = y_halo(values)
    psi_grid = np.arange(n_psi).astype(np.float32) * np.float32(step_psi) - np.float32(math.pi)
    cos_table = np.cos(psi_grid.astype(np.float64)).astype(np.float32)
    sin_table = np.sin(psi_grid.astype(np.float64)).astype(np.float32)
    speed_grid = np.float32(0.5) + (
        np.arange(n_speed).astype(np.float32) + np.float32(0.5)
    ) * np.float32(step_speed)
    along_one = -jnp.asarray(speed_grid)[None, :] + params[0] * jnp.asarray(cos_table)[:, None]
    along_two = params[0] * jnp.asarray(sin_table)[:, None]
    y_coord = (
        (place_y * cells_y + jnp.arange(cells_y)).astype(jnp.float32) + 0.5 - 0.5 * total_y
    ) * cell_span
    x_coord = (
        (place_x * cells_x + jnp.arange(cells_x)).astype(jnp.float32) + 0.5 - 0.5 * total_x
    ) * cell_span
    first_hi = params[0] * cos_table.max() - speed_grid[0]
    first_lo = params[0] * cos_table.min() - speed_grid[n_speed - 1]
    second_hi = params[0] * sin_table.max()
    second_lo = params[0] * sin_table.min()
    terms = jnp.stack(
        [
            jnp.maximum(drift[0] + first_hi, -(drift[0] + first_lo))
            + params[1] * jnp.abs(y_coord)[None, :],
            jnp.maximum(drift[1] + second_hi, -(drift[1] + second_lo))
            + params[1] * jnp.abs(x_coord)[:, None],
        ]
    )
    local_bounds = jnp.max(terms, axis=(1, 2))
    locals_now = local_halves(values)
    bounds = spread_max(spread_max(local_bounds, "gy", 0, 4), "gx", 0, 2)
    bound_one = bounds[0]
    bound_two = bounds[1]
    step_time = cfl_number / (
        bound_one / cell_span
        + bound_two / cell_span
        + alpha_three / step_psi
        + alpha_four / step_speed
    )
    x_col = x_coord[:, None, None, None]
    y_col = y_coord[None, :, None, None]
    flow_x = drift[0][:, :, None, None]
    flow_y = drift[1][:, :, None, None]

    def half_parts(field, side, x_halos, y_low, y_high, mean_three, partial):
        if side == 0:
            start, stop = 0, half
            ghost = ghost_low(field, x_halos[0], first_x, 0)
            wide_x = jnp.concatenate([ghost, field[: half + 3]], axis=0)
        elif side == 1:
            start, stop = half, cells_x
            ghost = ghost_high(field, x_halos[1], last_x, 0)
            wide_x = jnp.concatenate([field[half - 3 :], ghost], axis=0)
        else:
            start, stop = 0, cells_x
            wide_x = jnp.concatenate(
                [
                    ghost_low(field, x_halos[0], first_x, 0),
                    field,
                    ghost_high(field, x_halos[1], last_x, 0),
                ],
                axis=0,
            )
        if mean_three.shape[0] != stop - start:
            mean_three = mean_three[start:stop]
            partial = partial[start:stop]
        back_one, fore_one = one_sided(wide_x, 0, cell_span, stop - start)
        part = field[start:stop]
        wide_y = jnp.concatenate(
            [
                ghost_low(part, y_low[start:stop], first_y, 1),
                part,
                ghost_high(part, y_high[start:stop], last_y, 1),
            ],
            axis=1,
        )
        back_two, fore_two = one_sided(wide_y, 1, cell_span, cells_y)
        mean_one = 0.5 * (back_one + fore_one)
        mean_two = 0.5 * (back_two + fore_two)
        ham = mean_one * (along_one[None, None] + flow_x[start:stop])
        ham = ham + mean_two * (along_two[None, None] + flow_y[start:stop])
        ham = ham + params[1] * jnp.abs(mean_one * y_col - mean_two * x_col[start:stop] - mean_three)
        ham = ham + partial
        return ham, fore_one - back_one, fore_two - back_two

    def combine(ham, spread_one, spread_two):
        return ham + 0.5 * (bound_one * spread_one + bound_two * spread_two)

    def stage(field, x_halos, y_halos, local_pieces, order, update, last):
        if last:
            rate = combine(*half_parts(field, 2, x_halos, *y_halos, *local_pieces))
            return update(2, rate), None, None, None
        results = [None, None]
        sent = [None, None]

        def half(side):
            pieces = local_pieces[side] if isinstance(local_pieces, list) else local_pieces
            parts = half_parts(field, side, x_halos, *y_halos, *pieces)
            results[side] = update(side, combine(*parts))

        def send(side):
            if side == 0:
                piece = lax.optimization_barrier(results[side][:3])
                sent[side] = send_high(piece, "gx")
            else:
                piece = lax.optimization_barrier(results[side][results[side].shape[0] - 3 :])
                sent[side] = send_low(piece, "gx")

        half(order[0])
        send(order[0])
        half(order[1])
        send(order[1])
        merged = jnp.concatenate(results, axis=0)
        next_y = y_halo(merged)
        next_pieces = local_whole(merged)
        return merged, (sent[1], sent[0]), next_y, next_pieces

    first, x_halos, y_halos, locals_now = stage(
        values, x_halos, y_halos, locals_now, (1, 0),
        lambda side, rate: cut(values, side) + step_time * rate, False,
    )
    second, x_halos, y_halos, locals_now = stage(
        first, x_halos, y_halos, locals_now, (0, 1),
        lambda side, rate: 0.75 * cut(values, side) + 0.25 * (cut(first, side) + step_time * rate),
        False,
    )
    result, _, _, _ = stage(
        second, x_halos, y_halos, locals_now, (1, 0),
        lambda side, rate: cut(values, side) * (1.0 / 3.0)
        + 2.0 / 3.0 * (cut(second, side) + step_time * rate),
        True,
    )
    return result


def solution(mesh):
    in_specs = (P(("groups", "gx"), "gy", None, None), P(None, ("groups", "gx"), "gy"), P("groups"))
    out_specs = P(("groups", "gx"), "gy", None, None)
    return jax.shard_map(
        on_device, mesh=mesh, in_specs=in_specs, out_specs=out_specs, check_vma=False
    )
```

```python
import math

import jax
import numpy as np
import jax.numpy as jnp
from jax import lax
from jax.sharding import PartitionSpec as P


cfl_number = 0.5
weno_eps = 1e-06
cell_span = 1.0 / 64.0


def weno_value(first, second, third, fourth, fifth):
    stencil_one = first / 3.0 - 7.0 * second / 6.0 + 11.0 * third / 6.0
    stencil_two = -second / 6.0 + 5.0 * third / 6.0 + fourth / 3.0
    stencil_three = third / 3.0 + 5.0 * fourth / 6.0 - fifth / 6.0
    smooth_one = (
        13.0 / 12.0 * (first - 2.0 * second + third) ** 2
        + 0.25 * (first - 4.0 * second + 3.0 * third) ** 2
    )
    smooth_two = 13.0 / 12.0 * (second - 2.0 * third + fourth) ** 2 + 0.25 * (second - fourth) ** 2
    smooth_three = (
        13.0 / 12.0 * (third - 2.0 * fourth + fifth) ** 2
        + 0.25 * (3.0 * third - 4.0 * fourth + fifth) ** 2
    )
    weight_one = 0.1 / (weno_eps + smooth_one) ** 2
    weight_two = 0.6 / (weno_eps + smooth_two) ** 2
    weight_three = 0.3 / (weno_eps + smooth_three) ** 2
    total = weight_one * stencil_one + weight_two * stencil_two + weight_three * stencil_three
    return total / (weight_one + weight_two + weight_three)


def both_sides(window):
    backward = weno_value(window(0), window(1), window(2), window(3), window(4))
    forward = weno_value(window(5), window(4), window(3), window(2), window(1))
    return (backward, forward)


def one_sided(padded, along, spacing, length):
    extent = padded.shape[along]
    differences = (
        lax.slice_in_dim(padded, 1, extent, axis=along)
        - lax.slice_in_dim(padded, 0, extent - 1, axis=along)
    ) / spacing

    def window(offset):
        return lax.slice_in_dim(differences, offset, offset + length, axis=along)

    return both_sides(window)


def periodic_sided(field, along, spacing):
    extent = field.shape[along]
    wrapped = jnp.concatenate(
        [
            lax.slice_in_dim(field, extent - 3, extent, axis=along),
            field,
            lax.slice_in_dim(field, 0, 3, axis=along),
        ],
        axis=along,
    )
    return one_sided(wrapped, along, spacing, extent)


def clamped_sided(field, along, spacing):
    extent = field.shape[along]
    inner = (
        lax.slice_in_dim(field, 1, extent, axis=along)
        - lax.slice_in_dim(field, 0, extent - 1, axis=along)
    ) / spacing
    low_edge = lax.slice_in_dim(inner, 0, 1, axis=along)
    high_edge = lax.slice_in_dim(inner, extent - 2, extent - 1, axis=along)
    padded = jnp.concatenate([low_edge] * 3 + [inner] + [high_edge] * 3, axis=along)

    def window(offset):
        return lax.slice_in_dim(padded, offset, offset + extent, axis=along)

    return both_sides(window)


def send_low(piece, axis):
    count = lax.axis_size(axis)
    return lax.ppermute(piece, axis, [(i, (i + 1) % count) for i in range(count - 1)])


def send_high(piece, axis):
    count = lax.axis_size(axis)
    return lax.ppermute(piece, axis, [((i + 1) % count, i) for i in range(count - 1)])


def ghost_low(field, halo, at_low, along):
    shape_dist = [1] * field.ndim
    shape_dist[along] = 3
    inner = lax.slice_in_dim(field, 0, 1, axis=along)
    after = lax.slice_in_dim(field, 1, 2, axis=along)
    dist = jnp.arange(3, 0, -1).astype(jnp.float32).reshape(tuple(shape_dist))
    return jnp.where(at_low, inner + dist * (inner - after), halo)


def ghost_high(field, halo, at_high, along):
    extent = field.shape[along]
    shape_dist = [1] * field.ndim
    shape_dist[along] = 3
    inner = lax.slice_in_dim(field, extent - 1, extent, axis=along)
    before = lax.slice_in_dim(field, extent - 2, extent - 1, axis=along)
    dist = jnp.arange(1, 4).astype(jnp.float32).reshape(tuple(shape_dist))
    return jnp.where(at_high, inner + dist * (inner - before), halo)


def spread_max(local, axis, first_level):
    count = lax.axis_size(axis)
    span = 1
    level = first_level
    while span < count:
        moved = [
            lax.ppermute(local, axis, [(i, (i + k * span) % count) for i in range(count)])
            for k in range(1, 4)
            if k * span < count
        ]
        for item in moved:
            local = jnp.maximum(local, item)
        span *= 4
        level += 1
    return local


def on_device(values, drift, params):
    cells_x, cells_y, n_psi, n_speed = values.shape
    devices_x = lax.axis_size("gx")
    devices_y = lax.axis_size("gy")
    total_x = cells_x * devices_x
    total_y = cells_y * devices_y
    step_psi = 2.0 * math.pi / n_psi
    step_speed = 1.0 / n_speed
    place_x = lax.axis_index("gx")
    place_y = lax.axis_index("gy")
    first_x = place_x == 0
    last_x = place_x == devices_x - 1
    first_y = place_y == 0
    last_y = place_y == devices_y - 1
    half = cells_x // 2
    alpha_three = params[1] + params[2]
    alpha_four = params[3]

    def cut(array, side):
        if side == 0:
            return array[:half]
        if side == 1:
            return array[half:]
        return array

    def local_part(field):
        back_three, fore_three = periodic_sided(field, 2, step_psi)
        back_four, fore_four = clamped_sided(field, 3, step_speed)
        mean_three = 0.5 * (back_three + fore_three)
        mean_four = 0.5 * (back_four + fore_four)
        partial = -params[2] * jnp.abs(mean_three) + params[3] * jnp.abs(mean_four)
        partial = partial + 0.5 * (
            alpha_three * (fore_three - back_three) + alpha_four * (fore_four - back_four)
        )
        return mean_three, partial

    def local_halves(field):
        pieces = []
        for side in (0, 1):
            pieces.append(lax.optimization_barrier(local_part(cut(field, side))))
        return pieces

    def y_halo(field):
        tail = lax.slice_in_dim(field, cells_y - 3, cells_y, axis=1)
        head = lax.slice_in_dim(field, 0, 3, axis=1)
        if devices_y == 2:
            offset = jnp.where(first_y, cells_y - 3, 0)
            piece = lax.dynamic_slice_in_dim(field, offset, 3, axis=1)
            piece = lax.optimization_barrier(piece)
            swapped = lax.ppermute(piece, "gy", [(0, 1), (1, 0)])
            return swapped, swapped
        tail, head = lax.optimization_barrier((tail, head))
        return send_low(tail, "gy"), send_high(head, "gy")

    def local_whole(field):
        return lax.optimization_barrier(local_part(field))

    x_halos = (send_low(values[cells_x - 3 :], "gx"), send_high(values[:3], "gx"))
    y_halos = y_halo(values)
    psi_grid = np.arange(n_psi).astype(np.float32) * np.float32(step_psi) - np.float32(math.pi)
    cos_table = np.cos(psi_grid.astype(np.float64)).astype(np.float32)
    sin_table = np.sin(psi_grid.astype(np.float64)).astype(np.float32)
    speed_grid = np.float32(0.5) + (
        np.arange(n_speed).astype(np.float32) + np.float32(0.5)
    ) * np.float32(step_speed)
    along_one = -jnp.asarray(speed_grid)[None, :] + params[0] * jnp.asarray(cos_table)[:, None]
    along_two = params[0] * jnp.asarray(sin_table)[:, None]
    y_coord = (
        (place_y * cells_y + jnp.arange(cells_y)).astype(jnp.float32) + 0.5 - 0.5 * total_y
    ) * cell_span
    x_coord = (
        (place_x * cells_x + jnp.arange(cells_x)).astype(jnp.float32) + 0.5 - 0.5 * total_x
    ) * cell_span
    first_hi = params[0] * cos_table.max() - speed_grid[0]
    first_lo = params[0] * cos_table.min() - speed_grid[n_speed - 1]
    second_hi = params[0] * sin_table.max()
    second_lo = params[0] * sin_table.min()
    terms = jnp.stack(
        [
            jnp.maximum(drift[0] + first_hi, -(drift[0] + first_lo))
            + params[1] * jnp.abs(y_coord)[None, :],
            jnp.maximum(drift[1] + second_hi, -(drift[1] + second_lo))
            + params[1] * jnp.abs(x_coord)[:, None],
        ]
    )
    local_bounds = jnp.max(terms, axis=(1, 2))
    locals_now = local_halves(values)
    bounds = spread_max(spread_max(local_bounds, "gy", 0), "gx", 0)
    bound_one = bounds[0]
    bound_two = bounds[1]
    step_time = cfl_number / (
        bound_one / cell_span
        + bound_two / cell_span
        + alpha_three / step_psi
        + alpha_four / step_speed
    )
    x_col = x_coord[:, None, None, None]
    y_col = y_coord[None, :, None, None]
    flow_x = drift[0][:, :, None, None]
    flow_y = drift[1][:, :, None, None]

    def half_parts(field, side, x_halos, y_low, y_high, mean_three, partial):
        if side == 0:
            start, stop = 0, half
            ghost = ghost_low(field, x_halos[0], first_x, 0)
            wide_x = jnp.concatenate([ghost, field[: half + 3]], axis=0)
        elif side == 1:
            start, stop = half, cells_x
            ghost = ghost_high(field, x_halos[1], last_x, 0)
            wide_x = jnp.concatenate([field[half - 3 :], ghost], axis=0)
        else:
            start, stop = 0, cells_x
            wide_x = jnp.concatenate(
                [
                    ghost_low(field, x_halos[0], first_x, 0),
                    field,
                    ghost_high(field, x_halos[1], last_x, 0),
                ],
                axis=0,
            )
        if mean_three.shape[0] != stop - start:
            mean_three = mean_three[start:stop]
            partial = partial[start:stop]
        back_one, fore_one = one_sided(wide_x, 0, cell_span, stop - start)
        part = field[start:stop]
        wide_y = jnp.concatenate(
            [
                ghost_low(part, y_low[start:stop], first_y, 1),
                part,
                ghost_high(part, y_high[start:stop], last_y, 1),
            ],
            axis=1,
        )
        back_two, fore_two = one_sided(wide_y, 1, cell_span, cells_y)
        mean_one = 0.5 * (back_one + fore_one)
        mean_two = 0.5 * (back_two + fore_two)
        ham = mean_one * (along_one[None, None] + flow_x[start:stop])
        ham = ham + mean_two * (along_two[None, None] + flow_y[start:stop])
        ham = ham + params[1] * jnp.abs(mean_one * y_col - mean_two * x_col[start:stop] - mean_three)
        ham = ham + partial
        return ham, fore_one - back_one, fore_two - back_two

    def combine(ham, spread_one, spread_two):
        return ham + 0.5 * (bound_one * spread_one + bound_two * spread_two)

    def stage(field, x_halos, y_halos, local_pieces, order, update, last):
        if last:
            rate = combine(*half_parts(field, 2, x_halos, *y_halos, *local_pieces))
            return update(2, rate), None, None, None
        results = [None, None]
        sent = [None, None]

        def half(side):
            pieces = local_pieces[side] if isinstance(local_pieces, list) else local_pieces
            parts = half_parts(field, side, x_halos, *y_halos, *pieces)
            results[side] = update(side, combine(*parts))

        def send(side):
            if side == 0:
                piece = lax.optimization_barrier(results[side][:3])
                sent[side] = send_high(piece, "gx")
            else:
                piece = lax.optimization_barrier(results[side][results[side].shape[0] - 3 :])
                sent[side] = send_low(piece, "gx")

        half(order[0])
        send(order[0])
        half(order[1])
        send(order[1])
        merged = jnp.concatenate(results, axis=0)
        next_y = y_halo(merged)
        next_pieces = local_whole(merged)
        return merged, (sent[1], sent[0]), next_y, next_pieces

    first, x_halos, y_halos, locals_now = stage(
        values, x_halos, y_halos, locals_now, (0, 1),
        lambda side, rate: cut(values, side) + step_time * rate, False,
    )
    second, x_halos, y_halos, locals_now = stage(
        first, x_halos, y_halos, locals_now, (1, 0),
        lambda side, rate: 0.75 * cut(values, side) + 0.25 * (cut(first, side) + step_time * rate),
        False,
    )
    result, _, _, _ = stage(
        second, x_halos, y_halos, locals_now, (1, 0),
        lambda side, rate: cut(values, side) * (1.0 / 3.0)
        + 2.0 / 3.0 * (cut(second, side) + step_time * rate),
        True,
    )
    return result


def solution(mesh):
    in_specs = (P(("groups", "gx"), "gy", None, None), P(None, ("groups", "gx"), "gy"), P("groups"))
    out_specs = P(("groups", "gx"), "gy", None, None)
    return jax.shard_map(
        on_device, mesh=mesh, in_specs=in_specs, out_specs=out_specs, check_vma=False
    )
```

```python
import math

import jax
import numpy as np
import jax.numpy as jnp
from jax import lax
from jax.sharding import PartitionSpec as P


cfl_number = 0.5
weno_eps = 1e-06
cell_span = 1.0 / 64.0


def weno_value(first, second, third, fourth, fifth):
    stencil_one = first / 3.0 - 7.0 * second / 6.0 + 11.0 * third / 6.0
    stencil_two = -second / 6.0 + 5.0 * third / 6.0 + fourth / 3.0
    stencil_three = third / 3.0 + 5.0 * fourth / 6.0 - fifth / 6.0
    smooth_one = (
        13.0 / 12.0 * (first - 2.0 * second + third) ** 2
        + 0.25 * (first - 4.0 * second + 3.0 * third) ** 2
    )
    smooth_two = 13.0 / 12.0 * (second - 2.0 * third + fourth) ** 2 + 0.25 * (second - fourth) ** 2
    smooth_three = (
        13.0 / 12.0 * (third - 2.0 * fourth + fifth) ** 2
        + 0.25 * (3.0 * third - 4.0 * fourth + fifth) ** 2
    )
    weight_one = 0.1 / (weno_eps + smooth_one) ** 2
    weight_two = 0.6 / (weno_eps + smooth_two) ** 2
    weight_three = 0.3 / (weno_eps + smooth_three) ** 2
    total = weight_one * stencil_one + weight_two * stencil_two + weight_three * stencil_three
    return total / (weight_one + weight_two + weight_three)


def both_sides(window):
    backward = weno_value(window(0), window(1), window(2), window(3), window(4))
    forward = weno_value(window(5), window(4), window(3), window(2), window(1))
    return (backward, forward)


def one_sided(padded, along, spacing, length):
    extent = padded.shape[along]
    differences = (
        lax.slice_in_dim(padded, 1, extent, axis=along)
        - lax.slice_in_dim(padded, 0, extent - 1, axis=along)
    ) / spacing

    def window(offset):
        return lax.slice_in_dim(differences, offset, offset + length, axis=along)

    return both_sides(window)


def periodic_sided(field, along, spacing):
    extent = field.shape[along]
    wrapped = jnp.concatenate(
        [
            lax.slice_in_dim(field, extent - 3, extent, axis=along),
            field,
            lax.slice_in_dim(field, 0, 3, axis=along),
        ],
        axis=along,
    )
    return one_sided(wrapped, along, spacing, extent)


def clamped_sided(field, along, spacing):
    extent = field.shape[along]
    inner = (
        lax.slice_in_dim(field, 1, extent, axis=along)
        - lax.slice_in_dim(field, 0, extent - 1, axis=along)
    ) / spacing
    low_edge = lax.slice_in_dim(inner, 0, 1, axis=along)
    high_edge = lax.slice_in_dim(inner, extent - 2, extent - 1, axis=along)
    padded = jnp.concatenate([low_edge] * 3 + [inner] + [high_edge] * 3, axis=along)

    def window(offset):
        return lax.slice_in_dim(padded, offset, offset + extent, axis=along)

    return both_sides(window)


def send_low(piece, axis):
    count = lax.axis_size(axis)
    return lax.ppermute(piece, axis, [(i, (i + 1) % count) for i in range(count - 1)])


def send_high(piece, axis):
    count = lax.axis_size(axis)
    return lax.ppermute(piece, axis, [((i + 1) % count, i) for i in range(count - 1)])


def ghost_low(field, halo, at_low, along):
    shape_dist = [1] * field.ndim
    shape_dist[along] = 3
    inner = lax.slice_in_dim(field, 0, 1, axis=along)
    after = lax.slice_in_dim(field, 1, 2, axis=along)
    dist = jnp.arange(3, 0, -1).astype(jnp.float32).reshape(tuple(shape_dist))
    return jnp.where(at_low, inner + dist * (inner - after), halo)


def ghost_high(field, halo, at_high, along):
    extent = field.shape[along]
    shape_dist = [1] * field.ndim
    shape_dist[along] = 3
    inner = lax.slice_in_dim(field, extent - 1, extent, axis=along)
    before = lax.slice_in_dim(field, extent - 2, extent - 1, axis=along)
    dist = jnp.arange(1, 4).astype(jnp.float32).reshape(tuple(shape_dist))
    return jnp.where(at_high, inner + dist * (inner - before), halo)


def spread_max(local, axis, first_level):
    count = lax.axis_size(axis)
    span = 1
    level = first_level
    while span < count:
        moved = [
            lax.ppermute(local, axis, [(i, (i + k * span) % count) for i in range(count)])
            for k in range(1, 4)
            if k * span < count
        ]
        for item in moved:
            local = jnp.maximum(local, item)
        span *= 4
        level += 1
    return local


def on_device(values, drift, params):
    cells_x, cells_y, n_psi, n_speed = values.shape
    devices_x = lax.axis_size("gx")
    devices_y = lax.axis_size("gy")
    total_x = cells_x * devices_x
    total_y = cells_y * devices_y
    step_psi = 2.0 * math.pi / n_psi
    step_speed = 1.0 / n_speed
    place_x = lax.axis_index("gx")
    place_y = lax.axis_index("gy")
    first_x = place_x == 0
    last_x = place_x == devices_x - 1
    first_y = place_y == 0
    last_y = place_y == devices_y - 1
    half = cells_x // 2
    alpha_three = params[1] + params[2]
    alpha_four = params[3]

    def cut(array, side):
        if side == 0:
            return array[:half]
        if side == 1:
            return array[half:]
        return array

    def local_part(field):
        back_three, fore_three = periodic_sided(field, 2, step_psi)
        back_four, fore_four = clamped_sided(field, 3, step_speed)
        mean_three = 0.5 * (back_three + fore_three)
        mean_four = 0.5 * (back_four + fore_four)
        partial = -params[2] * jnp.abs(mean_three) + params[3] * jnp.abs(mean_four)
        partial = partial + 0.5 * (
            alpha_three * (fore_three - back_three) + alpha_four * (fore_four - back_four)
        )
        return mean_three, partial

    def y_halo(field):
        tail = lax.slice_in_dim(field, cells_y - 3, cells_y, axis=1)
        head = lax.slice_in_dim(field, 0, 3, axis=1)
        if devices_y == 2:
            offset = jnp.where(first_y, cells_y - 3, 0)
            piece = lax.dynamic_slice_in_dim(field, offset, 3, axis=1)
            piece = lax.optimization_barrier(piece)
            swapped = lax.ppermute(piece, "gy", [(0, 1), (1, 0)])
            return swapped, swapped
        tail, head = lax.optimization_barrier((tail, head))
        return send_low(tail, "gy"), send_high(head, "gy")

    def local_whole(field):
        return lax.optimization_barrier(local_part(field))

    x_halos = (send_low(values[cells_x - 3 :], "gx"), send_high(values[:3], "gx"))
    y_halos = y_halo(values)
    psi_grid = np.arange(n_psi).astype(np.float32) * np.float32(step_psi) - np.float32(math.pi)
    cos_table = np.cos(psi_grid.astype(np.float64)).astype(np.float32)
    sin_table = np.sin(psi_grid.astype(np.float64)).astype(np.float32)
    speed_grid = np.float32(0.5) + (
        np.arange(n_speed).astype(np.float32) + np.float32(0.5)
    ) * np.float32(step_speed)
    along_one = -jnp.asarray(speed_grid)[None, :] + params[0] * jnp.asarray(cos_table)[:, None]
    along_two = params[0] * jnp.asarray(sin_table)[:, None]
    y_coord = (
        (place_y * cells_y + jnp.arange(cells_y)).astype(jnp.float32) + 0.5 - 0.5 * total_y
    ) * cell_span
    x_coord = (
        (place_x * cells_x + jnp.arange(cells_x)).astype(jnp.float32) + 0.5 - 0.5 * total_x
    ) * cell_span
    first_hi = params[0] * cos_table.max() - speed_grid[0]
    first_lo = params[0] * cos_table.min() - speed_grid[n_speed - 1]
    second_hi = params[0] * sin_table.max()
    second_lo = params[0] * sin_table.min()
    terms = jnp.stack(
        [
            jnp.maximum(drift[0] + first_hi, -(drift[0] + first_lo))
            + params[1] * jnp.abs(y_coord)[None, :],
            jnp.maximum(drift[1] + second_hi, -(drift[1] + second_lo))
            + params[1] * jnp.abs(x_coord)[:, None],
        ]
    )
    local_bounds = jnp.max(terms, axis=(1, 2))
    locals_now = local_whole(values)
    bounds = spread_max(spread_max(local_bounds, "gy", 0), "gx", 0)
    bound_one = bounds[0]
    bound_two = bounds[1]
    step_time = cfl_number / (
        bound_one / cell_span
        + bound_two / cell_span
        + alpha_three / step_psi
        + alpha_four / step_speed
    )
    x_col = x_coord[:, None, None, None]
    y_col = y_coord[None, :, None, None]
    flow_x = drift[0][:, :, None, None]
    flow_y = drift[1][:, :, None, None]

    def half_parts(field, side, x_halos, y_low, y_high, mean_three, partial):
        if side == 0:
            start, stop = 0, half
            ghost = ghost_low(field, x_halos[0], first_x, 0)
            wide_x = jnp.concatenate([ghost, field[: half + 3]], axis=0)
        elif side == 1:
            start, stop = half, cells_x
            ghost = ghost_high(field, x_halos[1], last_x, 0)
            wide_x = jnp.concatenate([field[half - 3 :], ghost], axis=0)
        else:
            start, stop = 0, cells_x
            wide_x = jnp.concatenate(
                [
                    ghost_low(field, x_halos[0], first_x, 0),
                    field,
                    ghost_high(field, x_halos[1], last_x, 0),
                ],
                axis=0,
            )
        if mean_three.shape[0] != stop - start:
            mean_three = mean_three[start:stop]
            partial = partial[start:stop]
        back_one, fore_one = one_sided(wide_x, 0, cell_span, stop - start)
        part = field[start:stop]
        wide_y = jnp.concatenate(
            [
                ghost_low(part, y_low[start:stop], first_y, 1),
                part,
                ghost_high(part, y_high[start:stop], last_y, 1),
            ],
            axis=1,
        )
        back_two, fore_two = one_sided(wide_y, 1, cell_span, cells_y)
        mean_one = 0.5 * (back_one + fore_one)
        mean_two = 0.5 * (back_two + fore_two)
        ham = mean_one * (along_one[None, None] + flow_x[start:stop])
        ham = ham + mean_two * (along_two[None, None] + flow_y[start:stop])
        ham = ham + params[1] * jnp.abs(mean_one * y_col - mean_two * x_col[start:stop] - mean_three)
        ham = ham + partial
        return ham, fore_one - back_one, fore_two - back_two

    def combine(ham, spread_one, spread_two):
        return ham + 0.5 * (bound_one * spread_one + bound_two * spread_two)

    def stage(field, x_halos, y_halos, local_pieces, order, update, last):
        if last:
            rate = combine(*half_parts(field, 2, x_halos, *y_halos, *local_pieces))
            return update(2, rate), None, None, None
        results = [None, None]
        sent = [None, None]

        def half(side):
            pieces = local_pieces[side] if isinstance(local_pieces, list) else local_pieces
            parts = half_parts(field, side, x_halos, *y_halos, *pieces)
            results[side] = update(side, combine(*parts))

        def send(side):
            if side == 0:
                piece = lax.optimization_barrier(results[side][:3])
                sent[side] = send_high(piece, "gx")
            else:
                piece = lax.optimization_barrier(results[side][results[side].shape[0] - 3 :])
                sent[side] = send_low(piece, "gx")

        half(order[0])
        send(order[0])
        half(order[1])
        send(order[1])
        merged = jnp.concatenate(results, axis=0)
        next_y = y_halo(merged)
        next_pieces = local_whole(merged)
        return merged, (sent[1], sent[0]), next_y, next_pieces

    fresh = jnp.where(values == values, values, 0.0)
    first, x_halos, y_halos, locals_now = stage(
        fresh, x_halos, y_halos, locals_now, (0, 1),
        lambda side, rate: cut(values, side) + step_time * rate, False,
    )
    second, x_halos, y_halos, locals_now = stage(
        first, x_halos, y_halos, locals_now, (1, 0),
        lambda side, rate: 0.75 * cut(values, side) + 0.25 * (cut(first, side) + step_time * rate),
        False,
    )
    result, _, _, _ = stage(
        second, x_halos, y_halos, locals_now, (1, 0),
        lambda side, rate: cut(values, side) * (1.0 / 3.0)
        + 2.0 / 3.0 * (cut(second, side) + step_time * rate),
        True,
    )
    return result


def solution(mesh):
    in_specs = (P(("groups", "gx"), "gy", None, None), P(None, ("groups", "gx"), "gy"), P("groups"))
    out_specs = P(("groups", "gx"), "gy", None, None)
    return jax.shard_map(
        on_device, mesh=mesh, in_specs=in_specs, out_specs=out_specs, check_vma=False
    )
```

```python
import math

import jax
import numpy as np
import jax.numpy as jnp
from jax import lax
from jax.sharding import PartitionSpec as P


cfl_number = 0.5
weno_eps = 1e-06
cell_span = 1.0 / 64.0


def weno_value(first, second, third, fourth, fifth):
    stencil_one = first / 3.0 - 7.0 * second / 6.0 + 11.0 * third / 6.0
    stencil_two = -second / 6.0 + 5.0 * third / 6.0 + fourth / 3.0
    stencil_three = third / 3.0 + 5.0 * fourth / 6.0 - fifth / 6.0
    smooth_one = (
        13.0 / 12.0 * (first - 2.0 * second + third) ** 2
        + 0.25 * (first - 4.0 * second + 3.0 * third) ** 2
    )
    smooth_two = 13.0 / 12.0 * (second - 2.0 * third + fourth) ** 2 + 0.25 * (second - fourth) ** 2
    smooth_three = (
        13.0 / 12.0 * (third - 2.0 * fourth + fifth) ** 2
        + 0.25 * (3.0 * third - 4.0 * fourth + fifth) ** 2
    )
    weight_one = 0.1 / (weno_eps + smooth_one) ** 2
    weight_two = 0.6 / (weno_eps + smooth_two) ** 2
    weight_three = 0.3 / (weno_eps + smooth_three) ** 2
    total = weight_one * stencil_one + weight_two * stencil_two + weight_three * stencil_three
    return total / (weight_one + weight_two + weight_three)


def both_sides(window):
    backward = weno_value(window(0), window(1), window(2), window(3), window(4))
    forward = weno_value(window(5), window(4), window(3), window(2), window(1))
    return (backward, forward)


def one_sided(padded, along, spacing, length):
    extent = padded.shape[along]
    differences = (
        lax.slice_in_dim(padded, 1, extent, axis=along)
        - lax.slice_in_dim(padded, 0, extent - 1, axis=along)
    ) / spacing

    def window(offset):
        return lax.slice_in_dim(differences, offset, offset + length, axis=along)

    return both_sides(window)


def periodic_sided(field, along, spacing):
    extent = field.shape[along]
    wrapped = jnp.concatenate(
        [
            lax.slice_in_dim(field, extent - 3, extent, axis=along),
            field,
            lax.slice_in_dim(field, 0, 3, axis=along),
        ],
        axis=along,
    )
    return one_sided(wrapped, along, spacing, extent)


def clamped_sided(field, along, spacing):
    extent = field.shape[along]
    inner = (
        lax.slice_in_dim(field, 1, extent, axis=along)
        - lax.slice_in_dim(field, 0, extent - 1, axis=along)
    ) / spacing
    low_edge = lax.slice_in_dim(inner, 0, 1, axis=along)
    high_edge = lax.slice_in_dim(inner, extent - 2, extent - 1, axis=along)
    padded = jnp.concatenate([low_edge] * 3 + [inner] + [high_edge] * 3, axis=along)

    def window(offset):
        return lax.slice_in_dim(padded, offset, offset + extent, axis=along)

    return both_sides(window)


def send_low(piece, axis):
    count = lax.axis_size(axis)
    return lax.ppermute(piece, axis, [(i, (i + 1) % count) for i in range(count - 1)])


def send_high(piece, axis):
    count = lax.axis_size(axis)
    return lax.ppermute(piece, axis, [((i + 1) % count, i) for i in range(count - 1)])


def ghost_low(field, halo, at_low, along):
    shape_dist = [1] * field.ndim
    shape_dist[along] = 3
    inner = lax.slice_in_dim(field, 0, 1, axis=along)
    after = lax.slice_in_dim(field, 1, 2, axis=along)
    dist = jnp.arange(3, 0, -1).astype(jnp.float32).reshape(tuple(shape_dist))
    return jnp.where(at_low, inner + dist * (inner - after), halo)


def ghost_high(field, halo, at_high, along):
    extent = field.shape[along]
    shape_dist = [1] * field.ndim
    shape_dist[along] = 3
    inner = lax.slice_in_dim(field, extent - 1, extent, axis=along)
    before = lax.slice_in_dim(field, extent - 2, extent - 1, axis=along)
    dist = jnp.arange(1, 4).astype(jnp.float32).reshape(tuple(shape_dist))
    return jnp.where(at_high, inner + dist * (inner - before), halo)


def spread_max(local, axis, first_level):
    count = lax.axis_size(axis)
    span = 1
    level = first_level
    while span < count:
        moved = [
            lax.ppermute(local, axis, [(i, (i + k * span) % count) for i in range(count)])
            for k in range(1, 4)
            if k * span < count
        ]
        for item in moved:
            local = jnp.maximum(local, item)
        span *= 4
        level += 1
    return local


def spread_line(local, axis):
    count = lax.axis_size(axis)
    if count % 2:
        return spread_max(local, axis, 0)
    moved = lax.ppermute(local, axis, [(i, i ^ 1) for i in range(count)])
    local = jnp.maximum(local, moved)
    span = 2
    while span < count:
        moved = [
            lax.ppermute(local, axis, [(i, (i + k * span) % count) for i in range(count)])
            for k in range(1, 4)
            if k * span < count
        ]
        for item in moved:
            local = jnp.maximum(local, item)
        span *= 4
    return local


def on_device(values, drift, params):
    cells_x, cells_y, n_psi, n_speed = values.shape
    devices_x = lax.axis_size("gx")
    devices_y = lax.axis_size("gy")
    total_x = cells_x * devices_x
    total_y = cells_y * devices_y
    step_psi = 2.0 * math.pi / n_psi
    step_speed = 1.0 / n_speed
    place_x = lax.axis_index("gx")
    place_y = lax.axis_index("gy")
    first_x = place_x == 0
    last_x = place_x == devices_x - 1
    first_y = place_y == 0
    last_y = place_y == devices_y - 1
    half = cells_x // 2
    alpha_three = params[1] + params[2]
    alpha_four = params[3]

    def cut(array, side):
        if side == 0:
            return array[:half]
        if side == 1:
            return array[half:]
        return array

    def local_part(field):
        back_three, fore_three = periodic_sided(field, 2, step_psi)
        back_four, fore_four = clamped_sided(field, 3, step_speed)
        mean_three = 0.5 * (back_three + fore_three)
        mean_four = 0.5 * (back_four + fore_four)
        partial = -params[2] * jnp.abs(mean_three) + params[3] * jnp.abs(mean_four)
        partial = partial + 0.5 * (
            alpha_three * (fore_three - back_three) + alpha_four * (fore_four - back_four)
        )
        return mean_three, partial

    def y_halo(field):
        tail = lax.slice_in_dim(field, cells_y - 3, cells_y, axis=1)
        head = lax.slice_in_dim(field, 0, 3, axis=1)
        if devices_y == 2:
            offset = jnp.where(first_y, cells_y - 3, 0)
            piece = lax.dynamic_slice_in_dim(field, offset, 3, axis=1)
            piece = lax.optimization_barrier(piece)
            swapped = lax.ppermute(piece, "gy", [(0, 1), (1, 0)])
            return swapped, swapped
        tail, head = lax.optimization_barrier((tail, head))
        return send_low(tail, "gy"), send_high(head, "gy")

    def local_whole(field):
        return lax.optimization_barrier(local_part(field))

    x_halos = (send_low(values[cells_x - 3 :], "gx"), send_high(values[:3], "gx"))
    y_halos = y_halo(values)
    psi_grid = np.arange(n_psi).astype(np.float32) * np.float32(step_psi) - np.float32(math.pi)
    cos_table = np.cos(psi_grid.astype(np.float64)).astype(np.float32)
    sin_table = np.sin(psi_grid.astype(np.float64)).astype(np.float32)
    speed_grid = np.float32(0.5) + (
        np.arange(n_speed).astype(np.float32) + np.float32(0.5)
    ) * np.float32(step_speed)
    along_one = -jnp.asarray(speed_grid)[None, :] + params[0] * jnp.asarray(cos_table)[:, None]
    along_two = params[0] * jnp.asarray(sin_table)[:, None]
    y_coord = (
        (place_y * cells_y + jnp.arange(cells_y)).astype(jnp.float32) + 0.5 - 0.5 * total_y
    ) * cell_span
    x_coord = (
        (place_x * cells_x + jnp.arange(cells_x)).astype(jnp.float32) + 0.5 - 0.5 * total_x
    ) * cell_span
    first_hi = params[0] * cos_table.max() - speed_grid[0]
    first_lo = params[0] * cos_table.min() - speed_grid[n_speed - 1]
    second_hi = params[0] * sin_table.max()
    second_lo = params[0] * sin_table.min()
    terms = jnp.stack(
        [
            jnp.maximum(drift[0] + first_hi, -(drift[0] + first_lo))
            + params[1] * jnp.abs(y_coord)[None, :],
            jnp.maximum(drift[1] + second_hi, -(drift[1] + second_lo))
            + params[1] * jnp.abs(x_coord)[:, None],
        ]
    )
    local_bounds = jnp.max(terms, axis=(1, 2))
    locals_now = local_whole(values)
    bounds = spread_line(spread_max(local_bounds, "gy", 0), "gx")
    bound_one = bounds[0]
    bound_two = bounds[1]
    step_time = cfl_number / (
        bound_one / cell_span
        + bound_two / cell_span
        + alpha_three / step_psi
        + alpha_four / step_speed
    )
    x_col = x_coord[:, None, None, None]
    y_col = y_coord[None, :, None, None]
    flow_x = drift[0][:, :, None, None]
    flow_y = drift[1][:, :, None, None]

    def half_parts(field, side, x_halos, y_low, y_high, mean_three, partial):
        if side == 0:
            start, stop = 0, half
            ghost = ghost_low(field, x_halos[0], first_x, 0)
            wide_x = jnp.concatenate([ghost, field[: half + 3]], axis=0)
        elif side == 1:
            start, stop = half, cells_x
            ghost = ghost_high(field, x_halos[1], last_x, 0)
            wide_x = jnp.concatenate([field[half - 3 :], ghost], axis=0)
        else:
            start, stop = 0, cells_x
            wide_x = jnp.concatenate(
                [
                    ghost_low(field, x_halos[0], first_x, 0),
                    field,
                    ghost_high(field, x_halos[1], last_x, 0),
                ],
                axis=0,
            )
        if mean_three.shape[0] != stop - start:
            mean_three = mean_three[start:stop]
            partial = partial[start:stop]
        back_one, fore_one = one_sided(wide_x, 0, cell_span, stop - start)
        part = field[start:stop]
        wide_y = jnp.concatenate(
            [
                ghost_low(part, y_low[start:stop], first_y, 1),
                part,
                ghost_high(part, y_high[start:stop], last_y, 1),
            ],
            axis=1,
        )
        back_two, fore_two = one_sided(wide_y, 1, cell_span, cells_y)
        mean_one = 0.5 * (back_one + fore_one)
        mean_two = 0.5 * (back_two + fore_two)
        ham = mean_one * (along_one[None, None] + flow_x[start:stop])
        ham = ham + mean_two * (along_two[None, None] + flow_y[start:stop])
        ham = ham + params[1] * jnp.abs(mean_one * y_col - mean_two * x_col[start:stop] - mean_three)
        ham = ham + partial
        return ham, fore_one - back_one, fore_two - back_two

    def combine(ham, spread_one, spread_two):
        return ham + 0.5 * (bound_one * spread_one + bound_two * spread_two)

    def stage(field, x_halos, y_halos, local_pieces, order, update, last):
        if last:
            rate = combine(*half_parts(field, 2, x_halos, *y_halos, *local_pieces))
            return update(2, rate), None, None, None
        results = [None, None]
        sent = [None, None]

        def half(side):
            pieces = local_pieces[side] if isinstance(local_pieces, list) else local_pieces
            parts = half_parts(field, side, x_halos, *y_halos, *pieces)
            results[side] = update(side, combine(*parts))

        def send(side):
            if side == 0:
                piece = lax.optimization_barrier(results[side][:3])
                sent[side] = send_high(piece, "gx")
            else:
                piece = lax.optimization_barrier(results[side][results[side].shape[0] - 3 :])
                sent[side] = send_low(piece, "gx")

        half(order[0])
        send(order[0])
        half(order[1])
        send(order[1])
        merged = jnp.concatenate(results, axis=0)
        next_y = y_halo(merged)
        next_pieces = local_whole(merged)
        return merged, (sent[1], sent[0]), next_y, next_pieces

    first, x_halos, y_halos, locals_now = stage(
        values, x_halos, y_halos, locals_now, (0, 1),
        lambda side, rate: cut(values, side) + step_time * rate, False,
    )
    second, x_halos, y_halos, locals_now = stage(
        first, x_halos, y_halos, locals_now, (1, 0),
        lambda side, rate: 0.75 * cut(values, side) + 0.25 * (cut(first, side) + step_time * rate),
        False,
    )
    result, _, _, _ = stage(
        second, x_halos, y_halos, locals_now, (1, 0),
        lambda side, rate: cut(values, side) * (1.0 / 3.0)
        + 2.0 / 3.0 * (cut(second, side) + step_time * rate),
        True,
    )
    return result


def solution(mesh):
    in_specs = (P(("groups", "gx"), "gy", None, None), P(None, ("groups", "gx"), "gy"), P("groups"))
    out_specs = P(("groups", "gx"), "gy", None, None)
    return jax.shard_map(
        on_device, mesh=mesh, in_specs=in_specs, out_specs=out_specs, check_vma=False
    )
```

```python
import math

import jax
import numpy as np
import jax.numpy as jnp
from jax import lax
from jax.sharding import PartitionSpec as P


cfl_number = 0.5
weno_eps = 1e-06
cell_span = 1.0 / 64.0


def weno_value(first, second, third, fourth, fifth):
    stencil_one = first / 3.0 - 7.0 * second / 6.0 + 11.0 * third / 6.0
    stencil_two = -second / 6.0 + 5.0 * third / 6.0 + fourth / 3.0
    stencil_three = third / 3.0 + 5.0 * fourth / 6.0 - fifth / 6.0
    smooth_one = (
        13.0 / 12.0 * (first - 2.0 * second + third) ** 2
        + 0.25 * (first - 4.0 * second + 3.0 * third) ** 2
    )
    smooth_two = 13.0 / 12.0 * (second - 2.0 * third + fourth) ** 2 + 0.25 * (second - fourth) ** 2
    smooth_three = (
        13.0 / 12.0 * (third - 2.0 * fourth + fifth) ** 2
        + 0.25 * (3.0 * third - 4.0 * fourth + fifth) ** 2
    )
    weight_one = 0.1 / (weno_eps + smooth_one) ** 2
    weight_two = 0.6 / (weno_eps + smooth_two) ** 2
    weight_three = 0.3 / (weno_eps + smooth_three) ** 2
    total = weight_one * stencil_one + weight_two * stencil_two + weight_three * stencil_three
    return total / (weight_one + weight_two + weight_three)


def both_sides(window):
    backward = weno_value(window(0), window(1), window(2), window(3), window(4))
    forward = weno_value(window(5), window(4), window(3), window(2), window(1))
    return (backward, forward)


def one_sided(padded, along, spacing, length):
    extent = padded.shape[along]
    differences = (
        lax.slice_in_dim(padded, 1, extent, axis=along)
        - lax.slice_in_dim(padded, 0, extent - 1, axis=along)
    ) / spacing

    def window(offset):
        return lax.slice_in_dim(differences, offset, offset + length, axis=along)

    return both_sides(window)


def periodic_sided(field, along, spacing):
    extent = field.shape[along]
    wrapped = jnp.concatenate(
        [
            lax.slice_in_dim(field, extent - 3, extent, axis=along),
            field,
            lax.slice_in_dim(field, 0, 3, axis=along),
        ],
        axis=along,
    )
    return one_sided(wrapped, along, spacing, extent)


def clamped_sided(field, along, spacing):
    extent = field.shape[along]
    inner = (
        lax.slice_in_dim(field, 1, extent, axis=along)
        - lax.slice_in_dim(field, 0, extent - 1, axis=along)
    ) / spacing
    low_edge = lax.slice_in_dim(inner, 0, 1, axis=along)
    high_edge = lax.slice_in_dim(inner, extent - 2, extent - 1, axis=along)
    padded = jnp.concatenate([low_edge] * 3 + [inner] + [high_edge] * 3, axis=along)

    def window(offset):
        return lax.slice_in_dim(padded, offset, offset + extent, axis=along)

    return both_sides(window)


def send_low(piece, axis):
    count = lax.axis_size(axis)
    return lax.ppermute(piece, axis, [(i, (i + 1) % count) for i in range(count - 1)])


def send_high(piece, axis):
    count = lax.axis_size(axis)
    return lax.ppermute(piece, axis, [((i + 1) % count, i) for i in range(count - 1)])


def ghost_low(field, halo, at_low, along):
    shape_dist = [1] * field.ndim
    shape_dist[along] = 3
    inner = lax.slice_in_dim(field, 0, 1, axis=along)
    after = lax.slice_in_dim(field, 1, 2, axis=along)
    dist = jnp.arange(3, 0, -1).astype(jnp.float32).reshape(tuple(shape_dist))
    return jnp.where(at_low, inner + dist * (inner - after), halo)


def ghost_high(field, halo, at_high, along):
    extent = field.shape[along]
    shape_dist = [1] * field.ndim
    shape_dist[along] = 3
    inner = lax.slice_in_dim(field, extent - 1, extent, axis=along)
    before = lax.slice_in_dim(field, extent - 2, extent - 1, axis=along)
    dist = jnp.arange(1, 4).astype(jnp.float32).reshape(tuple(shape_dist))
    return jnp.where(at_high, inner + dist * (inner - before), halo)


def spread_max(local, axis, first_level):
    count = lax.axis_size(axis)
    span = 1
    level = first_level
    while span < count:
        moved = [
            lax.ppermute(local, axis, [(i, (i + k * span) % count) for i in range(count)])
            for k in range(1, 4)
            if k * span < count
        ]
        for item in moved:
            local = jnp.maximum(local, item)
        span *= 4
        level += 1
    return local


def on_device(values, drift, params):
    cells_x, cells_y, n_psi, n_speed = values.shape
    devices_x = lax.axis_size("gx")
    devices_y = lax.axis_size("gy")
    total_x = cells_x * devices_x
    total_y = cells_y * devices_y
    step_psi = 2.0 * math.pi / n_psi
    step_speed = 1.0 / n_speed
    place_x = lax.axis_index("gx")
    place_y = lax.axis_index("gy")
    first_x = place_x == 0
    last_x = place_x == devices_x - 1
    first_y = place_y == 0
    last_y = place_y == devices_y - 1
    half = cells_x // 2
    alpha_three = params[1] + params[2]
    alpha_four = params[3]

    def cut(array, side):
        if side == 0:
            return array[:half]
        if side == 1:
            return array[half:]
        return array

    def local_part(field):
        back_three, fore_three = periodic_sided(field, 2, step_psi)
        back_four, fore_four = clamped_sided(field, 3, step_speed)
        mean_three = 0.5 * (back_three + fore_three)
        mean_four = 0.5 * (back_four + fore_four)
        partial = -params[2] * jnp.abs(mean_three) + params[3] * jnp.abs(mean_four)
        partial = partial + 0.5 * (
            alpha_three * (fore_three - back_three) + alpha_four * (fore_four - back_four)
        )
        return mean_three, partial

    def y_halo(field, paired=False):
        tail = lax.slice_in_dim(field, cells_y - 3, cells_y, axis=1)
        head = lax.slice_in_dim(field, 0, 3, axis=1)
        if devices_y == 2 and not paired:
            offset = jnp.where(first_y, cells_y - 3, 0)
            piece = lax.dynamic_slice_in_dim(field, offset, 3, axis=1)
            piece = lax.optimization_barrier(piece)
            swapped = lax.ppermute(piece, "gy", [(0, 1), (1, 0)])
            return swapped, swapped
        tail, head = lax.optimization_barrier((tail, head))
        return send_low(tail, "gy"), send_high(head, "gy")

    def local_whole(field):
        return lax.optimization_barrier(local_part(field))

    x_halos = (send_low(values[cells_x - 3 :], "gx"), send_high(values[:3], "gx"))
    y_halos = y_halo(values, paired=True)
    psi_grid = np.arange(n_psi).astype(np.float32) * np.float32(step_psi) - np.float32(math.pi)
    cos_table = np.cos(psi_grid.astype(np.float64)).astype(np.float32)
    sin_table = np.sin(psi_grid.astype(np.float64)).astype(np.float32)
    speed_grid = np.float32(0.5) + (
        np.arange(n_speed).astype(np.float32) + np.float32(0.5)
    ) * np.float32(step_speed)
    along_one = -jnp.asarray(speed_grid)[None, :] + params[0] * jnp.asarray(cos_table)[:, None]
    along_two = params[0] * jnp.asarray(sin_table)[:, None]
    y_coord = (
        (place_y * cells_y + jnp.arange(cells_y)).astype(jnp.float32) + 0.5 - 0.5 * total_y
    ) * cell_span
    x_coord = (
        (place_x * cells_x + jnp.arange(cells_x)).astype(jnp.float32) + 0.5 - 0.5 * total_x
    ) * cell_span
    first_hi = params[0] * cos_table.max() - speed_grid[0]
    first_lo = params[0] * cos_table.min() - speed_grid[n_speed - 1]
    second_hi = params[0] * sin_table.max()
    second_lo = params[0] * sin_table.min()
    terms = jnp.stack(
        [
            jnp.maximum(drift[0] + first_hi, -(drift[0] + first_lo))
            + params[1] * jnp.abs(y_coord)[None, :],
            jnp.maximum(drift[1] + second_hi, -(drift[1] + second_lo))
            + params[1] * jnp.abs(x_coord)[:, None],
        ]
    )
    local_bounds = jnp.max(terms, axis=(1, 2))
    locals_now = local_whole(values)
    bounds = spread_max(spread_max(local_bounds, "gy", 0), "gx", 0)
    bound_one = bounds[0]
    bound_two = bounds[1]
    step_time = cfl_number / (
        bound_one / cell_span
        + bound_two / cell_span
        + alpha_three / step_psi
        + alpha_four / step_speed
    )
    x_col = x_coord[:, None, None, None]
    y_col = y_coord[None, :, None, None]
    flow_x = drift[0][:, :, None, None]
    flow_y = drift[1][:, :, None, None]

    def half_parts(field, side, x_halos, y_low, y_high, mean_three, partial):
        if side == 0:
            start, stop = 0, half
            ghost = ghost_low(field, x_halos[0], first_x, 0)
            wide_x = jnp.concatenate([ghost, field[: half + 3]], axis=0)
        elif side == 1:
            start, stop = half, cells_x
            ghost = ghost_high(field, x_halos[1], last_x, 0)
            wide_x = jnp.concatenate([field[half - 3 :], ghost], axis=0)
        else:
            start, stop = 0, cells_x
            wide_x = jnp.concatenate(
                [
                    ghost_low(field, x_halos[0], first_x, 0),
                    field,
                    ghost_high(field, x_halos[1], last_x, 0),
                ],
                axis=0,
            )
        if mean_three.shape[0] != stop - start:
            mean_three = mean_three[start:stop]
            partial = partial[start:stop]
        back_one, fore_one = one_sided(wide_x, 0, cell_span, stop - start)
        part = field[start:stop]
        wide_y = jnp.concatenate(
            [
                ghost_low(part, y_low[start:stop], first_y, 1),
                part,
                ghost_high(part, y_high[start:stop], last_y, 1),
            ],
            axis=1,
        )
        back_two, fore_two = one_sided(wide_y, 1, cell_span, cells_y)
        mean_one = 0.5 * (back_one + fore_one)
        mean_two = 0.5 * (back_two + fore_two)
        ham = mean_one * (along_one[None, None] + flow_x[start:stop])
        ham = ham + mean_two * (along_two[None, None] + flow_y[start:stop])
        ham = ham + params[1] * jnp.abs(mean_one * y_col - mean_two * x_col[start:stop] - mean_three)
        ham = ham + partial
        return ham, fore_one - back_one, fore_two - back_two

    def combine(ham, spread_one, spread_two):
        return ham + 0.5 * (bound_one * spread_one + bound_two * spread_two)

    def stage(field, x_halos, y_halos, local_pieces, order, update, last):
        if last:
            rate = combine(*half_parts(field, 2, x_halos, *y_halos, *local_pieces))
            return update(2, rate), None, None, None
        results = [None, None]
        sent = [None, None]

        def half(side):
            pieces = local_pieces[side] if isinstance(local_pieces, list) else local_pieces
            parts = half_parts(field, side, x_halos, *y_halos, *pieces)
            results[side] = update(side, combine(*parts))

        def send(side):
            if side == 0:
                piece = lax.optimization_barrier(results[side][:3])
                sent[side] = send_high(piece, "gx")
            else:
                piece = lax.optimization_barrier(results[side][results[side].shape[0] - 3 :])
                sent[side] = send_low(piece, "gx")

        half(order[0])
        send(order[0])
        half(order[1])
        send(order[1])
        merged = jnp.concatenate(results, axis=0)
        next_y = y_halo(merged)
        next_pieces = local_whole(merged)
        return merged, (sent[1], sent[0]), next_y, next_pieces

    first, x_halos, y_halos, locals_now = stage(
        values, x_halos, y_halos, locals_now, (0, 1),
        lambda side, rate: cut(values, side) + step_time * rate, False,
    )
    second, x_halos, y_halos, locals_now = stage(
        first, x_halos, y_halos, locals_now, (1, 0),
        lambda side, rate: 0.75 * cut(values, side) + 0.25 * (cut(first, side) + step_time * rate),
        False,
    )
    result, _, _, _ = stage(
        second, x_halos, y_halos, locals_now, (1, 0),
        lambda side, rate: cut(values, side) * (1.0 / 3.0)
        + 2.0 / 3.0 * (cut(second, side) + step_time * rate),
        True,
    )
    return result


def solution(mesh):
    in_specs = (P(("groups", "gx"), "gy", None, None), P(None, ("groups", "gx"), "gy"), P("groups"))
    out_specs = P(("groups", "gx"), "gy", None, None)
    return jax.shard_map(
        on_device, mesh=mesh, in_specs=in_specs, out_specs=out_specs, check_vma=False
    )
```

```python
import math

import jax
import numpy as np
import jax.numpy as jnp
from jax import lax
from jax.sharding import PartitionSpec as P


cfl_number = 0.5
weno_eps = 1e-06
cell_span = 1.0 / 64.0


def weno_value(first, second, third, fourth, fifth):
    stencil_one = first / 3.0 - 7.0 * second / 6.0 + 11.0 * third / 6.0
    stencil_two = -second / 6.0 + 5.0 * third / 6.0 + fourth / 3.0
    stencil_three = third / 3.0 + 5.0 * fourth / 6.0 - fifth / 6.0
    smooth_one = (
        13.0 / 12.0 * (first - 2.0 * second + third) ** 2
        + 0.25 * (first - 4.0 * second + 3.0 * third) ** 2
    )
    smooth_two = 13.0 / 12.0 * (second - 2.0 * third + fourth) ** 2 + 0.25 * (second - fourth) ** 2
    smooth_three = (
        13.0 / 12.0 * (third - 2.0 * fourth + fifth) ** 2
        + 0.25 * (3.0 * third - 4.0 * fourth + fifth) ** 2
    )
    weight_one = 0.1 / (weno_eps + smooth_one) ** 2
    weight_two = 0.6 / (weno_eps + smooth_two) ** 2
    weight_three = 0.3 / (weno_eps + smooth_three) ** 2
    total = weight_one * stencil_one + weight_two * stencil_two + weight_three * stencil_three
    return total / (weight_one + weight_two + weight_three)


def both_sides(window):
    backward = weno_value(window(0), window(1), window(2), window(3), window(4))
    forward = weno_value(window(5), window(4), window(3), window(2), window(1))
    return (backward, forward)


def one_sided(padded, along, spacing, length):
    extent = padded.shape[along]
    differences = (
        lax.slice_in_dim(padded, 1, extent, axis=along)
        - lax.slice_in_dim(padded, 0, extent - 1, axis=along)
    ) / spacing

    def window(offset):
        return lax.slice_in_dim(differences, offset, offset + length, axis=along)

    return both_sides(window)


def periodic_sided(field, along, spacing):
    extent = field.shape[along]
    wrapped = jnp.concatenate(
        [
            lax.slice_in_dim(field, extent - 3, extent, axis=along),
            field,
            lax.slice_in_dim(field, 0, 3, axis=along),
        ],
        axis=along,
    )
    return one_sided(wrapped, along, spacing, extent)


def clamped_sided(field, along, spacing):
    extent = field.shape[along]
    inner = (
        lax.slice_in_dim(field, 1, extent, axis=along)
        - lax.slice_in_dim(field, 0, extent - 1, axis=along)
    ) / spacing
    low_edge = lax.slice_in_dim(inner, 0, 1, axis=along)
    high_edge = lax.slice_in_dim(inner, extent - 2, extent - 1, axis=along)
    padded = jnp.concatenate([low_edge] * 3 + [inner] + [high_edge] * 3, axis=along)

    def window(offset):
        return lax.slice_in_dim(padded, offset, offset + extent, axis=along)

    return both_sides(window)


def send_low(piece, axis):
    count = lax.axis_size(axis)
    return lax.ppermute(piece, axis, [(i, (i + 1) % count) for i in range(count - 1)])


def send_high(piece, axis):
    count = lax.axis_size(axis)
    return lax.ppermute(piece, axis, [((i + 1) % count, i) for i in range(count - 1)])


def ghost_low(field, halo, at_low, along):
    shape_dist = [1] * field.ndim
    shape_dist[along] = 3
    inner = lax.slice_in_dim(field, 0, 1, axis=along)
    after = lax.slice_in_dim(field, 1, 2, axis=along)
    dist = jnp.arange(3, 0, -1).astype(jnp.float32).reshape(tuple(shape_dist))
    return jnp.where(at_low, inner + dist * (inner - after), halo)


def ghost_high(field, halo, at_high, along):
    extent = field.shape[along]
    shape_dist = [1] * field.ndim
    shape_dist[along] = 3
    inner = lax.slice_in_dim(field, extent - 1, extent, axis=along)
    before = lax.slice_in_dim(field, extent - 2, extent - 1, axis=along)
    dist = jnp.arange(1, 4).astype(jnp.float32).reshape(tuple(shape_dist))
    return jnp.where(at_high, inner + dist * (inner - before), halo)


def spread_max(local, axis, first_level):
    count = lax.axis_size(axis)
    span = 1
    level = first_level
    while span < count:
        moved = [
            lax.ppermute(local, axis, [(i, (i + k * span) % count) for i in range(count)])
            for k in range(1, 4)
            if k * span < count
        ]
        for item in moved:
            local = jnp.maximum(local, item)
        span *= 4
        level += 1
    return local


def on_device(values, drift, params):
    cells_x, cells_y, n_psi, n_speed = values.shape
    devices_x = lax.axis_size("gx")
    devices_y = lax.axis_size("gy")
    total_x = cells_x * devices_x
    total_y = cells_y * devices_y
    step_psi = 2.0 * math.pi / n_psi
    step_speed = 1.0 / n_speed
    place_x = lax.axis_index("gx")
    place_y = lax.axis_index("gy")
    first_x = place_x == 0
    last_x = place_x == devices_x - 1
    first_y = place_y == 0
    last_y = place_y == devices_y - 1
    half = cells_x // 2
    alpha_three = params[1] + params[2]
    alpha_four = params[3]

    def cut(array, side):
        if side == 0:
            return array[:half]
        if side == 1:
            return array[half:]
        return array

    def local_part(field):
        back_three, fore_three = periodic_sided(field, 2, step_psi)
        back_four, fore_four = clamped_sided(field, 3, step_speed)
        mean_three = 0.5 * (back_three + fore_three)
        mean_four = 0.5 * (back_four + fore_four)
        partial = -params[2] * jnp.abs(mean_three) + params[3] * jnp.abs(mean_four)
        partial = partial + 0.5 * (
            alpha_three * (fore_three - back_three) + alpha_four * (fore_four - back_four)
        )
        return mean_three, partial

    def y_halo(field):
        tail = lax.slice_in_dim(field, cells_y - 3, cells_y, axis=1)
        head = lax.slice_in_dim(field, 0, 3, axis=1)
        if devices_y == 2:
            offset = jnp.where(first_y, cells_y - 3, 0)
            piece = lax.dynamic_slice_in_dim(field, offset, 3, axis=1)
            piece = lax.optimization_barrier(piece)
            swapped = lax.ppermute(piece, "gy", [(0, 1), (1, 0)])
            return swapped, swapped
        tail, head = lax.optimization_barrier((tail, head))
        return send_low(tail, "gy"), send_high(head, "gy")

    def local_whole(field):
        return lax.optimization_barrier(local_part(field))

    x_halos = (send_low(values[cells_x - 3 :], "gx"), send_high(values[:3], "gx"))
    y_halos = y_halo(values)
    psi_grid = np.arange(n_psi).astype(np.float32) * np.float32(step_psi) - np.float32(math.pi)
    cos_table = np.cos(psi_grid.astype(np.float64)).astype(np.float32)
    sin_table = np.sin(psi_grid.astype(np.float64)).astype(np.float32)
    speed_grid = np.float32(0.5) + (
        np.arange(n_speed).astype(np.float32) + np.float32(0.5)
    ) * np.float32(step_speed)
    along_one = -jnp.asarray(speed_grid)[None, :] + params[0] * jnp.asarray(cos_table)[:, None]
    along_two = params[0] * jnp.asarray(sin_table)[:, None]
    y_coord = (
        (place_y * cells_y + jnp.arange(cells_y)).astype(jnp.float32) + 0.5 - 0.5 * total_y
    ) * cell_span
    x_coord = (
        (place_x * cells_x + jnp.arange(cells_x)).astype(jnp.float32) + 0.5 - 0.5 * total_x
    ) * cell_span
    first_hi = params[0] * cos_table.max() - speed_grid[0]
    first_lo = params[0] * cos_table.min() - speed_grid[n_speed - 1]
    second_hi = params[0] * sin_table.max()
    second_lo = params[0] * sin_table.min()
    terms = jnp.stack(
        [
            jnp.maximum(drift[0] + first_hi, -(drift[0] + first_lo))
            + params[1] * jnp.abs(y_coord)[None, :],
            jnp.maximum(drift[1] + second_hi, -(drift[1] + second_lo))
            + params[1] * jnp.abs(x_coord)[:, None],
        ]
    )
    local_bounds = jnp.max(terms, axis=(1, 2))
    locals_now = local_whole(values)
    bounds = spread_max(spread_max(local_bounds, "gy", 0), "gx", 0)
    bound_one = bounds[0]
    bound_two = bounds[1]
    step_time = cfl_number / (
        bound_one / cell_span
        + bound_two / cell_span
        + alpha_three / step_psi
        + alpha_four / step_speed
    )
    x_col = x_coord[:, None, None, None]
    y_col = y_coord[None, :, None, None]
    flow_x = drift[0][:, :, None, None]
    flow_y = drift[1][:, :, None, None]

    def half_parts(field, side, x_halos, y_low, y_high, mean_three, partial):
        if side == 0:
            start, stop = 0, half
            ghost = ghost_low(field, x_halos[0], first_x, 0)
            wide_x = jnp.concatenate([ghost, field[: half + 3]], axis=0)
        elif side == 1:
            start, stop = half, cells_x
            ghost = ghost_high(field, x_halos[1], last_x, 0)
            wide_x = jnp.concatenate([field[half - 3 :], ghost], axis=0)
        else:
            start, stop = 0, cells_x
            wide_x = jnp.concatenate(
                [
                    ghost_low(field, x_halos[0], first_x, 0),
                    field,
                    ghost_high(field, x_halos[1], last_x, 0),
                ],
                axis=0,
            )
        if mean_three.shape[0] != stop - start:
            mean_three = mean_three[start:stop]
            partial = partial[start:stop]
        back_one, fore_one = one_sided(wide_x, 0, cell_span, stop - start)
        part = field[start:stop]
        wide_y = jnp.concatenate(
            [
                ghost_low(part, y_low[start:stop], first_y, 1),
                part,
                ghost_high(part, y_high[start:stop], last_y, 1),
            ],
            axis=1,
        )
        back_two, fore_two = one_sided(wide_y, 1, cell_span, cells_y)
        mean_one = 0.5 * (back_one + fore_one)
        mean_two = 0.5 * (back_two + fore_two)
        ham = mean_one * (along_one[None, None] + flow_x[start:stop])
        ham = ham + mean_two * (along_two[None, None] + flow_y[start:stop])
        ham = ham + params[1] * jnp.abs(mean_one * y_col - mean_two * x_col[start:stop] - mean_three)
        ham = ham + partial
        return ham, fore_one - back_one, fore_two - back_two

    def combine(ham, spread_one, spread_two):
        return ham + 0.5 * (bound_one * spread_one + bound_two * spread_two)

    def stage(field, x_halos, y_halos, local_pieces, order, update, last):
        if last:
            rate = combine(*half_parts(field, 2, x_halos, *y_halos, *local_pieces))
            return update(2, rate), None, None, None
        results = [None, None]
        sent = [None, None]

        def half(side):
            pieces = local_pieces[side] if isinstance(local_pieces, list) else local_pieces
            parts = half_parts(field, side, x_halos, *y_halos, *pieces)
            results[side] = update(side, combine(*parts))

        def send(side):
            if side == 0:
                piece = results[side][:3]
                sent[side] = send_high(piece, "gx")
            else:
                piece = results[side][results[side].shape[0] - 3 :]
                sent[side] = send_low(piece, "gx")

        half(order[0])
        send(order[0])
        half(order[1])
        send(order[1])
        merged = jnp.concatenate(results, axis=0)
        next_y = y_halo(merged)
        next_pieces = local_whole(merged)
        return merged, (sent[1], sent[0]), next_y, next_pieces

    first, x_halos, y_halos, locals_now = stage(
        values, x_halos, y_halos, locals_now, (0, 1),
        lambda side, rate: cut(values, side) + step_time * rate, False,
    )
    second, x_halos, y_halos, locals_now = stage(
        first, x_halos, y_halos, locals_now, (1, 0),
        lambda side, rate: 0.75 * cut(values, side) + 0.25 * (cut(first, side) + step_time * rate),
        False,
    )
    result, _, _, _ = stage(
        second, x_halos, y_halos, locals_now, (1, 0),
        lambda side, rate: cut(values, side) * (1.0 / 3.0)
        + 2.0 / 3.0 * (cut(second, side) + step_time * rate),
        True,
    )
    return result


def solution(mesh):
    in_specs = (P(("groups", "gx"), "gy", None, None), P(None, ("groups", "gx"), "gy"), P("groups"))
    out_specs = P(("groups", "gx"), "gy", None, None)
    return jax.shard_map(
        on_device, mesh=mesh, in_specs=in_specs, out_specs=out_specs, check_vma=False
    )
```
